32 devices in a mesh: groups: 2 (over y), ty: 16 (over z, x, core).
Axes of the slice: x: 2, y: 2, z: 4, core: 2. Of those that a mesh axis runs over, the one named last changes fastest.
Arguments:
- image: float32 [2048, 2048], P(('groups', 'ty')), parts along dimension 0, may hold values from -6 to 6
- band_row: int32 [64], P(('groups', 'ty')), parts along dimension 0, may hold values from 0 to 32, as said below
- col_block: int32 [64], P(('groups', 'ty')), parts along dimension 0, may hold values from 0 to 15
- cell_index: int32 [64], P(('groups', 'ty')), parts along dimension 0, may hold values from 0 to 255
- offset_y: float32 [64, 128], P(('groups', 'ty')), parts along dimension 0, may hold values from 0 to 32
- offset_x: float32 [64, 128], P(('groups', 'ty')), parts along dimension 0, may hold values from 0 to 128
- flux_start: float32 [64, 128], P(('groups', 'ty')), parts along dimension 0, may hold values from 0.5 to 3
- psf_coef: float32 [9, 256], replicated, may hold values from -0.25 to 1.4
Outputs:
- fluxes: float32 [64, 128], P(('groups', 'ty')), parts along dimension 0
- residual: float32 [2048, 2048], P(('groups', 'ty')), parts along dimension 0
The draws below stay inside these ranges and needn't reach their ends.
There are 2 independent parts, one for each index of `groups`. The reference program is written for one: setup_inputs(seed, part) draws one part's arguments, and reference() takes and returns one part's arrays. A program takes and returns all parts, laid end to end along the dimension named above; an argument that names none is the same for every part. Nothing has to cross between parts.
Inputs may be any that keep to these rules, and one draw needn't show every extreme that they name: `band_row`: on every tile row, one of its 2 star blocks starts at row 0 and the other at row 32.
All inputs are finite; a program needn't handle non-finite values.
Results may differ from the reference program's by a relative error of at most 0.0003.
Values sent between devices are 32-bit elements; how exact they have to be, the bound alone decides.
No kernel may reach another device: no remote copies, remote signals or barrier semaphores. Data moves between devices by JAX's collectives and lax.ppermute only.
A program may use at most 64 MiB of HBM per device.

```python
import jax
import jax.numpy as jnp
from jax import lax

TILE_ROWS = 64
IMG_COLS = 2048
NB_DEV = 2
BLOCK_STARS = 128
CELLS = 256
REACH = 15
ITERS = 2
ROWS = 1024
BLOCKS = 32
N_TY = 16


def draw_band_row(key, part):
    strip_total = BLOCKS // NB_DEV
    edge_count = max(1, NB_DEV // 4)
    strip_keys = jax.random.split(jax.random.fold_in(key, 11), strip_total)

    def shuffle(strip_key):
        return jax.random.permutation(strip_key, NB_DEV)
    ranking = jnp.argsort(jax.vmap(shuffle)(strip_keys), axis=1)
    top_rows = jax.random.randint(jax.random.fold_in(key, 12), (strip_total, NB_DEV), 0, 16)
    low_rows = jax.random.randint(jax.random.fold_in(key, 13), (strip_total, NB_DEV), TILE_ROWS - 47, TILE_ROWS - 31)
    mid_rows = jax.random.randint(jax.random.fold_in(key, 14), (strip_total, NB_DEV), 16, TILE_ROWS - 47)
    start_rows = jnp.where(ranking < edge_count, top_rows, jnp.where(ranking < 2 * edge_count, low_rows, mid_rows))
    start_rows = jnp.where(ranking == 0, 0, start_rows)
    start_rows = jnp.where(ranking == edge_count, TILE_ROWS - 32, start_rows)
    return start_rows.reshape(BLOCKS).astype(jnp.int32)


def draw_psf_coef(key, part):
    main_lo, main_hi, side_spread, wing_lo, wing_hi = (0.8, 1.2, 0.2, 0.02, 0.06)
    main_coef = jax.random.uniform(jax.random.fold_in(key, 21), (1, CELLS), jnp.float32, main_lo, main_hi)
    side_coef = jax.random.uniform(jax.random.fold_in(key, 22), (7, CELLS), jnp.float32, -side_spread, side_spread)
    wing_coef = jax.random.uniform(jax.random.fold_in(key, 23), (1, CELLS), jnp.float32, wing_lo, wing_hi)
    return jnp.concatenate([main_coef, side_coef, wing_coef], axis=0)


def place_ends(array, rng, least, largest):
    spot = [jax.random.randint(jax.random.fold_in(rng, axis), (), 0, length) for axis, length in enumerate(array.shape)]
    longest = array.shape.index(max(array.shape))
    neighbour = spot[:longest] + [(spot[longest] + 1) % array.shape[longest]] + spot[longest + 1:]
    return array.at[tuple(spot)].set(least).at[tuple(neighbour)].set(largest)


def shard_levels(own_key, shape, cuts, least, high):
    def one(dim, parts):
        draws = jax.random.uniform(jax.random.fold_in(jax.random.fold_in(own_key, 6), dim), (parts,), jnp.float32, least / len(cuts), high / len(cuts))
        return jnp.repeat(jnp.exp(draws), shape[dim] // parts).reshape((-1,) + (1,) * (len(shape) - dim - 1))

    factor_of = one(*cuts[0])
    for cut in cuts[1:]:
        factor_of = factor_of * one(*cut)
    return factor_of


def normal_values(key, shape, spread, reach, cuts=(), held_as=jnp.bfloat16):
    entries = spread * jax.random.normal(key, shape, jnp.float32)
    if cuts:
        entries = entries * shard_levels(key, shape, cuts, -0.22, 0.18)
    return jnp.clip(entries, -reach, reach).astype(held_as)


def setup_inputs(seed: int = 0, part: int = 0) -> dict:
    streams_of = jax.random.split(jax.random.key(seed), 9)
    part_splits = jax.random.split(jax.random.fold_in(streams_of[8], part), 9)
    return {
        "image": normal_values(part_splits[0], (ROWS, IMG_COLS), 1.0, 6.0, ((0, 16),), jnp.float32),
        "band_row": draw_band_row(jax.random.fold_in(jax.random.fold_in(streams_of[8], part), 71), part),
        "col_block": place_ends(jax.random.randint(part_splits[2], (BLOCKS,), 0, IMG_COLS // 128), jax.random.fold_in(part_splits[2], 1), 0, (IMG_COLS // 128) - 1).astype(jnp.int32),
        "cell_index": place_ends(jax.random.randint(part_splits[3], (BLOCKS,), 0, CELLS), jax.random.fold_in(part_splits[3], 1), 0, CELLS - 1).astype(jnp.int32),
        "offset_y": jnp.clip(32.0 * jax.random.uniform(part_splits[4], (BLOCKS, BLOCK_STARS), jnp.float32) ** shard_levels(part_splits[4], (BLOCKS, BLOCK_STARS), ((0, 16),), -0.2, 0.2), 0.0, 32.0),
        "offset_x": jnp.clip(128.0 * jax.random.uniform(part_splits[5], (BLOCKS, BLOCK_STARS), jnp.float32) ** shard_levels(part_splits[5], (BLOCKS, BLOCK_STARS), ((0, 16),), -0.2, 0.2), 0.0, 128.0),
        "flux_start": jnp.clip(0.5 + 2.5 * jax.random.uniform(part_splits[6], (BLOCKS, BLOCK_STARS), jnp.float32) ** shard_levels(part_splits[6], (BLOCKS, BLOCK_STARS), ((0, 16),), -0.2, 0.2), 0.5, 3.0),
        "psf_coef": draw_psf_coef(jax.random.fold_in(streams_of[8], 71), part),
    }


HIGHEST = lax.Precision.HIGHEST


def profile(dist):
    tapered = jnp.maximum(0.0, 1.0 - (dist / 15.5) * (dist / 15.5))
    scaled = dist / 1.7
    core_part = jnp.exp(-0.5 * scaled * scaled) * tapered
    wing_part = jnp.exp(-dist * dist / 72.0) * tapered
    return jnp.stack([core_part, scaled * core_part, wing_part], axis=-2)


def placement(col_ids, col_count, dtype):
    slot_ids = jnp.arange(col_count + 1)
    left_hit = (slot_ids[None, :] == col_ids[:, None]).astype(dtype)
    right_hit = (slot_ids[None, :] == col_ids[:, None] + 1).astype(dtype)
    return jnp.stack([left_hit, right_hit])


def block_coefs(psf_coef, cell_index):
    cell_ids = jnp.arange(psf_coef.shape[1])
    picker = (cell_ids[:, None] == cell_index[None, :]).astype(psf_coef.dtype)
    return jnp.dot(psf_coef, picker, precision=HIGHEST)


def norms(ylocal, xoff, coefs):
    block_count = ylocal.shape[0]
    offsets = jnp.arange(-15, 17).astype(ylocal.dtype)
    rows_profile = profile(jnp.floor(ylocal)[:, None, :] + offsets[None, :, None] - ylocal[:, None, :])
    cols_profile = profile(jnp.floor(xoff)[:, None, :] + offsets[None, :, None] - xoff[:, None, :])
    gram_rows = jnp.einsum("jkas,jkcs->acjs", rows_profile, rows_profile, precision=HIGHEST)
    gram_cols = jnp.einsum("jkbs,jkds->bdjs", cols_profile, cols_profile, precision=HIGHEST)
    shaped = coefs.reshape(3, 3, block_count)
    return jnp.einsum("abj,cdj,acjs,bdjs->js", shaped, shaped, gram_rows, gram_cols, precision=HIGHEST)


def render(rows_profile, cols_profile, coefs, fluxes, col_ids, col_count):
    block_count, row_count, _, star_count = rows_profile.shape
    mixed = jnp.einsum("abj,jwbs->jwas", coefs.reshape(3, 3, block_count), cols_profile, precision=HIGHEST)
    mixed = mixed * fluxes[:, None, None, :]
    stamps = jnp.einsum("jhk,jwk->jhw", rows_profile.reshape(block_count, row_count, 3 * star_count),
                        mixed.reshape(block_count, 256, 3 * star_count), precision=HIGHEST)
    placed = placement(col_ids, col_count, stamps.dtype)
    canvas = jnp.einsum("pjc,jhpw->hcw", placed, stamps.reshape(block_count, row_count, 2, 128), precision=HIGHEST)
    return canvas.reshape(row_count, (col_count + 1) * 128)[:, 64:64 + 128 * col_count]


def fit_terms(resid_ext, rows_profile, cols_profile, coefs, col_ids, col_count):
    block_count, row_count, _, star_count = rows_profile.shape
    padded = jnp.pad(resid_ext, ((0, 0), (64, 64))).reshape(row_count, col_count + 1, 128)
    placed = placement(col_ids, col_count, resid_ext.dtype)
    windows = jnp.einsum("pjc,hcw->jhpw", placed, padded, precision=HIGHEST).reshape(block_count, row_count, 256)
    across = jnp.einsum("jhw,jwk->jhk", windows, cols_profile.reshape(block_count, 256, 3 * star_count),
                        precision=HIGHEST).reshape(block_count, row_count, 3, star_count)
    paired = jnp.einsum("jhas,jhbs->jabs", rows_profile, across, precision=HIGHEST)
    return jnp.einsum("abj,jabs->js", coefs.reshape(3, 3, block_count), paired, precision=HIGHEST)


def reference(image, band_row, col_block, cell_index, offset_y, offset_x, flux_start, psf_coef):
    col_count = IMG_COLS // 128
    coefs = block_coefs(psf_coef, cell_index)
    ylocal = band_row.astype(jnp.float32)[:, None] + offset_y
    weight = norms(ylocal, offset_x, coefs)
    ext_ids = jnp.arange(-REACH, TILE_ROWS + REACH).astype(jnp.float32)
    columns = jnp.arange(256).astype(jnp.float32) - 64.0
    strip_y = ylocal.reshape(N_TY, NB_DEV, BLOCK_STARS)
    strip_x = offset_x.reshape(N_TY, NB_DEV, BLOCK_STARS)
    strip_cols = col_block.reshape(N_TY, NB_DEV)
    strip_coefs = coefs.reshape(9, N_TY, NB_DEV).transpose(1, 0, 2)

    def model_of(fluxes):
        strip_flux = fluxes.reshape(N_TY, NB_DEV, BLOCK_STARS)

        def one_strip(strip_args):
            pos_y, pos_x, coef_here, flux_here, cols_here = strip_args
            return render(profile(ext_ids[None, :, None] - pos_y[:, None, :]),
                          profile(columns[None, :, None] - pos_x[:, None, :]),
                          coef_here, flux_here, cols_here, col_count)

        extended = lax.map(one_strip, (strip_y, strip_x, strip_coefs, strip_flux, strip_cols))
        model_img = extended[:, REACH:REACH + TILE_ROWS]
        model_img = model_img.at[1:, :REACH].add(extended[:-1, TILE_ROWS + REACH:])
        model_img = model_img.at[:-1, TILE_ROWS - REACH:].add(extended[1:, :REACH])
        return model_img.reshape(ROWS, IMG_COLS)

    def gradient(residue):
        full = jnp.pad(residue, ((REACH, REACH), (0, 0)))

        def one_strip(strip_args):
            strip_index, pos_y, pos_x, coef_here, cols_here = strip_args
            window = lax.dynamic_slice_in_dim(full, strip_index * TILE_ROWS, TILE_ROWS + 2 * REACH, 0)
            return fit_terms(window, profile(ext_ids[None, :, None] - pos_y[:, None, :]),
                             profile(columns[None, :, None] - pos_x[:, None, :]),
                             coef_here, cols_here, col_count)

        strip_ids = jnp.arange(N_TY).astype(jnp.int32)
        terms = lax.map(one_strip, (strip_ids, strip_y, strip_x, strip_coefs, strip_cols))
        return terms.reshape(BLOCKS, BLOCK_STARS)

    fluxes = flux_start
    for iteration in range(ITERS):
        residue = image - model_of(fluxes)
        fluxes = fluxes + 0.5 * gradient(residue) / weight
    residual = image - model_of(fluxes)
    return fluxes, residual
```

```python
import functools

import jax
import jax.numpy as jnp
from jax import lax
from jax.experimental import pallas as pl
from jax.experimental.pallas import tpu as pltpu
from jax.sharding import PartitionSpec as P

REACH = 15
ITERS = 2
HALO = 16
LANES = 128
WIN = 384
SLOTS = 8


HIGHEST = lax.Precision.HIGHEST


def profile(dist):
    tapered = jnp.maximum(0.0, 1.0 - dist / 15.5 * (dist / 15.5))
    scaled = dist / 1.7
    core_part = jnp.exp(-0.5 * scaled * scaled) * tapered
    wing_part = jnp.exp(-dist * dist / 72.0) * tapered
    return jnp.stack([core_part, scaled * core_part, wing_part], axis=-2)


def profile3(dist):
    tapered = jnp.maximum(0.0, 1.0 - dist / 15.5 * (dist / 15.5))
    scaled = dist / 1.7
    core_part = jnp.exp(-0.5 * scaled * scaled) * tapered
    wing_part = jnp.exp(-dist * dist / 72.0) * tapered
    return core_part, scaled * core_part, wing_part


def block_coefs(psf_coef, cell_index):
    cell_ids = jnp.arange(psf_coef.shape[1])
    picker = (cell_ids[:, None] == cell_index[None, :]).astype(psf_coef.dtype)
    return jnp.dot(psf_coef, picker, precision=HIGHEST)


def norms(ylocal, xoff, coefs):
    block_count = ylocal.shape[0]
    offsets = jnp.arange(-15, 17).astype(ylocal.dtype)
    rows_profile = profile(
        jnp.floor(ylocal)[:, None, :] + offsets[None, :, None] - ylocal[:, None, :]
    )
    cols_profile = profile(jnp.floor(xoff)[:, None, :] + offsets[None, :, None] - xoff[:, None, :])
    gram_rows = jnp.einsum("jkas,jkcs->acjs", rows_profile, rows_profile, precision=HIGHEST)
    gram_cols = jnp.einsum("jkbs,jkds->bdjs", cols_profile, cols_profile, precision=HIGHEST)
    shaped = coefs.reshape(3, 3, block_count)
    return jnp.einsum(
        "abj,cdj,acjs,bdjs->js", shaped, shaped, gram_rows, gram_cols, precision=HIGHEST
    )


def exchange(to_above, to_below):
    count = lax.axis_size("ty")
    forward = [(i, i + 1) for i in range(count - 1)]
    backward = [(i + 1, i) for i in range(count - 1)]
    from_above = lax.ppermute(to_below, "ty", forward)
    from_below = lax.ppermute(to_above, "ty", backward)
    return from_above, from_below


def phase_kernel(
    final, own, blocks, cols_ref, coef_ref, y_ref, x_ref, f_ref, w_ref, above_ref, img_ref,
    below_ref, mask_ref, out_ref, canvas
):
    ext_rows, pad_width = canvas.shape
    strip_rows, width = img_ref.shape
    canvas[...] = jnp.zeros_like(canvas)
    hpos = lax.broadcasted_iota(jnp.int32, (ext_rows, LANES), 0).astype(jnp.float32) - HALO
    wpos = lax.broadcasted_iota(jnp.int32, (WIN, LANES), 0).astype(jnp.float32) - LANES
    keep_above = hpos < REACH
    dims_nt = (((1,), (1,)), ((), ()))
    saved = []
    for j in range(blocks):
        rows = profile3(hpos - y_ref[j : j + 1, :])
        if j == own:
            rows_model = tuple(jnp.where(keep_above, r, 0.0) for r in rows)
        else:
            rows_model = rows
        cols = profile3(wpos - x_ref[j : j + 1, :])
        flux = f_ref[j : j + 1, :]
        stamp = None
        for a in range(3):
            base = 9 * j + 3 * a
            mixed = (
                coef_ref[base] * cols[0] + coef_ref[base + 1] * cols[1] + coef_ref[base + 2] * cols[2]
            ) * flux
            part = lax.dot_general(
                rows_model[a], mixed, dims_nt, precision=HIGHEST,
                preferred_element_type=jnp.float32,
            )
            stamp = part if stamp is None else stamp + part
        start = pl.multiple_of(cols_ref[j] * LANES, LANES)
        canvas[:, pl.ds(start, WIN)] += stamp
        if j < own:
            saved.append((rows, cols))
    if final:
        out_ref[...] = img_ref[...] - canvas[HALO : HALO + strip_rows, LANES : LANES + width]
        return
    top = (above_ref[...] - canvas[0:HALO, LANES : LANES + width]) * mask_ref[0:HALO, :]
    mid = (img_ref[...] - canvas[HALO : HALO + strip_rows, LANES : LANES + width]) * mask_ref[
        HALO : HALO + strip_rows, :
    ]
    bot = (below_ref[...] - canvas[HALO + strip_rows :, LANES : LANES + width]) * mask_ref[
        HALO + strip_rows :, :
    ]
    canvas[0:HALO, LANES : LANES + width] = top
    canvas[HALO : HALO + strip_rows, LANES : LANES + width] = mid
    canvas[HALO + strip_rows :, LANES : LANES + width] = bot
    canvas[:, 0:LANES] = jnp.zeros((ext_rows, LANES), jnp.float32)
    canvas[:, LANES + width :] = jnp.zeros((ext_rows, pad_width - LANES - width), jnp.float32)
    out_ref[...] = jnp.zeros_like(out_ref)
    for j in range(own):
        rows, cols = saved[j]
        start = pl.multiple_of(cols_ref[j] * LANES, LANES)
        window = canvas[:, pl.ds(start, WIN)]
        across = [
            jnp.dot(window, cols[b], precision=HIGHEST, preferred_element_type=jnp.float32)
            for b in range(3)
        ]
        grad = None
        for a in range(3):
            for b in range(3):
                paired = jnp.sum(rows[a] * across[b], axis=0, keepdims=True)
                term = coef_ref[9 * j + 3 * a + b] * paired
                grad = term if grad is None else grad + term
        out_ref[j : j + 1, :] = f_ref[j : j + 1, :] + 0.5 * grad / w_ref[j : j + 1, :]


def run_phase(final, own, blocks, cols, coef_flat, ys, xs, fs, ws, above, image, below, mask):
    strip_rows, width = image.shape
    ext_rows = strip_rows + 2 * HALO
    smem = pl.BlockSpec(memory_space=pltpu.SMEM)
    vmem = pl.BlockSpec(memory_space=pltpu.VMEM)
    if final:
        out_shape = jax.ShapeDtypeStruct((strip_rows, width), jnp.float32)
    else:
        out_shape = jax.ShapeDtypeStruct((SLOTS, LANES), jnp.float32)
    matmul_flops = 2 * 3 * ext_rows * WIN * LANES * (blocks + (0 if final else own))
    return pl.pallas_call(
        functools.partial(phase_kernel, final, own, blocks),
        out_shape=out_shape,
        in_specs=[smem, smem] + [vmem] * 8,
        out_specs=vmem,
        scratch_shapes=[pltpu.VMEM((ext_rows, width + 2 * LANES), jnp.float32)],
        cost_estimate=pl.CostEstimate(
            flops=6 * matmul_flops, transcendentals=blocks * 2 * (ext_rows + WIN) * LANES,
            bytes_accessed=4 * (ext_rows * width * (1 if final else 2)),
        ),
    )(cols, coef_flat, ys, xs, fs, ws, above, image, below, mask)


def local(image, band_row, col_block, cell_index, offset_y, offset_x, flux_start, psf_coef):
    strip_rows, strip_width = image.shape
    own = band_row.shape[0]
    coefs = block_coefs(psf_coef, cell_index)
    ylocal = band_row.astype(jnp.float32)[:, None] + offset_y
    weight = norms(ylocal, offset_x, coefs)

    top = (band_row[1] < band_row[0]).astype(jnp.int32)
    pick_top = top == 0

    def edge(values, axis):
        first = lax.index_in_dim(values, 0, axis, keepdims=False)
        second = lax.index_in_dim(values, 1, axis, keepdims=False)
        return jnp.where(pick_top, first, second), jnp.where(pick_top, second, first)

    y_top, y_bot = edge(ylocal, 0)
    x_top, x_bot = edge(offset_x, 0)
    f_top, f_bot = edge(flux_start, 0)
    c_top, c_bot = edge(coefs, 1)
    col_f = col_block.astype(jnp.float32)
    k_top, k_bot = edge(col_f, 0)

    def star_row(y, x, f, c, k):
        meta = jnp.concatenate([c, k[None], jnp.zeros((LANES - 10,), jnp.float32)])
        row = jnp.concatenate([y, x, f, meta, jnp.zeros((strip_width - 4 * LANES,), jnp.float32)])
        return row[None, :]

    send_up = jnp.concatenate(
        [image[:REACH], star_row(y_top, x_top, f_top, c_top, k_top)], axis=0
    )
    send_down = jnp.concatenate(
        [star_row(y_bot, x_bot, f_bot, c_bot, k_bot), image[strip_rows - REACH :]], axis=0
    )
    got_above, got_below = exchange(send_up, send_down)

    def unpack(row):
        return (
            row[0:LANES],
            row[LANES : 2 * LANES],
            row[2 * LANES : 3 * LANES],
            row[3 * LANES : 3 * LANES + 9],
            row[3 * LANES + 9],
        )

    ya, xa, fa, ca, ka = unpack(got_above[0])
    yb, xb, fb, cb, kb = unpack(got_below[REACH])

    ext_rows = strip_rows + 2 * HALO
    me = lax.axis_index("ty")
    last = lax.axis_size("ty") - 1
    h_ids = jnp.arange(ext_rows)
    row_ok = (h_ids >= HALO - REACH) & (h_ids < HALO + strip_rows + REACH)
    row_ok = row_ok & ((h_ids >= HALO) | (me > 0)) & ((h_ids < HALO + strip_rows) | (me < last))
    mask = row_ok.astype(jnp.float32)[:, None]

    blocks = own + 2
    spare = jnp.zeros((SLOTS - blocks, LANES), jnp.float32)
    ys = jnp.concatenate(
        [ylocal, (ya - strip_rows)[None], (yb + strip_rows)[None], spare], axis=0
    )
    xs = jnp.concatenate([offset_x, xa[None], xb[None], spare], axis=0)
    all_c = jnp.concatenate([coefs, ca[:, None], cb[:, None]], axis=1)
    coef_flat = all_c.T.reshape(-1)
    cols = jnp.concatenate(
        [col_block, ka.astype(jnp.int32)[None], kb.astype(jnp.int32)[None]]
    )
    ws = jnp.concatenate([weight, jnp.ones((SLOTS - own, LANES), jnp.float32)], axis=0)

    phase = functools.partial(
        run_phase, own=own, blocks=blocks, cols=cols, coef_flat=coef_flat, ys=ys, xs=xs, ws=ws,
        above=got_above, image=image, below=got_below, mask=mask,
    )
    fluxes = flux_start
    f_above, f_below = fa, fb
    for iteration in range(ITERS):
        fs = jnp.concatenate([fluxes, f_above[None], f_below[None], spare], axis=0)
        fluxes = phase(False, fs=fs)[:own]
        new_top, new_bot = edge(fluxes, 0)
        f_above, f_below = exchange(new_top, new_bot)
    fs = jnp.concatenate([fluxes, f_above[None], f_below[None], spare], axis=0)
    residual = phase(True, fs=fs)
    return (fluxes, residual)


def solution(mesh):
    return jax.shard_map(
        local,
        mesh=mesh,
        in_specs=(
            P(("groups", "ty"), None),
            P(("groups", "ty")),
            P(("groups", "ty")),
            P(("groups", "ty")),
            P(("groups", "ty"), None),
            P(("groups", "ty"), None),
            P(("groups", "ty"), None),
            P(),
        ),
        out_specs=(P(("groups", "ty"), None), P(("groups", "ty"), None)),
        check_vma=False,
    )
```

```python
import functools

import jax
import jax.numpy as jnp
from jax import lax
from jax.experimental import pallas as pl
from jax.experimental.pallas import tpu as pltpu
from jax.sharding import PartitionSpec as P

REACH = 15
ITERS = 2
HALO = 16
LANES = 128
WIN = 384
META = 8
PACKET = HALO + META


HIGHEST = lax.Precision.HIGHEST
DIMS_NT = (((1,), (1,)), ((), ()))


def profile3(dist):
    tapered = jnp.maximum(0.0, 1.0 - dist / 15.5 * (dist / 15.5))
    scaled = dist / 1.7
    core_part = jnp.exp(-0.5 * scaled * scaled) * tapered
    wing_part = jnp.exp(-dist * dist / 72.0) * tapered
    return core_part, scaled * core_part, wing_part


def exchange(to_above, to_below):
    count = lax.axis_size("ty")
    forward = [(i, i + 1) for i in range(count - 1)]
    backward = [(i + 1, i) for i in range(count - 1)]
    from_above = lax.ppermute(to_below, "ty", forward)
    from_below = lax.ppermute(to_above, "ty", backward)
    return from_above, from_below


def own_coefs(psf_ref, cell_ref, j):
    cell = cell_ref[j]
    return [psf_ref[k, cell] for k in range(9)]


def setup_kernel(
    band_ref, col_ref, cell_ref, psf_ref, img_ref, oy_ref, ox_ref, f_ref, up_ref, down_ref, w_ref
):
    strip_rows = img_ref.shape[0]
    own = oy_ref.shape[0]
    offs = lax.broadcasted_iota(jnp.int32, (32, LANES), 0).astype(jnp.float32) - 15.0
    lane = lax.broadcasted_iota(jnp.int32, (1, LANES), 1)
    ys, metas = [], []
    for j in range(own):
        y = band_ref[j].astype(jnp.float32) + oy_ref[j : j + 1, :]
        x = ox_ref[j : j + 1, :]
        c = own_coefs(psf_ref, cell_ref, j)
        rows = profile3(jnp.floor(y) + offs - y)
        cols = profile3(jnp.floor(x) + offs - x)
        gram_r = [[jnp.sum(rows[a] * rows[b], axis=0, keepdims=True) for b in range(3)] for a in range(3)]
        gram_c = [[jnp.sum(cols[a] * cols[b], axis=0, keepdims=True) for b in range(3)] for a in range(3)]
        weight = None
        for a in range(3):
            for cc in range(3):
                inner = None
                for b in range(3):
                    for d in range(3):
                        term = (c[3 * a + b] * c[3 * cc + d]) * gram_c[b][d]
                        inner = term if inner is None else inner + term
                term = gram_r[a][cc] * inner
                weight = term if weight is None else weight + term
        w_ref[j : j + 1, :] = weight
        meta = jnp.zeros((1, LANES), jnp.float32)
        for k in range(9):
            meta = jnp.where(lane == k, c[k], meta)
        meta = jnp.where(lane == 9, col_ref[j].astype(jnp.float32), meta)
        ys.append(y)
        metas.append(meta)
    top_first = band_ref[0] <= band_ref[1]

    def pick(first, second):
        return jnp.where(top_first, first, second), jnp.where(top_first, second, first)

    y_top, y_bot = pick(ys[0], ys[1])
    x_top, x_bot = pick(ox_ref[0:1, :], ox_ref[1:2, :])
    f_top, f_bot = pick(f_ref[0:1, :], f_ref[1:2, :])
    m_top, m_bot = pick(metas[0], metas[1])
    up_ref[...] = jnp.zeros_like(up_ref)
    down_ref[...] = jnp.zeros_like(down_ref)
    up_ref[0:HALO, :] = img_ref[0:HALO, :]
    for r, v in enumerate((y_top, x_top, f_top, m_top)):
        up_ref[HALO + r : HALO + r + 1, 0:LANES] = v
    for r, v in enumerate((y_bot, x_bot, f_bot, m_bot)):
        down_ref[r : r + 1, 0:LANES] = v
    down_ref[META:PACKET, :] = img_ref[strip_rows - HALO : strip_rows, :]


def phase_kernel(
    final, above_row, below_row,
    band_ref, col_ref, cell_ref, psf_ref, nbm_ref, flag_ref,
    oy_ref, ox_ref, f_ref, w_ref, above_ref, img_ref, below_ref, fa_ref, fb_ref,
    *rest,
):
    if final:
        out_ref, canvas = rest
    else:
        fout_ref, up_ref, down_ref, canvas = rest
    ext_rows, pad_width = canvas.shape
    strip_rows, width = img_ref.shape
    own = oy_ref.shape[0]
    canvas[...] = jnp.zeros_like(canvas)
    hpos = lax.broadcasted_iota(jnp.int32, (ext_rows, LANES), 0).astype(jnp.float32) - HALO
    wpos = lax.broadcasted_iota(jnp.int32, (WIN, LANES), 0).astype(jnp.float32) - LANES
    keep_above = hpos < REACH

    specs = []
    for j in range(own):
        y = band_ref[j].astype(jnp.float32) + oy_ref[j : j + 1, :]
        specs.append((y, ox_ref[j : j + 1, :], f_ref[j : j + 1, :],
                      own_coefs(psf_ref, cell_ref, j), col_ref[j]))
    specs.append((
        above_ref[0:1, 0:LANES] - strip_rows, above_ref[1:2, 0:LANES],
        fa_ref[above_row : above_row + 1, 0:LANES],
        [nbm_ref[k] for k in range(9)], nbm_ref[9].astype(jnp.int32),
    ))
    specs.append((
        below_ref[HALO : HALO + 1, 0:LANES] + strip_rows, below_ref[HALO + 1 : HALO + 2, 0:LANES],
        fb_ref[below_row : below_row + 1, 0:LANES],
        [nbm_ref[16 + k] for k in range(9)], nbm_ref[16 + 9].astype(jnp.int32),
    ))

    saved = []
    for j, (y, x, flux, c, col) in enumerate(specs):
        rows = profile3(hpos - y)
        if j == own:
            rows_model = tuple(jnp.where(keep_above, r, 0.0) for r in rows)
        else:
            rows_model = rows
        cols = profile3(wpos - x)
        stamp = None
        for a in range(3):
            mixed = (c[3 * a] * cols[0] + c[3 * a + 1] * cols[1] + c[3 * a + 2] * cols[2]) * flux
            part = lax.dot_general(
                rows_model[a], mixed, DIMS_NT, precision=HIGHEST,
                preferred_element_type=jnp.float32,
            )
            stamp = part if stamp is None else stamp + part
        start = pl.multiple_of(col * LANES, LANES)
        canvas[:, pl.ds(start, WIN)] += stamp
        if j < own:
            saved.append((rows, cols, c, start))
    inner = slice(LANES, LANES + width)
    if final:
        out_ref[...] = img_ref[...] - canvas[HALO : HALO + strip_rows, inner]
        return
    edge_ids = lax.broadcasted_iota(jnp.int32, (HALO, width), 0)
    top_ok = (edge_ids >= HALO - REACH) & (flag_ref[0] > 0)
    bot_ok = (edge_ids < REACH) & (flag_ref[1] > 0)
    top = jnp.where(top_ok, above_ref[META:PACKET, :] - canvas[0:HALO, inner], 0.0)
    bot = jnp.where(bot_ok, below_ref[0:HALO, :] - canvas[HALO + strip_rows :, inner], 0.0)
    mid = img_ref[...] - canvas[HALO : HALO + strip_rows, inner]
    canvas[0:HALO, inner] = top
    canvas[HALO : HALO + strip_rows, inner] = mid
    canvas[HALO + strip_rows :, inner] = bot
    canvas[:, 0:LANES] = jnp.zeros((ext_rows, LANES), jnp.float32)
    canvas[:, LANES + width :] = jnp.zeros((ext_rows, pad_width - LANES - width), jnp.float32)
    news = []
    for j in range(own):
        rows, cols, c, start = saved[j]
        window = canvas[:, pl.ds(start, WIN)]
        across = [
            jnp.dot(window, cols[b], precision=HIGHEST, preferred_element_type=jnp.float32)
            for b in range(3)
        ]
        grad = None
        for a in range(3):
            for b in range(3):
                paired = jnp.sum(rows[a] * across[b], axis=0, keepdims=True)
                term = c[3 * a + b] * paired
                grad = term if grad is None else grad + term
        new = f_ref[j : j + 1, :] + 0.5 * grad / w_ref[j : j + 1, :]
        fout_ref[j : j + 1, :] = new
        news.append(new)
    top_first = band_ref[0] <= band_ref[1]
    up_ref[...] = jnp.where(top_first, news[0], news[1])
    down_ref[...] = jnp.where(top_first, news[1], news[0])


def local(image, band_row, col_block, cell_index, offset_y, offset_x, flux_start, psf_coef):
    strip_rows, strip_width = image.shape
    own = band_row.shape[0]
    f32 = jnp.float32
    smem = pl.BlockSpec(memory_space=pltpu.SMEM)
    vmem = pl.BlockSpec(memory_space=pltpu.VMEM)
    packet = jax.ShapeDtypeStruct((PACKET, strip_width), f32)
    send_up, send_down, weight = pl.pallas_call(
        setup_kernel,
        out_shape=(packet, packet, jax.ShapeDtypeStruct((own, LANES), f32)),
        in_specs=[smem] * 4 + [vmem] * 4,
        out_specs=(vmem, vmem, vmem),
    )(band_row, col_block, cell_index, psf_coef, image, offset_y, offset_x, flux_start)
    got_above, got_below = exchange(send_up, send_down)

    me = lax.axis_index("ty")
    last = lax.axis_size("ty") - 1
    flags = jnp.stack([me > 0, me < last]).astype(jnp.int32)
    nbm = jnp.concatenate([got_above[3, :16], got_below[HALO + 3, :16]])

    ext_rows = strip_rows + 2 * HALO
    blocks = own + 2
    flops = 6 * 2 * 3 * ext_rows * WIN * LANES * (blocks + own)
    flux_shape = jax.ShapeDtypeStruct((own, LANES), f32)
    edge_shape = jax.ShapeDtypeStruct((1, LANES), f32)
    common = (band_row, col_block, cell_index, psf_coef, nbm, flags,
              offset_y, offset_x)

    def phase(final, fluxes, fa, fb, above_row, below_row):
        kernel = functools.partial(phase_kernel, final, above_row, below_row)
        if final:
            out_shape = jax.ShapeDtypeStruct((strip_rows, strip_width), f32)
            out_specs = vmem
        else:
            out_shape = (flux_shape, edge_shape, edge_shape)
            out_specs = (vmem, vmem, vmem)
        return pl.pallas_call(
            kernel,
            out_shape=out_shape,
            in_specs=[smem] * 6 + [vmem] * 9,
            out_specs=out_specs,
            scratch_shapes=[pltpu.VMEM((ext_rows, strip_width + 2 * LANES), f32)],
            cost_estimate=pl.CostEstimate(
                flops=flops, transcendentals=blocks * 2 * (ext_rows + WIN) * LANES,
                bytes_accessed=4 * ext_rows * strip_width * 2,
            ),
        )(*common, fluxes, weight, got_above, image, got_below, fa, fb)

    fluxes = flux_start
    fa, fb = got_above, got_below
    above_row, below_row = 2, HALO + 2
    for iteration in range(ITERS):
        fluxes, new_top, new_bot = phase(False, fluxes, fa, fb, above_row, below_row)
        fa, fb = exchange(new_top, new_bot)
        above_row, below_row = 0, 0
    residual = phase(True, fluxes, fa, fb, above_row, below_row)
    return (fluxes, residual)


def solution(mesh):
    return jax.shard_map(
        local,
        mesh=mesh,
        in_specs=(
            P(("groups", "ty"), None),
            P(("groups", "ty")),
            P(("groups", "ty")),
            P(("groups", "ty")),
            P(("groups", "ty"), None),
            P(("groups", "ty"), None),
            P(("groups", "ty"), None),
            P(),
        ),
        out_specs=(P(("groups", "ty"), None), P(("groups", "ty"), None)),
        check_vma=False,
    )
```

```python
import functools

import jax
import jax.numpy as jnp
from jax import lax
from jax.experimental import pallas as pl
from jax.experimental.pallas import tpu as pltpu
from jax.sharding import PartitionSpec as P

REACH = 15
ITERS = 2
HALO = 16
LANES = 128
WIN = 384
PACKET = HALO


HIGHEST = lax.Precision.HIGHEST
DIMS_NT = (((1,), (1,)), ((), ()))


def profile3(dist):
    tapered_arg = dist * (1.0 / 15.5)
    tapered = jnp.maximum(0.0, 1.0 - tapered_arg * tapered_arg)
    scaled = dist * (1.0 / 1.7)
    core_part = jnp.exp(-0.5 * scaled * scaled) * tapered
    wing_part = jnp.exp(dist * dist * (-1.0 / 72.0)) * tapered
    return core_part, scaled * core_part, wing_part


def exchange(to_above, to_below):
    count = lax.axis_size("ty")
    forward = [(i, i + 1) for i in range(count - 1)]
    backward = [(i + 1, i) for i in range(count - 1)]
    from_above = lax.ppermute(to_below, "ty", forward)
    from_below = lax.ppermute(to_above, "ty", backward)
    return from_above, from_below


def own_coefs(psf_ref, cell_ref, j):
    cell = cell_ref[j]
    return [psf_ref[k, cell] for k in range(9)]


def setup_kernel(
    band_ref, col_ref, cell_ref, psf_ref, img_ref, oy_ref, ox_ref, f_ref, up_ref, down_ref, w_ref
):
    strip_rows = img_ref.shape[0]
    own = oy_ref.shape[0]
    offs = lax.broadcasted_iota(jnp.int32, (32, LANES), 0).astype(jnp.float32) - 15.0
    lane = lax.broadcasted_iota(jnp.int32, (1, LANES), 1)
    ys, metas = [], []
    for j in range(own):
        y = band_ref[j].astype(jnp.float32) + oy_ref[j : j + 1, :]
        x = ox_ref[j : j + 1, :]
        c = own_coefs(psf_ref, cell_ref, j)
        rows = profile3(jnp.floor(y) + offs - y)
        cols = profile3(jnp.floor(x) + offs - x)
        gram_r = [[jnp.sum(rows[a] * rows[b], axis=0, keepdims=True) for b in range(3)] for a in range(3)]
        gram_c = [[jnp.sum(cols[a] * cols[b], axis=0, keepdims=True) for b in range(3)] for a in range(3)]
        weight = None
        for a in range(3):
            for cc in range(3):
                inner = None
                for b in range(3):
                    for d in range(3):
                        term = (c[3 * a + b] * c[3 * cc + d]) * gram_c[b][d]
                        inner = term if inner is None else inner + term
                term = gram_r[a][cc] * inner
                weight = term if weight is None else weight + term
        w_ref[j : j + 1, :] = weight
        meta = jnp.zeros((1, LANES), jnp.float32)
        for k in range(9):
            meta = jnp.where(lane == k, c[k], meta)
        meta = jnp.where(lane == 9, col_ref[j].astype(jnp.float32), meta)
        ys.append(y)
        metas.append(meta)
    top_first = band_ref[0] <= band_ref[1]

    def pick(first, second):
        return jnp.where(top_first, first, second), jnp.where(top_first, second, first)

    y_top, y_bot = pick(ys[0], ys[1])
    x_top, x_bot = pick(ox_ref[0:1, :], ox_ref[1:2, :])
    f_top, f_bot = pick(f_ref[0:1, :], f_ref[1:2, :])
    m_top, m_bot = pick(metas[0], metas[1])
    up_ref[...] = img_ref[0:HALO, :]
    for r, v in enumerate((y_top, x_top, f_top, m_top)):
        up_ref[HALO - 1 : HALO, r * LANES : (r + 1) * LANES] = v
    down_ref[...] = img_ref[strip_rows - HALO : strip_rows, :]
    for r, v in enumerate((y_bot, x_bot, f_bot, m_bot)):
        down_ref[0:1, r * LANES : (r + 1) * LANES] = v


def phase_kernel(
    final, above_col, below_row, below_col,
    band_ref, col_ref, cell_ref, psf_ref, nbm_ref, flag_ref,
    oy_ref, ox_ref, f_ref, w_ref, above_ref, img_ref, below_ref, fa_ref, fb_ref,
    *rest,
):
    if final:
        out_ref, canvas = rest
    else:
        fout_ref, up_ref, down_ref, canvas = rest
    ext_rows, pad_width = canvas.shape
    strip_rows, width = img_ref.shape
    own = oy_ref.shape[0]
    canvas[...] = jnp.zeros_like(canvas)
    hpos = lax.broadcasted_iota(jnp.int32, (ext_rows, LANES), 0).astype(jnp.float32) - HALO
    wpos = lax.broadcasted_iota(jnp.int32, (WIN, LANES), 0).astype(jnp.float32) - LANES
    keep_above = hpos < REACH

    specs = []
    for j in range(own):
        y = band_ref[j].astype(jnp.float32) + oy_ref[j : j + 1, :]
        specs.append((y, ox_ref[j : j + 1, :], f_ref[j : j + 1, :],
                      own_coefs(psf_ref, cell_ref, j), col_ref[j]))
    specs.append((
        above_ref[0:1, 0:LANES] - strip_rows, above_ref[0:1, LANES : 2 * LANES],
        fa_ref[0:1, above_col : above_col + LANES],
        [nbm_ref[k] for k in range(9)], nbm_ref[9].astype(jnp.int32),
    ))
    specs.append((
        below_ref[HALO - 1 : HALO, 0:LANES] + strip_rows,
        below_ref[HALO - 1 : HALO, LANES : 2 * LANES],
        fb_ref[below_row : below_row + 1, below_col : below_col + LANES],
        [nbm_ref[16 + k] for k in range(9)], nbm_ref[16 + 9].astype(jnp.int32),
    ))

    saved = []
    for j, (y, x, flux, c, col) in enumerate(specs):
        rows = profile3(hpos - y)
        if j == own:
            rows_model = tuple(jnp.where(keep_above, r, 0.0) for r in rows)
        else:
            rows_model = rows
        cols = profile3(wpos - x)
        stamp = None
        for a in range(3):
            mixed = (c[3 * a] * cols[0] + c[3 * a + 1] * cols[1] + c[3 * a + 2] * cols[2]) * flux
            part = lax.dot_general(
                rows_model[a], mixed, DIMS_NT, precision=HIGHEST,
                preferred_element_type=jnp.float32,
            )
            stamp = part if stamp is None else stamp + part
        start = pl.multiple_of(col * LANES, LANES)
        canvas[:, pl.ds(start, WIN)] += stamp
        if j < own:
            saved.append((rows, cols, c, start))
    inner = slice(LANES, LANES + width)
    if final:
        out_ref[...] = img_ref[...] - canvas[HALO : HALO + strip_rows, inner]
        return
    edge_ids = lax.broadcasted_iota(jnp.int32, (HALO, width), 0)
    top_ok = (edge_ids >= HALO - REACH) & (flag_ref[0] > 0)
    bot_ok = (edge_ids < REACH) & (flag_ref[1] > 0)
    top = jnp.where(top_ok, above_ref[...] - canvas[0:HALO, inner], 0.0)
    bot = jnp.where(bot_ok, below_ref[0:HALO, :] - canvas[HALO + strip_rows :, inner], 0.0)
    mid = img_ref[...] - canvas[HALO : HALO + strip_rows, inner]
    canvas[0:HALO, inner] = top
    canvas[HALO : HALO + strip_rows, inner] = mid
    canvas[HALO + strip_rows :, inner] = bot
    canvas[:, 0:LANES] = jnp.zeros((ext_rows, LANES), jnp.float32)
    canvas[:, LANES + width :] = jnp.zeros((ext_rows, pad_width - LANES - width), jnp.float32)
    news = []
    for j in range(own):
        rows, cols, c, start = saved[j]
        window = canvas[:, pl.ds(start, WIN)]
        across = [
            jnp.dot(window, cols[b], precision=HIGHEST, preferred_element_type=jnp.float32)
            for b in range(3)
        ]
        grad = None
        for a in range(3):
            for b in range(3):
                paired = jnp.sum(rows[a] * across[b], axis=0, keepdims=True)
                term = c[3 * a + b] * paired
                grad = term if grad is None else grad + term
        new = f_ref[j : j + 1, :] + 0.5 * grad / w_ref[j : j + 1, :]
        fout_ref[j : j + 1, :] = new
        news.append(new)
    top_first = band_ref[0] <= band_ref[1]
    up_ref[...] = jnp.where(top_first, news[0], news[1])
    down_ref[...] = jnp.where(top_first, news[1], news[0])


def local(image, band_row, col_block, cell_index, offset_y, offset_x, flux_start, psf_coef):
    strip_rows, strip_width = image.shape
    own = band_row.shape[0]
    f32 = jnp.float32
    smem = pl.BlockSpec(memory_space=pltpu.SMEM)
    vmem = pl.BlockSpec(memory_space=pltpu.VMEM)
    packet = jax.ShapeDtypeStruct((PACKET, strip_width), f32)
    send_up, send_down, weight = pl.pallas_call(
        setup_kernel,
        out_shape=(packet, packet, jax.ShapeDtypeStruct((own, LANES), f32)),
        in_specs=[smem] * 4 + [vmem] * 4,
        out_specs=(vmem, vmem, vmem),
    )(band_row, col_block, cell_index, psf_coef, image, offset_y, offset_x, flux_start)
    got_above, got_below = exchange(send_up, send_down)

    me = lax.axis_index("ty")
    last = lax.axis_size("ty") - 1
    flags = jnp.stack([me > 0, me < last]).astype(jnp.int32)
    nbm = jnp.concatenate(
        [got_above[0, 3 * LANES : 3 * LANES + 16], got_below[HALO - 1, 3 * LANES : 3 * LANES + 16]]
    )

    ext_rows = strip_rows + 2 * HALO
    blocks = own + 2
    flops = 6 * 2 * 3 * ext_rows * WIN * LANES * (blocks + own)
    flux_shape = jax.ShapeDtypeStruct((own, LANES), f32)
    edge_shape = jax.ShapeDtypeStruct((1, LANES), f32)
    common = (band_row, col_block, cell_index, psf_coef, nbm, flags,
              offset_y, offset_x)

    def phase(final, fluxes, fa, fb, flux_at):
        kernel = functools.partial(phase_kernel, final, *flux_at)
        if final:
            out_shape = jax.ShapeDtypeStruct((strip_rows, strip_width), f32)
            out_specs = vmem
        else:
            out_shape = (flux_shape, edge_shape, edge_shape)
            out_specs = (vmem, vmem, vmem)
        return pl.pallas_call(
            kernel,
            out_shape=out_shape,
            in_specs=[smem] * 6 + [vmem] * 9,
            out_specs=out_specs,
            scratch_shapes=[pltpu.VMEM((ext_rows, strip_width + 2 * LANES), f32)],
            cost_estimate=pl.CostEstimate(
                flops=flops, transcendentals=blocks * 2 * (ext_rows + WIN) * LANES,
                bytes_accessed=4 * ext_rows * strip_width * 2,
            ),
        )(*common, fluxes, weight, got_above, image, got_below, fa, fb)

    fluxes = flux_start
    fa, fb = got_above, got_below
    flux_at = (2 * LANES, HALO - 1, 2 * LANES)
    for iteration in range(ITERS):
        fluxes, new_top, new_bot = phase(False, fluxes, fa, fb, flux_at)
        fa, fb = exchange(new_top, new_bot)
        flux_at = (0, 0, 0)
    residual = phase(True, fluxes, fa, fb, flux_at)
    return (fluxes, residual)


def solution(mesh):
    return jax.shard_map(
        local,
        mesh=mesh,
        in_specs=(
            P(("groups", "ty"), None),
            P(("groups", "ty")),
            P(("groups", "ty")),
            P(("groups", "ty")),
            P(("groups", "ty"), None),
            P(("groups", "ty"), None),
            P(("groups", "ty"), None),
            P(),
        ),
        out_specs=(P(("groups", "ty"), None), P(("groups", "ty"), None)),
        check_vma=False,
    )
```

```python
import functools

import jax
import jax.numpy as jnp
from jax import lax
from jax.experimental import pallas as pl
from jax.experimental.pallas import tpu as pltpu
from jax.sharding import PartitionSpec as P

REACH = 15
ITERS = 2
HALO = 16
LANES = 128
WIN = 384
PACKET = HALO


HIGHEST = lax.Precision.HIGHEST
DIMS_NT = (((1,), (1,)), ((), ()))


def profile3(dist):
    tapered_arg = dist * (1.0 / 15.5)
    tapered = jnp.maximum(0.0, 1.0 - tapered_arg * tapered_arg)
    scaled = dist * (1.0 / 1.7)
    core_part = jnp.exp(-0.5 * scaled * scaled) * tapered
    wing_part = jnp.exp(dist * dist * (-1.0 / 72.0)) * tapered
    return core_part, scaled * core_part, wing_part


def exchange(to_above, to_below):
    count = lax.axis_size("ty")
    forward = [(i, i + 1) for i in range(count - 1)]
    backward = [(i + 1, i) for i in range(count - 1)]
    from_above = lax.ppermute(to_below, "ty", forward)
    from_below = lax.ppermute(to_above, "ty", backward)
    return from_above, from_below


def own_coefs(psf_ref, cell_ref, j):
    cell = cell_ref[j]
    return [psf_ref[k, cell] for k in range(9)]


def setup_kernel(
    band_ref, col_ref, cell_ref, psf_ref, img_ref, oy_ref, ox_ref, f_ref, up_ref, down_ref, w_ref
):
    strip_rows = img_ref.shape[0]
    own = oy_ref.shape[0]
    offs = lax.broadcasted_iota(jnp.int32, (32, LANES), 0).astype(jnp.float32) - 15.0
    lane = lax.broadcasted_iota(jnp.int32, (1, LANES), 1)
    ys, metas = [], []
    for j in range(own):
        y = band_ref[j].astype(jnp.float32) + oy_ref[j : j + 1, :]
        x = ox_ref[j : j + 1, :]
        c = own_coefs(psf_ref, cell_ref, j)
        rows = profile3(jnp.floor(y) + offs - y)
        cols = profile3(jnp.floor(x) + offs - x)
        gram_r = [[jnp.sum(rows[a] * rows[b], axis=0, keepdims=True) for b in range(3)] for a in range(3)]
        gram_c = [[jnp.sum(cols[a] * cols[b], axis=0, keepdims=True) for b in range(3)] for a in range(3)]
        weight = None
        for a in range(3):
            for cc in range(3):
                inner = None
                for b in range(3):
                    for d in range(3):
                        term = (c[3 * a + b] * c[3 * cc + d]) * gram_c[b][d]
                        inner = term if inner is None else inner + term
                term = gram_r[a][cc] * inner
                weight = term if weight is None else weight + term
        w_ref[j : j + 1, :] = weight
        meta = jnp.zeros((1, LANES), jnp.float32)
        for k in range(9):
            meta = jnp.where(lane == k, c[k], meta)
        meta = jnp.where(lane == 9, col_ref[j].astype(jnp.float32), meta)
        ys.append(y)
        metas.append(meta)
    top_first = band_ref[0] <= band_ref[1]

    def pick(first, second):
        return jnp.where(top_first, first, second), jnp.where(top_first, second, first)

    y_top, y_bot = pick(ys[0], ys[1])
    x_top, x_bot = pick(ox_ref[0:1, :], ox_ref[1:2, :])
    f_top, f_bot = pick(f_ref[0:1, :], f_ref[1:2, :])
    m_top, m_bot = pick(metas[0], metas[1])
    up_ref[...] = img_ref[0:HALO, :]
    for r, v in enumerate((y_top, x_top, f_top, m_top)):
        up_ref[HALO - 1 : HALO, r * LANES : (r + 1) * LANES] = v
    down_ref[...] = img_ref[strip_rows - HALO : strip_rows, :]
    for r, v in enumerate((y_bot, x_bot, f_bot, m_bot)):
        down_ref[0:1, r * LANES : (r + 1) * LANES] = v


def add_stamp(canvas, y, x, flux, c, col, keep_rows=None):
    ext_rows = canvas.shape[0]
    hpos = lax.broadcasted_iota(jnp.int32, (ext_rows, LANES), 0).astype(jnp.float32) - HALO
    wpos = lax.broadcasted_iota(jnp.int32, (WIN, LANES), 0).astype(jnp.float32) - LANES
    rows = profile3(hpos - y)
    if keep_rows is not None:
        rows = tuple(jnp.where(hpos < keep_rows, r, 0.0) for r in rows)
    cols = profile3(wpos - x)
    stamp = None
    for a in range(3):
        mixed = (c[3 * a] * cols[0] + c[3 * a + 1] * cols[1] + c[3 * a + 2] * cols[2]) * flux
        part = lax.dot_general(
            rows[a], mixed, DIMS_NT, precision=HIGHEST, preferred_element_type=jnp.float32,
        )
        stamp = part if stamp is None else stamp + part
    start = pl.multiple_of(col * LANES, LANES)
    canvas[:, pl.ds(start, WIN)] += stamp


def own_kernel(band_ref, col_ref, cell_ref, psf_ref, oy_ref, ox_ref, f_ref, canvas):
    canvas[...] = jnp.zeros_like(canvas)
    for j in range(oy_ref.shape[0]):
        y = band_ref[j].astype(jnp.float32) + oy_ref[j : j + 1, :]
        add_stamp(canvas, y, ox_ref[j : j + 1, :], f_ref[j : j + 1, :],
                  own_coefs(psf_ref, cell_ref, j), col_ref[j])


def phase_kernel(
    final, above_col, below_row, below_col,
    band_ref, col_ref, cell_ref, psf_ref, nbm_ref, flag_ref,
    oy_ref, ox_ref, f_ref, w_ref, above_ref, img_ref, below_ref, fa_ref, fb_ref, own_ref,
    *rest,
):
    if final:
        out_ref, canvas = rest
    else:
        fout_ref, up_ref, down_ref, canvas = rest
    ext_rows, pad_width = canvas.shape
    strip_rows, width = img_ref.shape
    own = oy_ref.shape[0]
    canvas[...] = own_ref[...]
    add_stamp(
        canvas, above_ref[0:1, 0:LANES] - strip_rows, above_ref[0:1, LANES : 2 * LANES],
        fa_ref[0:1, above_col : above_col + LANES],
        [nbm_ref[k] for k in range(9)], nbm_ref[9].astype(jnp.int32), keep_rows=REACH,
    )
    add_stamp(
        canvas, below_ref[HALO - 1 : HALO, 0:LANES] + strip_rows,
        below_ref[HALO - 1 : HALO, LANES : 2 * LANES],
        fb_ref[below_row : below_row + 1, below_col : below_col + LANES],
        [nbm_ref[16 + k] for k in range(9)], nbm_ref[16 + 9].astype(jnp.int32),
    )
    inner = slice(LANES, LANES + width)
    if final:
        out_ref[...] = img_ref[...] - canvas[HALO : HALO + strip_rows, inner]
        return
    edge_ids = lax.broadcasted_iota(jnp.int32, (HALO, width), 0)
    top_ok = (edge_ids >= HALO - REACH) & (flag_ref[0] > 0)
    bot_ok = (edge_ids < REACH) & (flag_ref[1] > 0)
    top = jnp.where(top_ok, above_ref[...] - canvas[0:HALO, inner], 0.0)
    bot = jnp.where(bot_ok, below_ref[0:HALO, :] - canvas[HALO + strip_rows :, inner], 0.0)
    mid = img_ref[...] - canvas[HALO : HALO + strip_rows, inner]
    canvas[0:HALO, inner] = top
    canvas[HALO : HALO + strip_rows, inner] = mid
    canvas[HALO + strip_rows :, inner] = bot
    canvas[:, 0:LANES] = jnp.zeros((ext_rows, LANES), jnp.float32)
    canvas[:, LANES + width :] = jnp.zeros((ext_rows, pad_width - LANES - width), jnp.float32)
    hpos = lax.broadcasted_iota(jnp.int32, (ext_rows, LANES), 0).astype(jnp.float32) - HALO
    wpos = lax.broadcasted_iota(jnp.int32, (WIN, LANES), 0).astype(jnp.float32) - LANES
    news = []
    for j in range(own):
        y = band_ref[j].astype(jnp.float32) + oy_ref[j : j + 1, :]
        rows = profile3(hpos - y)
        cols = profile3(wpos - ox_ref[j : j + 1, :])
        c = own_coefs(psf_ref, cell_ref, j)
        start = pl.multiple_of(col_ref[j] * LANES, LANES)
        window = canvas[:, pl.ds(start, WIN)]
        across = [
            jnp.dot(window, cols[b], precision=HIGHEST, preferred_element_type=jnp.float32)
            for b in range(3)
        ]
        grad = None
        for a in range(3):
            for b in range(3):
                paired = jnp.sum(rows[a] * across[b], axis=0, keepdims=True)
                term = c[3 * a + b] * paired
                grad = term if grad is None else grad + term
        new = f_ref[j : j + 1, :] + 0.5 * grad / w_ref[j : j + 1, :]
        fout_ref[j : j + 1, :] = new
        news.append(new)
    top_first = band_ref[0] <= band_ref[1]
    up_ref[...] = jnp.where(top_first, news[0], news[1])
    down_ref[...] = jnp.where(top_first, news[1], news[0])


def local(image, band_row, col_block, cell_index, offset_y, offset_x, flux_start, psf_coef):
    strip_rows, strip_width = image.shape
    own = band_row.shape[0]
    f32 = jnp.float32
    smem = pl.BlockSpec(memory_space=pltpu.SMEM)
    vmem = pl.BlockSpec(memory_space=pltpu.VMEM)
    packet = jax.ShapeDtypeStruct((PACKET, strip_width), f32)
    send_up, send_down, weight = pl.pallas_call(
        setup_kernel,
        out_shape=(packet, packet, jax.ShapeDtypeStruct((own, LANES), f32)),
        in_specs=[smem] * 4 + [vmem] * 4,
        out_specs=(vmem, vmem, vmem),
    )(band_row, col_block, cell_index, psf_coef, image, offset_y, offset_x, flux_start)
    got_above, got_below = exchange(send_up, send_down)

    me = lax.axis_index("ty")
    last = lax.axis_size("ty") - 1
    flags = jnp.stack([me > 0, me < last]).astype(jnp.int32)
    nbm = jnp.concatenate(
        [got_above[0, 3 * LANES : 3 * LANES + 16], got_below[HALO - 1, 3 * LANES : 3 * LANES + 16]]
    )

    ext_rows = strip_rows + 2 * HALO
    blocks = own + 2
    flops = 6 * 2 * 3 * ext_rows * WIN * LANES * (blocks + own)
    flux_shape = jax.ShapeDtypeStruct((own, LANES), f32)
    edge_shape = jax.ShapeDtypeStruct((1, LANES), f32)
    common = (band_row, col_block, cell_index, psf_coef, nbm, flags,
              offset_y, offset_x)

    canvas_shape = jax.ShapeDtypeStruct((ext_rows, strip_width + 2 * LANES), f32)

    def own_part(fluxes):
        return pl.pallas_call(
            own_kernel,
            out_shape=canvas_shape,
            in_specs=[smem] * 4 + [vmem] * 3,
            out_specs=vmem,
            cost_estimate=pl.CostEstimate(
                flops=flops * own // (blocks + own), transcendentals=own * 2 * (ext_rows + WIN) * LANES,
                bytes_accessed=4 * ext_rows * (strip_width + 2 * LANES),
            ),
        )(band_row, col_block, cell_index, psf_coef, offset_y, offset_x, fluxes)

    def phase(final, fluxes, fa, fb, flux_at):
        kernel = functools.partial(phase_kernel, final, *flux_at)
        if final:
            out_shape = jax.ShapeDtypeStruct((strip_rows, strip_width), f32)
            out_specs = vmem
        else:
            out_shape = (flux_shape, edge_shape, edge_shape)
            out_specs = (vmem, vmem, vmem)
        return pl.pallas_call(
            kernel,
            out_shape=out_shape,
            in_specs=[smem] * 6 + [vmem] * 10,
            out_specs=out_specs,
            scratch_shapes=[pltpu.VMEM((ext_rows, strip_width + 2 * LANES), f32)],
            cost_estimate=pl.CostEstimate(
                flops=flops, transcendentals=blocks * 2 * (ext_rows + WIN) * LANES,
                bytes_accessed=4 * ext_rows * strip_width * 2,
            ),
        )(*common, fluxes, weight, got_above, image, got_below, fa, fb, own_part(fluxes))

    fluxes = flux_start
    fa, fb = got_above, got_below
    flux_at = (2 * LANES, HALO - 1, 2 * LANES)
    for iteration in range(ITERS):
        fluxes, new_top, new_bot = phase(False, fluxes, fa, fb, flux_at)
        fa, fb = exchange(new_top, new_bot)
        flux_at = (0, 0, 0)
    residual = phase(True, fluxes, fa, fb, flux_at)
    return (fluxes, residual)


def solution(mesh):
    return jax.shard_map(
        local,
        mesh=mesh,
        in_specs=(
            P(("groups", "ty"), None),
            P(("groups", "ty")),
            P(("groups", "ty")),
            P(("groups", "ty")),
            P(("groups", "ty"), None),
            P(("groups", "ty"), None),
            P(("groups", "ty"), None),
            P(),
        ),
        out_specs=(P(("groups", "ty"), None), P(("groups", "ty"), None)),
        check_vma=False,
    )
```

```python
import functools

import jax
import jax.numpy as jnp
from jax import lax
from jax.experimental import pallas as pl
from jax.experimental.pallas import tpu as pltpu
from jax.sharding import PartitionSpec as P

REACH = 15
ITERS = 2
HALO = 16
LANES = 128
WIN = 384
PACKET = HALO


HIGHEST = lax.Precision.HIGHEST
DIMS_NT = (((1,), (1,)), ((), ()))


def profile3(dist):
    tapered_arg = dist * (1.0 / 15.5)
    tapered = jnp.maximum(0.0, 1.0 - tapered_arg * tapered_arg)
    scaled = dist * (1.0 / 1.7)
    core_part = jnp.exp(-0.5 * scaled * scaled) * tapered
    wing_part = jnp.exp(dist * dist * (-1.0 / 72.0)) * tapered
    return core_part, scaled * core_part, wing_part


def split_dot(lhs, rhs, dims):
    lhs_hi = lhs.astype(jnp.bfloat16)
    lhs_lo = (lhs - lhs_hi.astype(jnp.float32)).astype(jnp.bfloat16)
    rhs_hi = rhs.astype(jnp.bfloat16)
    rhs_lo = (rhs - rhs_hi.astype(jnp.float32)).astype(jnp.bfloat16)

    def one(a, b):
        return lax.dot_general(a, b, dims, preferred_element_type=jnp.float32)

    return one(lhs_hi, rhs_hi) + (one(lhs_hi, rhs_lo) + one(lhs_lo, rhs_hi))


DIMS_NN = (((1,), (0,)), ((), ()))


def exchange(to_above, to_below):
    count = lax.axis_size("ty")
    forward = [(i, i + 1) for i in range(count - 1)]
    backward = [(i + 1, i) for i in range(count - 1)]
    from_above = lax.ppermute(to_below, "ty", forward)
    from_below = lax.ppermute(to_above, "ty", backward)
    return from_above, from_below


def own_coefs(psf_ref, cell_ref, j):
    cell = cell_ref[j]
    return [psf_ref[k, cell] for k in range(9)]


def setup_kernel(
    band_ref, col_ref, cell_ref, psf_ref, img_ref, oy_ref, ox_ref, f_ref, up_ref, down_ref, w_ref
):
    strip_rows = img_ref.shape[0]
    own = oy_ref.shape[0]
    offs = lax.broadcasted_iota(jnp.int32, (32, LANES), 0).astype(jnp.float32) - 15.0
    lane = lax.broadcasted_iota(jnp.int32, (1, LANES), 1)
    ys, metas = [], []
    for j in range(own):
        y = band_ref[j].astype(jnp.float32) + oy_ref[j : j + 1, :]
        x = ox_ref[j : j + 1, :]
        c = own_coefs(psf_ref, cell_ref, j)
        rows = profile3(jnp.floor(y) + offs - y)
        cols = profile3(jnp.floor(x) + offs - x)
        gram_r = [[jnp.sum(rows[a] * rows[b], axis=0, keepdims=True) for b in range(3)] for a in range(3)]
        gram_c = [[jnp.sum(cols[a] * cols[b], axis=0, keepdims=True) for b in range(3)] for a in range(3)]
        weight = None
        for a in range(3):
            for cc in range(3):
                inner = None
                for b in range(3):
                    for d in range(3):
                        term = (c[3 * a + b] * c[3 * cc + d]) * gram_c[b][d]
                        inner = term if inner is None else inner + term
                term = gram_r[a][cc] * inner
                weight = term if weight is None else weight + term
        w_ref[j : j + 1, :] = weight
        meta = jnp.zeros((1, LANES), jnp.float32)
        for k in range(9):
            meta = jnp.where(lane == k, c[k], meta)
        meta = jnp.where(lane == 9, col_ref[j].astype(jnp.float32), meta)
        ys.append(y)
        metas.append(meta)
    top_first = band_ref[0] <= band_ref[1]

    def pick(first, second):
        return jnp.where(top_first, first, second), jnp.where(top_first, second, first)

    y_top, y_bot = pick(ys[0], ys[1])
    x_top, x_bot = pick(ox_ref[0:1, :], ox_ref[1:2, :])
    f_top, f_bot = pick(f_ref[0:1, :], f_ref[1:2, :])
    m_top, m_bot = pick(metas[0], metas[1])
    up_ref[...] = img_ref[0:HALO, :]
    for r, v in enumerate((y_top, x_top, f_top, m_top)):
        up_ref[HALO - 1 : HALO, r * LANES : (r + 1) * LANES] = v
    down_ref[...] = img_ref[strip_rows - HALO : strip_rows, :]
    for r, v in enumerate((y_bot, x_bot, f_bot, m_bot)):
        down_ref[0:1, r * LANES : (r + 1) * LANES] = v


def phase_kernel(
    final, above_col, below_row, below_col,
    band_ref, col_ref, cell_ref, psf_ref, nbm_ref, flag_ref,
    oy_ref, ox_ref, f_ref, w_ref, above_ref, img_ref, below_ref, fa_ref, fb_ref,
    *rest,
):
    if final:
        out_ref, canvas = rest
    else:
        fout_ref, up_ref, down_ref, canvas = rest
    ext_rows, pad_width = canvas.shape
    strip_rows, width = img_ref.shape
    own = oy_ref.shape[0]
    canvas[...] = jnp.zeros_like(canvas)
    hpos = lax.broadcasted_iota(jnp.int32, (ext_rows, LANES), 0).astype(jnp.float32) - HALO
    wpos = lax.broadcasted_iota(jnp.int32, (WIN, LANES), 0).astype(jnp.float32) - LANES
    keep_above = hpos < REACH

    specs = []
    for j in range(own):
        y = band_ref[j].astype(jnp.float32) + oy_ref[j : j + 1, :]
        specs.append((y, ox_ref[j : j + 1, :], f_ref[j : j + 1, :],
                      own_coefs(psf_ref, cell_ref, j), col_ref[j]))
    specs.append((
        above_ref[0:1, 0:LANES] - strip_rows, above_ref[0:1, LANES : 2 * LANES],
        fa_ref[0:1, above_col : above_col + LANES],
        [nbm_ref[k] for k in range(9)], nbm_ref[9].astype(jnp.int32),
    ))
    specs.append((
        below_ref[HALO - 1 : HALO, 0:LANES] + strip_rows,
        below_ref[HALO - 1 : HALO, LANES : 2 * LANES],
        fb_ref[below_row : below_row + 1, below_col : below_col + LANES],
        [nbm_ref[16 + k] for k in range(9)], nbm_ref[16 + 9].astype(jnp.int32),
    ))

    saved = []
    for j, (y, x, flux, c, col) in enumerate(specs):
        rows = profile3(hpos - y)
        if j == own:
            rows_model = tuple(jnp.where(keep_above, r, 0.0) for r in rows)
        else:
            rows_model = rows
        cols = profile3(wpos - x)
        mixed = [
            (c[3 * a] * cols[0] + c[3 * a + 1] * cols[1] + c[3 * a + 2] * cols[2]) * flux
            for a in range(3)
        ]
        stamp = split_dot(
            jnp.concatenate(rows_model, axis=1), jnp.concatenate(mixed, axis=1), DIMS_NT
        )
        start = pl.multiple_of(col * LANES, LANES)
        canvas[:, pl.ds(start, WIN)] += stamp
        if j < own:
            saved.append((rows, cols, c, start))
    inner = slice(LANES, LANES + width)
    if final:
        out_ref[...] = img_ref[...] - canvas[HALO : HALO + strip_rows, inner]
        return
    edge_ids = lax.broadcasted_iota(jnp.int32, (HALO, width), 0)
    top_ok = (edge_ids >= HALO - REACH) & (flag_ref[0] > 0)
    bot_ok = (edge_ids < REACH) & (flag_ref[1] > 0)
    top = jnp.where(top_ok, above_ref[...] - canvas[0:HALO, inner], 0.0)
    bot = jnp.where(bot_ok, below_ref[0:HALO, :] - canvas[HALO + strip_rows :, inner], 0.0)
    mid = img_ref[...] - canvas[HALO : HALO + strip_rows, inner]
    canvas[0:HALO, inner] = top
    canvas[HALO : HALO + strip_rows, inner] = mid
    canvas[HALO + strip_rows :, inner] = bot
    canvas[:, 0:LANES] = jnp.zeros((ext_rows, LANES), jnp.float32)
    canvas[:, LANES + width :] = jnp.zeros((ext_rows, pad_width - LANES - width), jnp.float32)
    news = []
    for j in range(own):
        rows, cols, c, start = saved[j]
        window = canvas[:, pl.ds(start, WIN)]
        across_all = split_dot(window, jnp.concatenate(cols, axis=1), DIMS_NN)
        across = [across_all[:, b * LANES : (b + 1) * LANES] for b in range(3)]
        grad = None
        for a in range(3):
            for b in range(3):
                paired = jnp.sum(rows[a] * across[b], axis=0, keepdims=True)
                term = c[3 * a + b] * paired
                grad = term if grad is None else grad + term
        new = f_ref[j : j + 1, :] + 0.5 * grad / w_ref[j : j + 1, :]
        fout_ref[j : j + 1, :] = new
        news.append(new)
    top_first = band_ref[0] <= band_ref[1]
    up_ref[...] = jnp.where(top_first, news[0], news[1])
    down_ref[...] = jnp.where(top_first, news[1], news[0])


def local(image, band_row, col_block, cell_index, offset_y, offset_x, flux_start, psf_coef):
    strip_rows, strip_width = image.shape
    own = band_row.shape[0]
    f32 = jnp.float32
    smem = pl.BlockSpec(memory_space=pltpu.SMEM)
    vmem = pl.BlockSpec(memory_space=pltpu.VMEM)
    packet = jax.ShapeDtypeStruct((PACKET, strip_width), f32)
    send_up, send_down, weight = pl.pallas_call(
        setup_kernel,
        out_shape=(packet, packet, jax.ShapeDtypeStruct((own, LANES), f32)),
        in_specs=[smem] * 4 + [vmem] * 4,
        out_specs=(vmem, vmem, vmem),
    )(band_row, col_block, cell_index, psf_coef, image, offset_y, offset_x, flux_start)
    got_above, got_below = exchange(send_up, send_down)

    me = lax.axis_index("ty")
    last = lax.axis_size("ty") - 1
    flags = jnp.stack([me > 0, me < last]).astype(jnp.int32)
    nbm = jnp.concatenate(
        [got_above[0, 3 * LANES : 3 * LANES + 16], got_below[HALO - 1, 3 * LANES : 3 * LANES + 16]]
    )

    ext_rows = strip_rows + 2 * HALO
    blocks = own + 2
    flops = 6 * 2 * 3 * ext_rows * WIN * LANES * (blocks + own)
    flux_shape = jax.ShapeDtypeStruct((own, LANES), f32)
    edge_shape = jax.ShapeDtypeStruct((1, LANES), f32)
    common = (band_row, col_block, cell_index, psf_coef, nbm, flags,
              offset_y, offset_x)

    def phase(final, fluxes, fa, fb, flux_at):
        kernel = functools.partial(phase_kernel, final, *flux_at)
        if final:
            out_shape = jax.ShapeDtypeStruct((strip_rows, strip_width), f32)
            out_specs = vmem
        else:
            out_shape = (flux_shape, edge_shape, edge_shape)
            out_specs = (vmem, vmem, vmem)
        return pl.pallas_call(
            kernel,
            out_shape=out_shape,
            in_specs=[smem] * 6 + [vmem] * 9,
            out_specs=out_specs,
            scratch_shapes=[pltpu.VMEM((ext_rows, strip_width + 2 * LANES), f32)],
            cost_estimate=pl.CostEstimate(
                flops=flops, transcendentals=blocks * 2 * (ext_rows + WIN) * LANES,
                bytes_accessed=4 * ext_rows * strip_width * 2,
            ),
        )(*common, fluxes, weight, got_above, image, got_below, fa, fb)

    fluxes = flux_start
    fa, fb = got_above, got_below
    flux_at = (2 * LANES, HALO - 1, 2 * LANES)
    for iteration in range(ITERS):
        fluxes, new_top, new_bot = phase(False, fluxes, fa, fb, flux_at)
        fa, fb = exchange(new_top, new_bot)
        flux_at = (0, 0, 0)
    residual = phase(True, fluxes, fa, fb, flux_at)
    return (fluxes, residual)


def solution(mesh):
    return jax.shard_map(
        local,
        mesh=mesh,
        in_specs=(
            P(("groups", "ty"), None),
            P(("groups", "ty")),
            P(("groups", "ty")),
            P(("groups", "ty")),
            P(("groups", "ty"), None),
            P(("groups", "ty"), None),
            P(("groups", "ty"), None),
            P(),
        ),
        out_specs=(P(("groups", "ty"), None), P(("groups", "ty"), None)),
        check_vma=False,
    )
```

```python
import functools

import jax
import jax.numpy as jnp
from jax import lax
from jax.experimental import pallas as pl
from jax.experimental.pallas import tpu as pltpu
from jax.sharding import PartitionSpec as P

REACH = 15
ITERS = 2
LANES = 128
WIN = 384
SLOTS = 8

DIMS_NT = (((1,), (1,)), ((), ()))
DIMS_NN = (((1,), (0,)), ((), ()))


def profile3(dist):
    tapered_arg = dist * (1.0 / 15.5)
    tapered = jnp.maximum(0.0, 1.0 - tapered_arg * tapered_arg)
    scaled = dist * (1.0 / 1.7)
    core_part = jnp.exp(-0.5 * scaled * scaled) * tapered
    wing_part = jnp.exp(dist * dist * (-1.0 / 72.0)) * tapered
    return core_part, scaled * core_part, wing_part


def split_dot(lhs, rhs, dims):
    lhs_hi = lhs.astype(jnp.bfloat16)
    lhs_lo = (lhs - lhs_hi.astype(jnp.float32)).astype(jnp.bfloat16)
    rhs_hi = rhs.astype(jnp.bfloat16)
    rhs_lo = (rhs - rhs_hi.astype(jnp.float32)).astype(jnp.bfloat16)

    def one(a, b):
        return lax.dot_general(a, b, dims, preferred_element_type=jnp.float32)

    return one(lhs_hi, rhs_hi) + (one(lhs_hi, rhs_lo) + one(lhs_lo, rhs_hi))


def exchange(to_above, to_below):
    count = lax.axis_size("ty")
    forward = [(i, i + 1) for i in range(count - 1)]
    backward = [(i + 1, i) for i in range(count - 1)]
    from_above = lax.ppermute(to_below, "ty", forward)
    from_below = lax.ppermute(to_above, "ty", backward)
    return from_above, from_below


def own_coefs(psf_ref, cell_ref, j):
    cell = cell_ref[j]
    return [psf_ref[k, cell] for k in range(9)]


def setup_kernel(band_ref, col_ref, cell_ref, psf_ref, oy_ref, ox_ref, f_ref, up_ref, down_ref, w_ref):
    own = oy_ref.shape[0]
    offs = lax.broadcasted_iota(jnp.int32, (32, LANES), 0).astype(jnp.float32) - 15.0
    lane = lax.broadcasted_iota(jnp.int32, (1, LANES), 1)
    ys, metas, weights = [], [], []
    for j in range(own):
        y = band_ref[j].astype(jnp.float32) + oy_ref[j : j + 1, :]
        x = ox_ref[j : j + 1, :]
        c = own_coefs(psf_ref, cell_ref, j)
        rows = profile3(jnp.floor(y) + offs - y)
        cols = profile3(jnp.floor(x) + offs - x)
        gram_r = [[jnp.sum(rows[a] * rows[b], axis=0, keepdims=True) for b in range(3)] for a in range(3)]
        gram_c = [[jnp.sum(cols[a] * cols[b], axis=0, keepdims=True) for b in range(3)] for a in range(3)]
        weight = None
        for a in range(3):
            for cc in range(3):
                inner = None
                for b in range(3):
                    for d in range(3):
                        term = (c[3 * a + b] * c[3 * cc + d]) * gram_c[b][d]
                        inner = term if inner is None else inner + term
                term = gram_r[a][cc] * inner
                weight = term if weight is None else weight + term
        w_ref[j : j + 1, :] = weight
        meta = jnp.zeros((1, LANES), jnp.float32)
        for k in range(9):
            meta = jnp.where(lane == k, c[k], meta)
        meta = jnp.where(lane == 9, col_ref[j].astype(jnp.float32), meta)
        ys.append(y)
        metas.append(meta)
        weights.append(weight)
    top_first = band_ref[0] <= band_ref[1]

    def pick(first, second):
        return jnp.where(top_first, first, second), jnp.where(top_first, second, first)

    tops, bots = zip(*[
        pick(*pair) for pair in (
            (ys[0], ys[1]), (ox_ref[0:1, :], ox_ref[1:2, :]), (f_ref[0:1, :], f_ref[1:2, :]),
            (weights[0], weights[1]), (metas[0], metas[1]),
        )
    ])
    up_ref[...] = jnp.zeros_like(up_ref)
    down_ref[...] = jnp.zeros_like(down_ref)
    for r in range(5):
        up_ref[r : r + 1, :] = tops[r]
        down_ref[r : r + 1, :] = bots[r]


def phase_kernel(
    final, first,
    band_ref, col_ref, cell_ref, psf_ref, pas_ref, pbs_ref,
    oy_ref, ox_ref, w_ref, pa_ref, pb_ref, img_ref, f_ref, l_ref, ra_ref, rb_ref,
    *rest,
):
    if final:
        out_ref, fluxout_ref, canvas = rest
    else:
        fout_ref, lout_ref, up_ref, down_ref, canvas = rest
    rows_n, pad_width = canvas.shape
    strip_rows, width = img_ref.shape
    own = oy_ref.shape[0]
    top_first = band_ref[0] <= band_ref[1]

    if first:
        fluxes = [f_ref[0:1, :], f_ref[1:2, :], pa_ref[2:3, :], pb_ref[2:3, :]]
    else:
        weights = [w_ref[0:1, :], w_ref[1:2, :], pa_ref[3:4, :], pb_ref[3:4, :]]
        from_above = ra_ref[0:1, :]
        from_below = rb_ref[0:1, :]
        extra = [
            jnp.where(top_first, from_above, from_below),
            jnp.where(top_first, from_below, from_above),
            ra_ref[1:2, :],
            rb_ref[1:2, :],
        ]
        fluxes = []
        for j in range(own + 2):
            grad = l_ref[j : j + 1, :] + extra[j]
            safe = jnp.where(weights[j] == 0.0, 1.0, weights[j])
            fluxes.append(f_ref[j : j + 1, :] + 0.5 * grad / safe)

    specs = []
    for j in range(own):
        y = band_ref[j].astype(jnp.float32) + oy_ref[j : j + 1, :]
        specs.append((y, ox_ref[j : j + 1, :], own_coefs(psf_ref, cell_ref, j), col_ref[j], None))
    specs.append((
        pa_ref[0:1, :] - strip_rows, pa_ref[1:2, :], [pas_ref[4, k] for k in range(9)],
        pas_ref[4, 9].astype(jnp.int32), REACH,
    ))
    specs.append((
        pb_ref[0:1, :] + strip_rows, pb_ref[1:2, :], [pbs_ref[4, k] for k in range(9)],
        pbs_ref[4, 9].astype(jnp.int32), None,
    ))

    canvas[...] = jnp.zeros_like(canvas)
    hpos = lax.broadcasted_iota(jnp.int32, (rows_n, LANES), 0).astype(jnp.float32)
    wpos = lax.broadcasted_iota(jnp.int32, (WIN, LANES), 0).astype(jnp.float32) - LANES
    saved = []
    for j, (y, x, c, col, keep) in enumerate(specs):
        rows = profile3(hpos - y)
        if keep is not None:
            rows = tuple(jnp.where(hpos < keep, r, 0.0) for r in rows)
        cols = profile3(wpos - x)
        mixed = [
            (c[3 * a] * cols[0] + c[3 * a + 1] * cols[1] + c[3 * a + 2] * cols[2]) * fluxes[j]
            for a in range(3)
        ]
        stamp = split_dot(jnp.concatenate(rows, axis=1), jnp.concatenate(mixed, axis=1), DIMS_NT)
        start = pl.multiple_of(col * LANES, LANES)
        canvas[:, pl.ds(start, WIN)] += stamp
        saved.append((rows, cols, c, start))
    inner = slice(LANES, LANES + width)
    if final:
        out_ref[...] = img_ref[...] - canvas[:, inner]
        for j in range(own):
            fluxout_ref[j : j + 1, :] = fluxes[j]
        return
    canvas[:, inner] = img_ref[...] - canvas[:, inner]
    canvas[:, 0:LANES] = jnp.zeros((rows_n, LANES), jnp.float32)
    canvas[:, LANES + width :] = jnp.zeros((rows_n, pad_width - LANES - width), jnp.float32)
    fout_ref[...] = jnp.zeros_like(fout_ref)
    lout_ref[...] = jnp.zeros_like(lout_ref)
    partial = []
    for j, (rows, cols, c, start) in enumerate(saved):
        window = canvas[:, pl.ds(start, WIN)]
        across_all = split_dot(window, jnp.concatenate(cols, axis=1), DIMS_NN)
        grad = None
        for a in range(3):
            for b in range(3):
                paired = jnp.sum(rows[a] * across_all[:, b * LANES : (b + 1) * LANES], axis=0,
                                 keepdims=True)
                term = c[3 * a + b] * paired
                grad = term if grad is None else grad + term
        partial.append(grad)
        fout_ref[j : j + 1, :] = fluxes[j]
        lout_ref[j : j + 1, :] = grad
    top_part = jnp.where(top_first, partial[0], partial[1])
    bot_part = jnp.where(top_first, partial[1], partial[0])
    up_ref[0:1, :] = partial[own]
    up_ref[1:2, :] = top_part
    down_ref[0:1, :] = partial[own + 1]
    down_ref[1:2, :] = bot_part


def local(image, band_row, col_block, cell_index, offset_y, offset_x, flux_start, psf_coef):
    strip_rows, strip_width = image.shape
    own = band_row.shape[0]
    f32 = jnp.float32
    smem = pl.BlockSpec(memory_space=pltpu.SMEM)
    vmem = pl.BlockSpec(memory_space=pltpu.VMEM)
    packet = jax.ShapeDtypeStruct((SLOTS, LANES), f32)
    send_up, send_down, weight = pl.pallas_call(
        setup_kernel,
        out_shape=(packet, packet, jax.ShapeDtypeStruct((own, LANES), f32)),
        in_specs=[smem] * 4 + [vmem] * 3,
        out_specs=(vmem, vmem, vmem),
    )(band_row, col_block, cell_index, psf_coef, offset_y, offset_x, flux_start)
    got_above, got_below = exchange(send_up, send_down)

    blocks = own + 2
    flops = 2 * 3 * 2 * strip_rows * WIN * 3 * LANES * blocks
    state_shape = jax.ShapeDtypeStruct((SLOTS, LANES), f32)
    part_shape = jax.ShapeDtypeStruct((2, LANES), f32)
    common = (band_row, col_block, cell_index, psf_coef, got_above, got_below,
              offset_y, offset_x, weight, got_above, got_below, image)

    def phase(final, first, fluxes, partials, from_above, from_below):
        kernel = functools.partial(phase_kernel, final, first)
        if final:
            out_shape = (jax.ShapeDtypeStruct((strip_rows, strip_width), f32),
                         jax.ShapeDtypeStruct((own, LANES), f32))
            out_specs = (vmem, vmem)
        else:
            out_shape = (state_shape, state_shape, part_shape, part_shape)
            out_specs = (vmem, vmem, vmem, vmem)
        return pl.pallas_call(
            kernel,
            out_shape=out_shape,
            in_specs=[smem] * 6 + [vmem] * 10,
            out_specs=out_specs,
            scratch_shapes=[pltpu.VMEM((strip_rows, strip_width + 2 * LANES), f32)],
            cost_estimate=pl.CostEstimate(
                flops=flops, transcendentals=blocks * 2 * (strip_rows + WIN) * LANES,
                bytes_accessed=4 * strip_rows * strip_width * 2,
            ),
        )(*common, fluxes, partials, from_above, from_below)

    state, partials, up, down = phase(False, True, flux_start, flux_start, flux_start, flux_start)
    for iteration in range(1, ITERS):
        from_above, from_below = exchange(up, down)
        state, partials, up, down = phase(False, False, state, partials, from_above, from_below)
    from_above, from_below = exchange(up, down)
    residual, fluxes = phase(True, False, state, partials, from_above, from_below)
    return (fluxes, residual)


def solution(mesh):
    return jax.shard_map(
        local,
        mesh=mesh,
        in_specs=(
            P(("groups", "ty"), None),
            P(("groups", "ty")),
            P(("groups", "ty")),
            P(("groups", "ty")),
            P(("groups", "ty"), None),
            P(("groups", "ty"), None),
            P(("groups", "ty"), None),
            P(),
        ),
        out_specs=(P(("groups", "ty"), None), P(("groups", "ty"), None)),
        check_vma=False,
    )
```

```python
import functools

import jax
import jax.numpy as jnp
from jax import lax
from jax.experimental import pallas as pl
from jax.experimental.pallas import tpu as pltpu
from jax.sharding import PartitionSpec as P

REACH = 15
ITERS = 2
LANES = 128
WIN = 384
SLOTS = 8

DIMS_NT = (((1,), (1,)), ((), ()))
DIMS_NN = (((1,), (0,)), ((), ()))


def profile3(dist):
    tapered_arg = dist * (1.0 / 15.5)
    tapered = jnp.maximum(0.0, 1.0 - tapered_arg * tapered_arg)
    scaled = dist * (1.0 / 1.7)
    core_part = jnp.exp(-0.5 * scaled * scaled) * tapered
    wing_part = jnp.exp(dist * dist * (-1.0 / 72.0)) * tapered
    return core_part, scaled * core_part, wing_part


def split_dot(lhs, rhs, dims):
    lhs_hi = lhs.astype(jnp.bfloat16)
    lhs_lo = (lhs - lhs_hi.astype(jnp.float32)).astype(jnp.bfloat16)
    rhs_hi = rhs.astype(jnp.bfloat16)
    rhs_lo = (rhs - rhs_hi.astype(jnp.float32)).astype(jnp.bfloat16)

    def one(a, b):
        return lax.dot_general(a, b, dims, preferred_element_type=jnp.float32)

    return one(lhs_hi, rhs_hi) + (one(lhs_hi, rhs_lo) + one(lhs_lo, rhs_hi))


def exchange(to_above, to_below):
    count = lax.axis_size("ty")
    forward = [(i, i + 1) for i in range(count - 1)]
    backward = [(i + 1, i) for i in range(count - 1)]
    from_above = lax.ppermute(to_below, "ty", forward)
    from_below = lax.ppermute(to_above, "ty", backward)
    return from_above, from_below


def own_coefs(psf_ref, cell_ref, j):
    cell = cell_ref[j]
    return [psf_ref[k, cell] for k in range(9)]


def setup_kernel(band_ref, col_ref, cell_ref, psf_ref, oy_ref, ox_ref, f_ref, up_ref, down_ref, w_ref):
    own = oy_ref.shape[0]
    offs = lax.broadcasted_iota(jnp.int32, (32, LANES), 0).astype(jnp.float32) - 15.0
    lane = lax.broadcasted_iota(jnp.int32, (1, LANES), 1)
    ys, metas, weights = [], [], []
    for j in range(own):
        y = band_ref[j].astype(jnp.float32) + oy_ref[j : j + 1, :]
        x = ox_ref[j : j + 1, :]
        c = own_coefs(psf_ref, cell_ref, j)
        rows = profile3(jnp.floor(y) + offs - y)
        cols = profile3(jnp.floor(x) + offs - x)
        gram_r = [[jnp.sum(rows[a] * rows[b], axis=0, keepdims=True) for b in range(3)] for a in range(3)]
        gram_c = [[jnp.sum(cols[a] * cols[b], axis=0, keepdims=True) for b in range(3)] for a in range(3)]
        weight = None
        for a in range(3):
            for cc in range(3):
                inner = None
                for b in range(3):
                    for d in range(3):
                        term = (c[3 * a + b] * c[3 * cc + d]) * gram_c[b][d]
                        inner = term if inner is None else inner + term
                term = gram_r[a][cc] * inner
                weight = term if weight is None else weight + term
        w_ref[j : j + 1, :] = weight
        meta = jnp.zeros((1, LANES), jnp.float32)
        for k in range(9):
            meta = jnp.where(lane == k, c[k], meta)
        meta = jnp.where(lane == 9, col_ref[j].astype(jnp.float32), meta)
        ys.append(y)
        metas.append(meta)
        weights.append(weight)
    top_first = band_ref[0] <= band_ref[1]

    def pick(first, second):
        return jnp.where(top_first, first, second), jnp.where(top_first, second, first)

    tops, bots = zip(*[
        pick(*pair) for pair in (
            (ys[0], ys[1]), (ox_ref[0:1, :], ox_ref[1:2, :]), (f_ref[0:1, :], f_ref[1:2, :]),
            (weights[0], weights[1]), (metas[0], metas[1]),
        )
    ])
    up_ref[...] = jnp.zeros_like(up_ref)
    down_ref[...] = jnp.zeros_like(down_ref)
    for r in range(5):
        up_ref[r : r + 1, :] = tops[r]
        down_ref[r : r + 1, :] = bots[r]


def phase_kernel(
    final, first,
    band_ref, col_ref, cell_ref, psf_ref, pas_ref, pbs_ref,
    oy_ref, ox_ref, w_ref, pa_ref, pb_ref, img_ref, f_ref, l_ref, ra_ref, rb_ref,
    *rest,
):
    if final:
        out_ref, fluxout_ref, canvas = rest
    else:
        fout_ref, lout_ref, up_ref, down_ref, canvas = rest
    rows_n, pad_width = canvas.shape
    strip_rows, width = img_ref.shape
    own = oy_ref.shape[0]
    top_first = band_ref[0] <= band_ref[1]

    if first:
        fluxes = [f_ref[0:1, :], f_ref[1:2, :], pa_ref[2:3, :], pb_ref[2:3, :]]
    else:
        weights = [w_ref[0:1, :], w_ref[1:2, :], pa_ref[3:4, :], pb_ref[3:4, :]]
        from_above = ra_ref[0:1, :]
        from_below = rb_ref[0:1, :]
        extra = [
            jnp.where(top_first, from_above, from_below),
            jnp.where(top_first, from_below, from_above),
            ra_ref[1:2, :],
            rb_ref[1:2, :],
        ]
        fluxes = []
        for j in range(own + 2):
            grad = l_ref[j : j + 1, :] + extra[j]
            safe = jnp.where(weights[j] == 0.0, 1.0, weights[j])
            fluxes.append(f_ref[j : j + 1, :] + 0.5 * grad / safe)

    specs = []
    for j in range(own):
        y = band_ref[j].astype(jnp.float32) + oy_ref[j : j + 1, :]
        specs.append((y, ox_ref[j : j + 1, :], own_coefs(psf_ref, cell_ref, j), col_ref[j], None))
    specs.append((
        pa_ref[0:1, :] - strip_rows, pa_ref[1:2, :], [pas_ref[4, k] for k in range(9)],
        pas_ref[4, 9].astype(jnp.int32), REACH,
    ))
    specs.append((
        pb_ref[0:1, :] + strip_rows, pb_ref[1:2, :], [pbs_ref[4, k] for k in range(9)],
        pbs_ref[4, 9].astype(jnp.int32), None,
    ))

    canvas[...] = jnp.zeros_like(canvas)
    hpos = lax.broadcasted_iota(jnp.int32, (rows_n, LANES), 0).astype(jnp.float32)
    wpos = lax.broadcasted_iota(jnp.int32, (WIN, LANES), 0).astype(jnp.float32) - LANES
    saved = []
    for j, (y, x, c, col, keep) in enumerate(specs):
        rows = profile3(hpos - y)
        if keep is not None:
            rows = tuple(jnp.where(hpos < keep, r, 0.0) for r in rows)
        cols = profile3(wpos - x)
        mixed = [
            (c[3 * a] * cols[0] + c[3 * a + 1] * cols[1] + c[3 * a + 2] * cols[2]) * fluxes[j]
            for a in range(3)
        ]
        stamp = split_dot(jnp.concatenate(rows, axis=1), jnp.concatenate(mixed, axis=1), DIMS_NT)
        start = pl.multiple_of(col * LANES, LANES)
        canvas[:, pl.ds(start, WIN)] += stamp
        saved.append((rows, cols, c, start))
    inner = slice(LANES, LANES + width)
    if final:
        out_ref[...] = img_ref[...] - canvas[:, inner]
        for j in range(own):
            fluxout_ref[j : j + 1, :] = fluxes[j]
        return
    canvas[:, inner] = img_ref[...] - canvas[:, inner]
    canvas[:, 0:LANES] = jnp.zeros((rows_n, LANES), jnp.float32)
    canvas[:, LANES + width :] = jnp.zeros((rows_n, pad_width - LANES - width), jnp.float32)
    fout_ref[...] = jnp.zeros_like(fout_ref)
    lout_ref[...] = jnp.zeros_like(lout_ref)
    partial = []
    for j, (rows, cols, c, start) in enumerate(saved):
        window = canvas[:, pl.ds(start, WIN)]
        across_all = split_dot(window, jnp.concatenate(cols, axis=1), DIMS_NN)
        grad = None
        for a in range(3):
            for b in range(3):
                paired = jnp.sum(rows[a] * across_all[:, b * LANES : (b + 1) * LANES], axis=0,
                                 keepdims=True)
                term = c[3 * a + b] * paired
                grad = term if grad is None else grad + term
        partial.append(grad)
        fout_ref[j : j + 1, :] = fluxes[j]
        lout_ref[j : j + 1, :] = grad
    top_part = jnp.where(top_first, partial[0], partial[1])
    bot_part = jnp.where(top_first, partial[1], partial[0])
    up_ref[0:1, :] = partial[own]
    up_ref[1:2, :] = top_part
    down_ref[0:1, :] = partial[own + 1]
    down_ref[1:2, :] = bot_part


def vmem_operands(*arrays):
    return [pltpu.with_memory_space_constraint(a, pltpu.VMEM) for a in arrays]


def local(image, band_row, col_block, cell_index, offset_y, offset_x, flux_start, psf_coef):
    strip_rows, strip_width = image.shape
    own = band_row.shape[0]
    f32 = jnp.float32
    smem = pl.BlockSpec(memory_space=pltpu.SMEM)
    vmem = pl.BlockSpec(memory_space=pltpu.VMEM)
    packet = jax.ShapeDtypeStruct((SLOTS, LANES), f32)
    send_up, send_down, weight = pl.pallas_call(
        setup_kernel,
        out_shape=(packet, packet, jax.ShapeDtypeStruct((own, LANES), f32)),
        in_specs=[smem] * 4 + [vmem] * 3,
        out_specs=(vmem, vmem, vmem),
    )(band_row, col_block, cell_index, psf_coef, offset_y, offset_x, flux_start)
    got_above, got_below = exchange(send_up, send_down)

    blocks = own + 2
    flops = 2 * 3 * 2 * strip_rows * WIN * 3 * LANES * blocks
    state_shape = jax.ShapeDtypeStruct((SLOTS, LANES), f32)
    part_shape = pltpu.VMEM((2, LANES), f32)
    common = (band_row, col_block, cell_index, psf_coef, got_above, got_below,
              offset_y, offset_x, weight, got_above, got_below, image)

    def phase(final, first, fluxes, partials, from_above, from_below):
        kernel = functools.partial(phase_kernel, final, first)
        if final:
            out_shape = (jax.ShapeDtypeStruct((strip_rows, strip_width), f32),
                         jax.ShapeDtypeStruct((own, LANES), f32))
            out_specs = (vmem, vmem)
        else:
            out_shape = (state_shape, state_shape, part_shape, part_shape)
            out_specs = (vmem, vmem, vmem, vmem)
        return pl.pallas_call(
            kernel,
            out_shape=out_shape,
            in_specs=[smem] * 6 + [vmem] * 10,
            out_specs=out_specs,
            scratch_shapes=[pltpu.VMEM((strip_rows, strip_width + 2 * LANES), f32)],
            cost_estimate=pl.CostEstimate(
                flops=flops, transcendentals=blocks * 2 * (strip_rows + WIN) * LANES,
                bytes_accessed=4 * strip_rows * strip_width * 2,
            ),
        )(*common, fluxes, partials, *vmem_operands(from_above, from_below))

    state, partials, up, down = phase(False, True, flux_start, flux_start, flux_start, flux_start)
    for iteration in range(1, ITERS):
        from_above, from_below = exchange(up, down)
        state, partials, up, down = phase(False, False, state, partials, from_above, from_below)
    from_above, from_below = exchange(up, down)
    residual, fluxes = phase(True, False, state, partials, from_above, from_below)
    return (fluxes, residual)


def solution(mesh):
    return jax.shard_map(
        local,
        mesh=mesh,
        in_specs=(
            P(("groups", "ty"), None),
            P(("groups", "ty")),
            P(("groups", "ty")),
            P(("groups", "ty")),
            P(("groups", "ty"), None),
            P(("groups", "ty"), None),
            P(("groups", "ty"), None),
            P(),
        ),
        out_specs=(P(("groups", "ty"), None), P(("groups", "ty"), None)),
        check_vma=False,
    )
```

```python
import functools

import jax
import jax.numpy as jnp
from jax import lax
from jax.experimental import pallas as pl
from jax.experimental.pallas import tpu as pltpu
from jax.sharding import PartitionSpec as P

REACH = 15
ITERS = 2
LANES = 128
WIN = 384
SPAN = 256
SLOTS = 8

DIMS_NT = (((1,), (1,)), ((), ()))
DIMS_NN = (((1,), (0,)), ((), ()))


def profile3(dist):
    tapered_arg = dist * (1.0 / 15.5)
    tapered = jnp.maximum(0.0, 1.0 - tapered_arg * tapered_arg)
    scaled = dist * (1.0 / 1.7)
    core_part = jnp.exp(-0.5 * scaled * scaled) * tapered
    wing_part = jnp.exp(dist * dist * (-1.0 / 72.0)) * tapered
    return core_part, scaled * core_part, wing_part


def split_dot(lhs, rhs, dims):
    lhs_hi = lhs.astype(jnp.bfloat16)
    lhs_lo = (lhs - lhs_hi.astype(jnp.float32)).astype(jnp.bfloat16)
    rhs_hi = rhs.astype(jnp.bfloat16)
    rhs_lo = (rhs - rhs_hi.astype(jnp.float32)).astype(jnp.bfloat16)

    def one(a, b):
        return lax.dot_general(a, b, dims, preferred_element_type=jnp.float32)

    return one(lhs_hi, rhs_hi) + (one(lhs_hi, rhs_lo) + one(lhs_lo, rhs_hi))


def exchange(to_above, to_below):
    count = lax.axis_size("ty")
    forward = [(i, i + 1) for i in range(count - 1)]
    backward = [(i + 1, i) for i in range(count - 1)]
    from_above = lax.ppermute(to_below, "ty", forward)
    from_below = lax.ppermute(to_above, "ty", backward)
    return from_above, from_below


def own_coefs(psf_ref, cell_ref, j):
    cell = cell_ref[j]
    return [psf_ref[k, cell] for k in range(9)]


def setup_kernel(band_ref, col_ref, cell_ref, psf_ref, oy_ref, ox_ref, f_ref, up_ref, down_ref, w_ref):
    own = oy_ref.shape[0]
    offs = lax.broadcasted_iota(jnp.int32, (32, LANES), 0).astype(jnp.float32) - 15.0
    lane = lax.broadcasted_iota(jnp.int32, (1, LANES), 1)
    ys, metas, weights = [], [], []
    for j in range(own):
        y = band_ref[j].astype(jnp.float32) + oy_ref[j : j + 1, :]
        x = ox_ref[j : j + 1, :]
        c = own_coefs(psf_ref, cell_ref, j)
        rows = profile3(jnp.floor(y) + offs - y)
        cols = profile3(jnp.floor(x) + offs - x)
        gram_r = [[jnp.sum(rows[a] * rows[b], axis=0, keepdims=True) for b in range(3)] for a in range(3)]
        gram_c = [[jnp.sum(cols[a] * cols[b], axis=0, keepdims=True) for b in range(3)] for a in range(3)]
        weight = None
        for a in range(3):
            for cc in range(3):
                inner = None
                for b in range(3):
                    for d in range(3):
                        term = (c[3 * a + b] * c[3 * cc + d]) * gram_c[b][d]
                        inner = term if inner is None else inner + term
                term = gram_r[a][cc] * inner
                weight = term if weight is None else weight + term
        w_ref[j : j + 1, :] = weight
        meta = jnp.zeros((1, LANES), jnp.float32)
        for k in range(9):
            meta = jnp.where(lane == k, c[k], meta)
        meta = jnp.where(lane == 9, col_ref[j].astype(jnp.float32), meta)
        ys.append(y)
        metas.append(meta)
        weights.append(weight)
    top_first = band_ref[0] <= band_ref[1]

    def pick(first, second):
        return jnp.where(top_first, first, second), jnp.where(top_first, second, first)

    tops, bots = zip(*[
        pick(*pair) for pair in (
            (ys[0], ys[1]), (ox_ref[0:1, :], ox_ref[1:2, :]), (f_ref[0:1, :], f_ref[1:2, :]),
            (weights[0], weights[1]), (metas[0], metas[1]),
        )
    ])
    up_ref[...] = jnp.zeros_like(up_ref)
    down_ref[...] = jnp.zeros_like(down_ref)
    for r in range(5):
        up_ref[r : r + 1, :] = tops[r]
        down_ref[r : r + 1, :] = bots[r]


def phase_kernel(
    final, first,
    band_ref, col_ref, cell_ref, psf_ref, pas_ref, pbs_ref,
    oy_ref, ox_ref, w_ref, pa_ref, pb_ref, img_ref, f_ref, l_ref, ra_ref, rb_ref,
    *rest,
):
    if final:
        out_ref, fluxout_ref, canvas = rest
    else:
        fout_ref, lout_ref, up_ref, down_ref, canvas = rest
    rows_n, pad_width = canvas.shape
    strip_rows, width = img_ref.shape
    own = oy_ref.shape[0]
    top_first = band_ref[0] <= band_ref[1]

    if first:
        fluxes = [f_ref[0:1, :], f_ref[1:2, :], pa_ref[2:3, :], pb_ref[2:3, :]]
    else:
        weights = [w_ref[0:1, :], w_ref[1:2, :], pa_ref[3:4, :], pb_ref[3:4, :]]
        from_above = ra_ref[0:1, :]
        from_below = rb_ref[0:1, :]
        extra = [
            jnp.where(top_first, from_above, from_below),
            jnp.where(top_first, from_below, from_above),
            ra_ref[1:2, :],
            rb_ref[1:2, :],
        ]
        fluxes = []
        for j in range(own + 2):
            grad = l_ref[j : j + 1, :] + extra[j]
            safe = jnp.where(weights[j] == 0.0, 1.0, weights[j])
            fluxes.append(f_ref[j : j + 1, :] + 0.5 * grad / safe)

    specs = []
    for j in range(own):
        y = band_ref[j].astype(jnp.float32) + oy_ref[j : j + 1, :]
        specs.append((y, ox_ref[j : j + 1, :], own_coefs(psf_ref, cell_ref, j), col_ref[j], None))
    specs.append((
        pa_ref[0:1, :] - strip_rows, pa_ref[1:2, :], [pas_ref[4, k] for k in range(9)],
        pas_ref[4, 9].astype(jnp.int32), REACH,
    ))
    specs.append((
        pb_ref[0:1, :] + strip_rows, pb_ref[1:2, :], [pbs_ref[4, k] for k in range(9)],
        pbs_ref[4, 9].astype(jnp.int32), None,
    ))

    canvas[...] = jnp.zeros_like(canvas)
    hpos = lax.broadcasted_iota(jnp.int32, (rows_n, LANES), 0).astype(jnp.float32)
    wpos = lax.broadcasted_iota(jnp.int32, (SPAN, LANES), 0).astype(jnp.float32) - LANES // 2
    spare = jnp.zeros((rows_n, WIN - SPAN), jnp.float32)
    saved = []
    for j, (y, x, c, col, keep) in enumerate(specs):
        rows = profile3(hpos - y)
        if keep is not None:
            rows = tuple(jnp.where(hpos < keep, r, 0.0) for r in rows)
        cols = profile3(wpos - x)
        mixed = [
            (c[3 * a] * cols[0] + c[3 * a + 1] * cols[1] + c[3 * a + 2] * cols[2]) * fluxes[j]
            for a in range(3)
        ]
        stamp = split_dot(jnp.concatenate(rows, axis=1), jnp.concatenate(mixed, axis=1), DIMS_NT)
        start = pl.multiple_of(col * LANES, LANES)
        canvas[:, pl.ds(start, WIN)] += pltpu.roll(
            jnp.concatenate([stamp, spare], axis=1), LANES // 2, 1
        )
        saved.append((rows, cols, c, start))
    inner = slice(LANES, LANES + width)
    if final:
        out_ref[...] = img_ref[...] - canvas[:, inner]
        for j in range(own):
            fluxout_ref[j : j + 1, :] = fluxes[j]
        return
    canvas[:, inner] = img_ref[...] - canvas[:, inner]
    canvas[:, 0:LANES] = jnp.zeros((rows_n, LANES), jnp.float32)
    canvas[:, LANES + width :] = jnp.zeros((rows_n, pad_width - LANES - width), jnp.float32)
    fout_ref[...] = jnp.zeros_like(fout_ref)
    lout_ref[...] = jnp.zeros_like(lout_ref)
    partial = []
    for j, (rows, cols, c, start) in enumerate(saved):
        window = pltpu.roll(canvas[:, pl.ds(start, WIN)], WIN - LANES // 2, 1)[:, :SPAN]
        across_all = split_dot(window, jnp.concatenate(cols, axis=1), DIMS_NN)
        grad = None
        for a in range(3):
            for b in range(3):
                paired = jnp.sum(rows[a] * across_all[:, b * LANES : (b + 1) * LANES], axis=0,
                                 keepdims=True)
                term = c[3 * a + b] * paired
                grad = term if grad is None else grad + term
        partial.append(grad)
        fout_ref[j : j + 1, :] = fluxes[j]
        lout_ref[j : j + 1, :] = grad
    top_part = jnp.where(top_first, partial[0], partial[1])
    bot_part = jnp.where(top_first, partial[1], partial[0])
    up_ref[0:1, :] = partial[own]
    up_ref[1:2, :] = top_part
    down_ref[0:1, :] = partial[own + 1]
    down_ref[1:2, :] = bot_part


def vmem_operands(*arrays):
    return [pltpu.with_memory_space_constraint(a, pltpu.VMEM) for a in arrays]


def local(image, band_row, col_block, cell_index, offset_y, offset_x, flux_start, psf_coef):
    strip_rows, strip_width = image.shape
    own = band_row.shape[0]
    f32 = jnp.float32
    smem = pl.BlockSpec(memory_space=pltpu.SMEM)
    vmem = pl.BlockSpec(memory_space=pltpu.VMEM)
    packet = jax.ShapeDtypeStruct((SLOTS, LANES), f32)
    send_up, send_down, weight = pl.pallas_call(
        setup_kernel,
        out_shape=(packet, packet, jax.ShapeDtypeStruct((own, LANES), f32)),
        in_specs=[smem] * 4 + [vmem] * 3,
        out_specs=(vmem, vmem, vmem),
    )(band_row, col_block, cell_index, psf_coef, offset_y, offset_x, flux_start)
    got_above, got_below = exchange(send_up, send_down)

    blocks = own + 2
    flops = 2 * 3 * 2 * strip_rows * WIN * 3 * LANES * blocks
    state_shape = jax.ShapeDtypeStruct((SLOTS, LANES), f32)
    part_shape = pltpu.VMEM((2, LANES), f32)
    common = (band_row, col_block, cell_index, psf_coef, got_above, got_below,
              offset_y, offset_x, weight, got_above, got_below, image)

    def phase(final, first, fluxes, partials, from_above, from_below):
        kernel = functools.partial(phase_kernel, final, first)
        if final:
            out_shape = (jax.ShapeDtypeStruct((strip_rows, strip_width), f32),
                         jax.ShapeDtypeStruct((own, LANES), f32))
            out_specs = (vmem, vmem)
        else:
            out_shape = (state_shape, state_shape, part_shape, part_shape)
            out_specs = (vmem, vmem, vmem, vmem)
        return pl.pallas_call(
            kernel,
            out_shape=out_shape,
            in_specs=[smem] * 6 + [vmem] * 10,
            out_specs=out_specs,
            scratch_shapes=[pltpu.VMEM((strip_rows, strip_width + 2 * LANES), f32)],
            cost_estimate=pl.CostEstimate(
                flops=flops, transcendentals=blocks * 2 * (strip_rows + WIN) * LANES,
                bytes_accessed=4 * strip_rows * strip_width * 2,
            ),
        )(*common, fluxes, partials, *vmem_operands(from_above, from_below))

    state, partials, up, down = phase(False, True, flux_start, flux_start, flux_start, flux_start)
    for iteration in range(1, ITERS):
        from_above, from_below = exchange(up, down)
        state, partials, up, down = phase(False, False, state, partials, from_above, from_below)
    from_above, from_below = exchange(up, down)
    residual, fluxes = phase(True, False, state, partials, from_above, from_below)
    return (fluxes, residual)


def solution(mesh):
    return jax.shard_map(
        local,
        mesh=mesh,
        in_specs=(
            P(("groups", "ty"), None),
            P(("groups", "ty")),
            P(("groups", "ty")),
            P(("groups", "ty")),
            P(("groups", "ty"), None),
            P(("groups", "ty"), None),
            P(("groups", "ty"), None),
            P(),
        ),
        out_specs=(P(("groups", "ty"), None), P(("groups", "ty"), None)),
        check_vma=False,
    )
```

```python
import functools

import jax
import jax.numpy as jnp
from jax import lax
from jax.experimental import pallas as pl
from jax.experimental.pallas import tpu as pltpu
from jax.sharding import PartitionSpec as P

REACH = 15
ITERS = 2
LANES = 128
WIN = 384
SPAN = 256
SLOTS = 8

DIMS_NT = (((1,), (1,)), ((), ()))
DIMS_NN = (((1,), (0,)), ((), ()))


def profile3(dist):
    tapered_arg = dist * (1.0 / 15.5)
    tapered = jnp.maximum(0.0, 1.0 - tapered_arg * tapered_arg)
    scaled = dist * (1.0 / 1.7)
    core_part = jnp.exp(-0.5 * scaled * scaled) * tapered
    wing_part = jnp.exp(dist * dist * (-1.0 / 72.0)) * tapered
    return core_part, scaled * core_part, wing_part


def split_dot(lhs, rhs, dims):
    lhs_hi = lhs.astype(jnp.bfloat16)
    lhs_lo = (lhs - lhs_hi.astype(jnp.float32)).astype(jnp.bfloat16)
    rhs_hi = rhs.astype(jnp.bfloat16)
    rhs_lo = (rhs - rhs_hi.astype(jnp.float32)).astype(jnp.bfloat16)

    def one(a, b):
        return lax.dot_general(a, b, dims, preferred_element_type=jnp.float32)

    return one(lhs_hi, rhs_hi) + (one(lhs_hi, rhs_lo) + one(lhs_lo, rhs_hi))


def split_bf16(value):
    hi = value.astype(jnp.bfloat16)
    return hi, (value - hi.astype(jnp.float32)).astype(jnp.bfloat16)


def presplit_dot(lhs, rhs_hi, rhs_lo, dims):
    lhs_hi, lhs_lo = split_bf16(lhs)

    def one(a, b):
        return lax.dot_general(a, b, dims, preferred_element_type=jnp.float32)

    return one(lhs_hi, rhs_hi) + (one(lhs_hi, rhs_lo) + one(lhs_lo, rhs_hi))


def exchange(to_above, to_below):
    count = lax.axis_size("ty")
    forward = [(i, i + 1) for i in range(count - 1)]
    backward = [(i + 1, i) for i in range(count - 1)]
    from_above = lax.ppermute(to_below, "ty", forward)
    from_below = lax.ppermute(to_above, "ty", backward)
    return from_above, from_below


def own_coefs(psf_ref, cell_ref, j):
    cell = cell_ref[j]
    return [psf_ref[k, cell] for k in range(9)]


def setup_kernel(band_ref, col_ref, cell_ref, psf_ref, oy_ref, ox_ref, f_ref, up_ref, down_ref, w_ref):
    own = oy_ref.shape[0]
    offs = lax.broadcasted_iota(jnp.int32, (32, LANES), 0).astype(jnp.float32) - 15.0
    lane = lax.broadcasted_iota(jnp.int32, (1, LANES), 1)
    ys, metas, weights = [], [], []
    for j in range(own):
        y = band_ref[j].astype(jnp.float32) + oy_ref[j : j + 1, :]
        x = ox_ref[j : j + 1, :]
        c = own_coefs(psf_ref, cell_ref, j)
        rows = profile3(jnp.floor(y) + offs - y)
        cols = profile3(jnp.floor(x) + offs - x)
        gram_r = [[jnp.sum(rows[a] * rows[b], axis=0, keepdims=True) for b in range(3)] for a in range(3)]
        gram_c = [[jnp.sum(cols[a] * cols[b], axis=0, keepdims=True) for b in range(3)] for a in range(3)]
        weight = None
        for a in range(3):
            for cc in range(3):
                inner = None
                for b in range(3):
                    for d in range(3):
                        term = (c[3 * a + b] * c[3 * cc + d]) * gram_c[b][d]
                        inner = term if inner is None else inner + term
                term = gram_r[a][cc] * inner
                weight = term if weight is None else weight + term
        w_ref[j : j + 1, :] = weight
        meta = jnp.zeros((1, LANES), jnp.float32)
        for k in range(9):
            meta = jnp.where(lane == k, c[k], meta)
        meta = jnp.where(lane == 9, col_ref[j].astype(jnp.float32), meta)
        ys.append(y)
        metas.append(meta)
        weights.append(weight)
    top_first = band_ref[0] <= band_ref[1]

    def pick(first, second):
        return jnp.where(top_first, first, second), jnp.where(top_first, second, first)

    tops, bots = zip(*[
        pick(*pair) for pair in (
            (ys[0], ys[1]), (ox_ref[0:1, :], ox_ref[1:2, :]), (f_ref[0:1, :], f_ref[1:2, :]),
            (weights[0], weights[1]), (metas[0], metas[1]),
        )
    ])
    up_ref[...] = jnp.zeros_like(up_ref)
    down_ref[...] = jnp.zeros_like(down_ref)
    for r in range(5):
        up_ref[r : r + 1, :] = tops[r]
        down_ref[r : r + 1, :] = bots[r]


def phase_kernel(
    final, first,
    band_ref, col_ref, cell_ref, psf_ref, pas_ref, pbs_ref,
    oy_ref, ox_ref, w_ref, pa_ref, pb_ref, img_ref, f_ref, l_ref, ra_ref, rb_ref,
    *rest,
):
    rest = list(rest)
    if not first:
        pre_refs, rest = rest[:5], rest[5:]
    if final:
        (out_ref, fluxout_ref), rest = rest[:2], rest[2:]
    else:
        (fout_ref, lout_ref, up_ref, down_ref), rest = rest[:4], rest[4:]
    if first:
        pre_refs, rest = rest[:5], rest[5:]
    (canvas,) = rest
    rows_n, pad_width = canvas.shape
    strip_rows, width = img_ref.shape
    own = oy_ref.shape[0]
    top_first = band_ref[0] <= band_ref[1]

    if first:
        fluxes = [f_ref[0:1, :], f_ref[1:2, :], pa_ref[2:3, :], pb_ref[2:3, :]]
    else:
        weights = [w_ref[0:1, :], w_ref[1:2, :], pa_ref[3:4, :], pb_ref[3:4, :]]
        from_above = ra_ref[0:1, :]
        from_below = rb_ref[0:1, :]
        extra = [
            jnp.where(top_first, from_above, from_below),
            jnp.where(top_first, from_below, from_above),
            ra_ref[1:2, :],
            rb_ref[1:2, :],
        ]
        fluxes = []
        for j in range(own + 2):
            grad = l_ref[j : j + 1, :] + extra[j]
            safe = jnp.where(weights[j] == 0.0, 1.0, weights[j])
            fluxes.append(f_ref[j : j + 1, :] + 0.5 * grad / safe)

    specs = []
    for j in range(own):
        y = band_ref[j].astype(jnp.float32) + oy_ref[j : j + 1, :]
        specs.append((y, ox_ref[j : j + 1, :], own_coefs(psf_ref, cell_ref, j), col_ref[j], None))
    specs.append((
        pa_ref[0:1, :] - strip_rows, pa_ref[1:2, :], [pas_ref[4, k] for k in range(9)],
        pas_ref[4, 9].astype(jnp.int32), REACH,
    ))
    specs.append((
        pb_ref[0:1, :] + strip_rows, pb_ref[1:2, :], [pbs_ref[4, k] for k in range(9)],
        pbs_ref[4, 9].astype(jnp.int32), None,
    ))

    canvas[...] = jnp.zeros_like(canvas)
    hpos = lax.broadcasted_iota(jnp.int32, (rows_n, LANES), 0).astype(jnp.float32)
    wpos = lax.broadcasted_iota(jnp.int32, (SPAN, LANES), 0).astype(jnp.float32) - LANES // 2
    spare = jnp.zeros((rows_n, WIN - SPAN), jnp.float32)
    saved = []
    for j, (y, x, c, col, keep) in enumerate(specs):
        if first:
            rows = profile3(hpos - y)
            if keep is not None:
                rows = tuple(jnp.where(hpos < keep, r, 0.0) for r in rows)
            cols = profile3(wpos - x)
            mixed = [c[3 * a] * cols[0] + c[3 * a + 1] * cols[1] + c[3 * a + 2] * cols[2]
                     for a in range(3)]
            rows_all = jnp.concatenate(rows, axis=1)
            mixed_hi, mixed_lo = split_bf16(jnp.concatenate(mixed, axis=1))
            cols_hi, cols_lo = split_bf16(jnp.concatenate(cols, axis=1))
            for ref, value in zip(pre_refs, (rows_all, mixed_hi, mixed_lo, cols_hi, cols_lo)):
                ref[j] = value
        else:
            rows_all = pre_refs[0][j]
            mixed_hi, mixed_lo = pre_refs[1][j], pre_refs[2][j]
            cols_hi, cols_lo = pre_refs[3][j], pre_refs[4][j]
        flux = fluxes[j]
        scaled = rows_all * jnp.concatenate([flux, flux, flux], axis=1)
        stamp = presplit_dot(scaled, mixed_hi, mixed_lo, DIMS_NT)
        start = pl.multiple_of(col * LANES, LANES)
        canvas[:, pl.ds(start, WIN)] += pltpu.roll(
            jnp.concatenate([stamp, spare], axis=1), LANES // 2, 1
        )
        saved.append((rows_all, cols_hi, cols_lo, c, start))
    inner = slice(LANES, LANES + width)
    if final:
        out_ref[...] = img_ref[...] - canvas[:, inner]
        for j in range(own):
            fluxout_ref[j : j + 1, :] = fluxes[j]
        return
    canvas[:, inner] = img_ref[...] - canvas[:, inner]
    canvas[:, 0:LANES] = jnp.zeros((rows_n, LANES), jnp.float32)
    canvas[:, LANES + width :] = jnp.zeros((rows_n, pad_width - LANES - width), jnp.float32)
    fout_ref[...] = jnp.zeros_like(fout_ref)
    lout_ref[...] = jnp.zeros_like(lout_ref)
    partial = []
    for j, (rows_all, cols_hi, cols_lo, c, start) in enumerate(saved):
        window = pltpu.roll(canvas[:, pl.ds(start, WIN)], WIN - LANES // 2, 1)[:, :SPAN]
        across_all = presplit_dot(window, cols_hi, cols_lo, DIMS_NN)
        grad = None
        for a in range(3):
            for b in range(3):
                paired = jnp.sum(
                    rows_all[:, a * LANES : (a + 1) * LANES]
                    * across_all[:, b * LANES : (b + 1) * LANES], axis=0, keepdims=True)
                term = c[3 * a + b] * paired
                grad = term if grad is None else grad + term
        partial.append(grad)
        fout_ref[j : j + 1, :] = fluxes[j]
        lout_ref[j : j + 1, :] = grad
    top_part = jnp.where(top_first, partial[0], partial[1])
    bot_part = jnp.where(top_first, partial[1], partial[0])
    up_ref[0:1, :] = partial[own]
    up_ref[1:2, :] = top_part
    down_ref[0:1, :] = partial[own + 1]
    down_ref[1:2, :] = bot_part


def vmem_operands(*arrays):
    return [pltpu.with_memory_space_constraint(a, pltpu.VMEM) for a in arrays]


def local(image, band_row, col_block, cell_index, offset_y, offset_x, flux_start, psf_coef):
    strip_rows, strip_width = image.shape
    own = band_row.shape[0]
    f32 = jnp.float32
    smem = pl.BlockSpec(memory_space=pltpu.SMEM)
    vmem = pl.BlockSpec(memory_space=pltpu.VMEM)
    packet = jax.ShapeDtypeStruct((SLOTS, LANES), f32)
    send_up, send_down, weight = pl.pallas_call(
        setup_kernel,
        out_shape=(packet, packet, jax.ShapeDtypeStruct((own, LANES), f32)),
        in_specs=[smem] * 4 + [vmem] * 3,
        out_specs=(vmem, vmem, vmem),
    )(band_row, col_block, cell_index, psf_coef, offset_y, offset_x, flux_start)
    got_above, got_below = exchange(send_up, send_down)

    blocks = own + 2
    flops = 2 * 3 * 2 * strip_rows * WIN * 3 * LANES * blocks
    state_shape = jax.ShapeDtypeStruct((SLOTS, LANES), f32)
    part_shape = pltpu.VMEM((2, LANES), f32)
    common = (band_row, col_block, cell_index, psf_coef, got_above, got_below,
              offset_y, offset_x, weight, got_above, got_below, image)

    pre_shapes = [pltpu.VMEM((blocks, strip_rows, 3 * LANES), f32)] + [
        pltpu.VMEM((blocks, SPAN, 3 * LANES), jnp.bfloat16)] * 4

    def phase(final, first, fluxes, partials, from_above, from_below, pre=()):
        kernel = functools.partial(phase_kernel, final, first)
        if final:
            out_shape = [jax.ShapeDtypeStruct((strip_rows, strip_width), f32),
                         jax.ShapeDtypeStruct((own, LANES), f32)]
        else:
            out_shape = [state_shape, state_shape, part_shape, part_shape]
        if first:
            out_shape = out_shape + pre_shapes
        return pl.pallas_call(
            kernel,
            out_shape=tuple(out_shape),
            in_specs=[smem] * 6 + [vmem] * (10 + len(pre)),
            out_specs=tuple([vmem] * len(out_shape)),
            scratch_shapes=[pltpu.VMEM((strip_rows, strip_width + 2 * LANES), f32)],
            cost_estimate=pl.CostEstimate(
                flops=flops, transcendentals=blocks * 2 * (strip_rows + WIN) * LANES,
                bytes_accessed=4 * strip_rows * strip_width * 2,
            ),
        )(*common, fluxes, partials, *vmem_operands(from_above, from_below, *pre))

    state, partials, up, down, *pre = phase(
        False, True, flux_start, flux_start, flux_start, flux_start
    )
    for iteration in range(1, ITERS):
        from_above, from_below = exchange(up, down)
        state, partials, up, down = phase(
            False, False, state, partials, from_above, from_below, pre
        )
    from_above, from_below = exchange(up, down)
    residual, fluxes = phase(True, False, state, partials, from_above, from_below, pre)
    return (fluxes, residual)


def solution(mesh):
    return jax.shard_map(
        local,
        mesh=mesh,
        in_specs=(
            P(("groups", "ty"), None),
            P(("groups", "ty")),
            P(("groups", "ty")),
            P(("groups", "ty")),
            P(("groups", "ty"), None),
            P(("groups", "ty"), None),
            P(("groups", "ty"), None),
            P(),
        ),
        out_specs=(P(("groups", "ty"), None), P(("groups", "ty"), None)),
        check_vma=False,
    )
```

```python
import functools

import jax
import jax.numpy as jnp
from jax import lax
from jax.experimental import pallas as pl
from jax.experimental.pallas import tpu as pltpu
from jax.sharding import PartitionSpec as P

REACH = 15
ITERS = 2
LANES = 128
WIN = 384
SPAN = 256
SLOTS = 8

DIMS_NT = (((1,), (1,)), ((), ()))
DIMS_NN = (((1,), (0,)), ((), ()))


def profile3(dist):
    tapered_arg = dist * (1.0 / 15.5)
    tapered = jnp.maximum(0.0, 1.0 - tapered_arg * tapered_arg)
    scaled = dist * (1.0 / 1.7)
    core_part = jnp.exp(-0.5 * scaled * scaled) * tapered
    wing_part = jnp.exp(dist * dist * (-1.0 / 72.0)) * tapered
    return core_part, scaled * core_part, wing_part


def split_dot(lhs, rhs, dims):
    lhs_hi = lhs.astype(jnp.bfloat16)
    lhs_lo = (lhs - lhs_hi.astype(jnp.float32)).astype(jnp.bfloat16)
    rhs_hi = rhs.astype(jnp.bfloat16)
    rhs_lo = (rhs - rhs_hi.astype(jnp.float32)).astype(jnp.bfloat16)

    def one(a, b):
        return lax.dot_general(a, b, dims, preferred_element_type=jnp.float32)

    return one(lhs_hi, rhs_hi) + (one(lhs_hi, rhs_lo) + one(lhs_lo, rhs_hi))


def exchange(first, second):
    count = lax.axis_size("ty")
    within = [(i, i ^ 1) for i in range(count) if (i ^ 1) < count]
    across = [(i, i + 1) for i in range(1, count - 1, 2)] + [
        (i + 1, i) for i in range(1, count - 1, 2)
    ]
    return lax.ppermute(first, "ty", within), lax.ppermute(second, "ty", across)


def even_device():
    return lax.axis_index("ty") % 2 == 0


def own_coefs(psf_ref, cell_ref, j):
    cell = cell_ref[j]
    return [psf_ref[k, cell] for k in range(9)]


def setup_kernel(band_ref, col_ref, cell_ref, psf_ref, oy_ref, ox_ref, f_ref, up_ref, down_ref, w_ref):
    own = oy_ref.shape[0]
    offs = lax.broadcasted_iota(jnp.int32, (32, LANES), 0).astype(jnp.float32) - 15.0
    lane = lax.broadcasted_iota(jnp.int32, (1, LANES), 1)
    ys, metas, weights = [], [], []
    for j in range(own):
        y = band_ref[j].astype(jnp.float32) + oy_ref[j : j + 1, :]
        x = ox_ref[j : j + 1, :]
        c = own_coefs(psf_ref, cell_ref, j)
        rows = profile3(jnp.floor(y) + offs - y)
        cols = profile3(jnp.floor(x) + offs - x)
        gram_r = [[jnp.sum(rows[a] * rows[b], axis=0, keepdims=True) for b in range(3)] for a in range(3)]
        gram_c = [[jnp.sum(cols[a] * cols[b], axis=0, keepdims=True) for b in range(3)] for a in range(3)]
        weight = None
        for a in range(3):
            for cc in range(3):
                inner = None
                for b in range(3):
                    for d in range(3):
                        term = (c[3 * a + b] * c[3 * cc + d]) * gram_c[b][d]
                        inner = term if inner is None else inner + term
                term = gram_r[a][cc] * inner
                weight = term if weight is None else weight + term
        w_ref[j : j + 1, :] = weight
        meta = jnp.zeros((1, LANES), jnp.float32)
        for k in range(9):
            meta = jnp.where(lane == k, c[k], meta)
        meta = jnp.where(lane == 9, col_ref[j].astype(jnp.float32), meta)
        ys.append(y)
        metas.append(meta)
        weights.append(weight)
    top_first = band_ref[0] <= band_ref[1]

    def pick(first, second):
        return jnp.where(top_first, first, second), jnp.where(top_first, second, first)

    tops, bots = zip(*[
        pick(*pair) for pair in (
            (ys[0], ys[1]), (ox_ref[0:1, :], ox_ref[1:2, :]), (f_ref[0:1, :], f_ref[1:2, :]),
            (weights[0], weights[1]), (metas[0], metas[1]),
        )
    ])
    even = even_device()
    first_ref, second_ref = up_ref, down_ref
    first_ref[...] = jnp.zeros_like(first_ref)
    second_ref[...] = jnp.zeros_like(second_ref)
    for r in range(5):
        first_ref[r : r + 1, :] = jnp.where(even, bots[r], tops[r])
        second_ref[r : r + 1, :] = jnp.where(even, tops[r], bots[r])


def phase_kernel(
    final, first,
    band_ref, col_ref, cell_ref, psf_ref, xs1_ref, xs2_ref,
    oy_ref, ox_ref, w_ref, x1_ref, x2_ref, img_ref, f_ref, l_ref, q1_ref, q2_ref,
    *rest,
):
    even = even_device()

    def above(ref1, ref2, row):
        return jnp.where(even, ref2[row : row + 1, :], ref1[row : row + 1, :])

    def below(ref1, ref2, row):
        return jnp.where(even, ref1[row : row + 1, :], ref2[row : row + 1, :])

    if final:
        out_ref, fluxout_ref, canvas = rest
    else:
        fout_ref, lout_ref, up_ref, down_ref, canvas = rest
    rows_n, pad_width = canvas.shape
    strip_rows, width = img_ref.shape
    own = oy_ref.shape[0]
    top_first = band_ref[0] <= band_ref[1]

    if first:
        fluxes = [f_ref[0:1, :], f_ref[1:2, :], above(x1_ref, x2_ref, 2), below(x1_ref, x2_ref, 2)]
    else:
        weights = [w_ref[0:1, :], w_ref[1:2, :], above(x1_ref, x2_ref, 3), below(x1_ref, x2_ref, 3)]
        from_above = above(q1_ref, q2_ref, 0)
        from_below = below(q1_ref, q2_ref, 0)
        extra = [
            jnp.where(top_first, from_above, from_below),
            jnp.where(top_first, from_below, from_above),
            above(q1_ref, q2_ref, 1),
            below(q1_ref, q2_ref, 1),
        ]
        fluxes = []
        for j in range(own + 2):
            grad = l_ref[j : j + 1, :] + extra[j]
            safe = jnp.where(weights[j] == 0.0, 1.0, weights[j])
            fluxes.append(f_ref[j : j + 1, :] + 0.5 * grad / safe)

    specs = []
    for j in range(own):
        y = band_ref[j].astype(jnp.float32) + oy_ref[j : j + 1, :]
        specs.append((y, ox_ref[j : j + 1, :], own_coefs(psf_ref, cell_ref, j), col_ref[j], None))
    specs.append((
        above(x1_ref, x2_ref, 0) - strip_rows, above(x1_ref, x2_ref, 1),
        [jnp.where(even, xs2_ref[4, k], xs1_ref[4, k]) for k in range(9)],
        jnp.where(even, xs2_ref[4, 9], xs1_ref[4, 9]).astype(jnp.int32), REACH,
    ))
    specs.append((
        below(x1_ref, x2_ref, 0) + strip_rows, below(x1_ref, x2_ref, 1),
        [jnp.where(even, xs1_ref[4, k], xs2_ref[4, k]) for k in range(9)],
        jnp.where(even, xs1_ref[4, 9], xs2_ref[4, 9]).astype(jnp.int32), None,
    ))

    canvas[...] = jnp.zeros_like(canvas)
    hpos = lax.broadcasted_iota(jnp.int32, (rows_n, LANES), 0).astype(jnp.float32)
    wpos = lax.broadcasted_iota(jnp.int32, (SPAN, LANES), 0).astype(jnp.float32) - LANES // 2
    spare = jnp.zeros((rows_n, WIN - SPAN), jnp.float32)
    saved = []
    for j, (y, x, c, col, keep) in enumerate(specs):
        rows = profile3(hpos - y)
        if keep is not None:
            rows = tuple(jnp.where(hpos < keep, r, 0.0) for r in rows)
        cols = profile3(wpos - x)
        mixed = [
            (c[3 * a] * cols[0] + c[3 * a + 1] * cols[1] + c[3 * a + 2] * cols[2]) * fluxes[j]
            for a in range(3)
        ]
        stamp = split_dot(jnp.concatenate(rows, axis=1), jnp.concatenate(mixed, axis=1), DIMS_NT)
        start = pl.multiple_of(col * LANES, LANES)
        canvas[:, pl.ds(start, WIN)] += pltpu.roll(
            jnp.concatenate([stamp, spare], axis=1), LANES // 2, 1
        )
        saved.append((rows, cols, c, start))
    inner = slice(LANES, LANES + width)
    if final:
        out_ref[...] = img_ref[...] - canvas[:, inner]
        for j in range(own):
            fluxout_ref[j : j + 1, :] = fluxes[j]
        return
    canvas[:, inner] = img_ref[...] - canvas[:, inner]
    canvas[:, 0:LANES] = jnp.zeros((rows_n, LANES), jnp.float32)
    canvas[:, LANES + width :] = jnp.zeros((rows_n, pad_width - LANES - width), jnp.float32)
    fout_ref[...] = jnp.zeros_like(fout_ref)
    lout_ref[...] = jnp.zeros_like(lout_ref)
    partial = []
    for j, (rows, cols, c, start) in enumerate(saved):
        window = pltpu.roll(canvas[:, pl.ds(start, WIN)], WIN - LANES // 2, 1)[:, :SPAN]
        across_all = split_dot(window, jnp.concatenate(cols, axis=1), DIMS_NN)
        grad = None
        for a in range(3):
            for b in range(3):
                paired = jnp.sum(rows[a] * across_all[:, b * LANES : (b + 1) * LANES], axis=0,
                                 keepdims=True)
                term = c[3 * a + b] * paired
                grad = term if grad is None else grad + term
        partial.append(grad)
        fout_ref[j : j + 1, :] = fluxes[j]
        lout_ref[j : j + 1, :] = grad
    top_part = jnp.where(top_first, partial[0], partial[1])
    bot_part = jnp.where(top_first, partial[1], partial[0])
    first_ref, second_ref = up_ref, down_ref
    first_ref[0:1, :] = jnp.where(even, partial[own + 1], partial[own])
    first_ref[1:2, :] = jnp.where(even, bot_part, top_part)
    second_ref[0:1, :] = jnp.where(even, partial[own], partial[own + 1])
    second_ref[1:2, :] = jnp.where(even, top_part, bot_part)


def vmem_operands(*arrays):
    return [pltpu.with_memory_space_constraint(a, pltpu.VMEM) for a in arrays]


def local(image, band_row, col_block, cell_index, offset_y, offset_x, flux_start, psf_coef):
    strip_rows, strip_width = image.shape
    own = band_row.shape[0]
    f32 = jnp.float32
    smem = pl.BlockSpec(memory_space=pltpu.SMEM)
    vmem = pl.BlockSpec(memory_space=pltpu.VMEM)
    packet = jax.ShapeDtypeStruct((SLOTS, LANES), f32)
    send_within, send_across, weight = pl.pallas_call(
        setup_kernel,
        out_shape=(packet, packet, jax.ShapeDtypeStruct((own, LANES), f32)),
        in_specs=[smem] * 4 + [vmem] * 3,
        out_specs=(vmem, vmem, vmem),
    )(band_row, col_block, cell_index, psf_coef, offset_y, offset_x, flux_start)
    got_within, got_across = exchange(send_within, send_across)

    blocks = own + 2
    flops = 2 * 3 * 2 * strip_rows * WIN * 3 * LANES * blocks
    state_shape = jax.ShapeDtypeStruct((SLOTS, LANES), f32)
    part_shape = pltpu.VMEM((2, LANES), f32)
    common = (band_row, col_block, cell_index, psf_coef, got_within, got_across,
              offset_y, offset_x, weight, got_within, got_across, image)

    def phase(final, first, fluxes, partials, swap_within, swap_across):
        kernel = functools.partial(phase_kernel, final, first)
        if final:
            out_shape = (jax.ShapeDtypeStruct((strip_rows, strip_width), f32),
                         jax.ShapeDtypeStruct((own, LANES), f32))
            out_specs = (vmem, vmem)
        else:
            out_shape = (state_shape, state_shape, part_shape, part_shape)
            out_specs = (vmem, vmem, vmem, vmem)
        return pl.pallas_call(
            kernel,
            out_shape=out_shape,
            in_specs=[smem] * 6 + [vmem] * 10,
            out_specs=out_specs,
            scratch_shapes=[pltpu.VMEM((strip_rows, strip_width + 2 * LANES), f32)],
            cost_estimate=pl.CostEstimate(
                flops=flops, transcendentals=blocks * 2 * (strip_rows + WIN) * LANES,
                bytes_accessed=4 * strip_rows * strip_width * 2,
            ),
        )(*common, fluxes, partials, *vmem_operands(swap_within, swap_across))

    state, partials, within, across = phase(False, True, flux_start, flux_start, flux_start, flux_start)
    for iteration in range(1, ITERS):
        swap_within, swap_across = exchange(within, across)
        state, partials, within, across = phase(False, False, state, partials, swap_within, swap_across)
    swap_within, swap_across = exchange(within, across)
    residual, fluxes = phase(True, False, state, partials, swap_within, swap_across)
    return (fluxes, residual)


def solution(mesh):
    return jax.shard_map(
        local,
        mesh=mesh,
        in_specs=(
            P(("groups", "ty"), None),
            P(("groups", "ty")),
            P(("groups", "ty")),
            P(("groups", "ty")),
            P(("groups", "ty"), None),
            P(("groups", "ty"), None),
            P(("groups", "ty"), None),
            P(),
        ),
        out_specs=(P(("groups", "ty"), None), P(("groups", "ty"), None)),
        check_vma=False,
    )
```

```python
import functools

import jax
import jax.numpy as jnp
from jax import lax
from jax.experimental import pallas as pl
from jax.experimental.pallas import tpu as pltpu
from jax.sharding import PartitionSpec as P

REACH = 15
ITERS = 2
LANES = 128
WIN = 384
SPAN = 256
SLOTS = 8

DIMS_NT = (((1,), (1,)), ((), ()))
DIMS_NN = (((1,), (0,)), ((), ()))


def profile3(dist):
    tapered_arg = dist * (1.0 / 15.5)
    tapered = jnp.maximum(0.0, 1.0 - tapered_arg * tapered_arg)
    scaled = dist * (1.0 / 1.7)
    core_part = jnp.exp(-0.5 * scaled * scaled) * tapered
    wing_part = jnp.exp(dist * dist * (-1.0 / 72.0)) * tapered
    return core_part, scaled * core_part, wing_part


def split_dot(lhs, rhs, dims):
    lhs_hi = lhs.astype(jnp.bfloat16)
    lhs_lo = (lhs - lhs_hi.astype(jnp.float32)).astype(jnp.bfloat16)
    rhs_hi = rhs.astype(jnp.bfloat16)
    rhs_lo = (rhs - rhs_hi.astype(jnp.float32)).astype(jnp.bfloat16)

    def one(a, b):
        return lax.dot_general(a, b, dims, preferred_element_type=jnp.float32)

    return one(lhs_hi, rhs_hi) + (one(lhs_hi, rhs_lo) + one(lhs_lo, rhs_hi))


def split_bf16(value):
    hi = value.astype(jnp.bfloat16)
    return hi, (value - hi.astype(jnp.float32)).astype(jnp.bfloat16)


def presplit_dot(lhs, rhs_hi, rhs_lo, dims):
    lhs_hi, lhs_lo = split_bf16(lhs)

    def one(a, b):
        return lax.dot_general(a, b, dims, preferred_element_type=jnp.float32)

    return one(lhs_hi, rhs_hi) + (one(lhs_hi, rhs_lo) + one(lhs_lo, rhs_hi))


def exchange(first, second):
    count = lax.axis_size("ty")
    within = [(i, i ^ 1) for i in range(count) if (i ^ 1) < count]
    across = [(i, i + 1) for i in range(1, count - 1, 2)] + [
        (i + 1, i) for i in range(1, count - 1, 2)
    ]
    return lax.ppermute(first, "ty", within), lax.ppermute(second, "ty", across)


def even_device():
    return lax.axis_index("ty") % 2 == 0


def own_coefs(psf_ref, cell_ref, j):
    cell = cell_ref[j]
    return [psf_ref[k, cell] for k in range(9)]


def setup_kernel(band_ref, col_ref, cell_ref, psf_ref, oy_ref, ox_ref, f_ref, up_ref, down_ref, w_ref):
    own = oy_ref.shape[0]
    offs = lax.broadcasted_iota(jnp.int32, (32, LANES), 0).astype(jnp.float32) - 15.0
    lane = lax.broadcasted_iota(jnp.int32, (1, LANES), 1)
    ys, metas, weights = [], [], []
    for j in range(own):
        y = band_ref[j].astype(jnp.float32) + oy_ref[j : j + 1, :]
        x = ox_ref[j : j + 1, :]
        c = own_coefs(psf_ref, cell_ref, j)
        rows = profile3(jnp.floor(y) + offs - y)
        cols = profile3(jnp.floor(x) + offs - x)
        gram_r = [[jnp.sum(rows[a] * rows[b], axis=0, keepdims=True) for b in range(3)] for a in range(3)]
        gram_c = [[jnp.sum(cols[a] * cols[b], axis=0, keepdims=True) for b in range(3)] for a in range(3)]
        weight = None
        for a in range(3):
            for cc in range(3):
                inner = None
                for b in range(3):
                    for d in range(3):
                        term = (c[3 * a + b] * c[3 * cc + d]) * gram_c[b][d]
                        inner = term if inner is None else inner + term
                term = gram_r[a][cc] * inner
                weight = term if weight is None else weight + term
        w_ref[j : j + 1, :] = weight
        meta = jnp.zeros((1, LANES), jnp.float32)
        for k in range(9):
            meta = jnp.where(lane == k, c[k], meta)
        meta = jnp.where(lane == 9, col_ref[j].astype(jnp.float32), meta)
        ys.append(y)
        metas.append(meta)
        weights.append(weight)
    top_first = band_ref[0] <= band_ref[1]

    def pick(first, second):
        return jnp.where(top_first, first, second), jnp.where(top_first, second, first)

    tops, bots = zip(*[
        pick(*pair) for pair in (
            (ys[0], ys[1]), (ox_ref[0:1, :], ox_ref[1:2, :]), (f_ref[0:1, :], f_ref[1:2, :]),
            (weights[0], weights[1]), (metas[0], metas[1]),
        )
    ])
    even = even_device()
    first_ref, second_ref = up_ref, down_ref
    first_ref[...] = jnp.zeros_like(first_ref)
    second_ref[...] = jnp.zeros_like(second_ref)
    for r in range(5):
        first_ref[r : r + 1, :] = jnp.where(even, bots[r], tops[r])
        second_ref[r : r + 1, :] = jnp.where(even, tops[r], bots[r])


def phase_kernel(
    final, first,
    band_ref, col_ref, cell_ref, psf_ref, xs1_ref, xs2_ref,
    oy_ref, ox_ref, w_ref, x1_ref, x2_ref, img_ref, f_ref, l_ref, q1_ref, q2_ref,
    *rest,
):
    even = even_device()

    def above(ref1, ref2, row):
        return jnp.where(even, ref2[row : row + 1, :], ref1[row : row + 1, :])

    def below(ref1, ref2, row):
        return jnp.where(even, ref1[row : row + 1, :], ref2[row : row + 1, :])

    if final:
        out_ref, fluxout_ref, canvas = rest
    else:
        fout_ref, lout_ref, up_ref, down_ref, canvas = rest
    rows_n, pad_width = canvas.shape
    strip_rows, width = img_ref.shape
    own = oy_ref.shape[0]
    top_first = band_ref[0] <= band_ref[1]

    if first:
        fluxes = [f_ref[0:1, :], f_ref[1:2, :], above(x1_ref, x2_ref, 2), below(x1_ref, x2_ref, 2)]
    else:
        weights = [w_ref[0:1, :], w_ref[1:2, :], above(x1_ref, x2_ref, 3), below(x1_ref, x2_ref, 3)]
        from_above = above(q1_ref, q2_ref, 0)
        from_below = below(q1_ref, q2_ref, 0)
        extra = [
            jnp.where(top_first, from_above, from_below),
            jnp.where(top_first, from_below, from_above),
            above(q1_ref, q2_ref, 1),
            below(q1_ref, q2_ref, 1),
        ]
        fluxes = []
        for j in range(own + 2):
            grad = l_ref[j : j + 1, :] + extra[j]
            safe = jnp.where(weights[j] == 0.0, 1.0, weights[j])
            fluxes.append(f_ref[j : j + 1, :] + 0.5 * grad / safe)

    specs = []
    for j in range(own):
        y = band_ref[j].astype(jnp.float32) + oy_ref[j : j + 1, :]
        specs.append((y, ox_ref[j : j + 1, :], own_coefs(psf_ref, cell_ref, j), col_ref[j], None))
    specs.append((
        above(x1_ref, x2_ref, 0) - strip_rows, above(x1_ref, x2_ref, 1),
        [jnp.where(even, xs2_ref[4, k], xs1_ref[4, k]) for k in range(9)],
        jnp.where(even, xs2_ref[4, 9], xs1_ref[4, 9]).astype(jnp.int32), REACH,
    ))
    specs.append((
        below(x1_ref, x2_ref, 0) + strip_rows, below(x1_ref, x2_ref, 1),
        [jnp.where(even, xs1_ref[4, k], xs2_ref[4, k]) for k in range(9)],
        jnp.where(even, xs1_ref[4, 9], xs2_ref[4, 9]).astype(jnp.int32), None,
    ))

    canvas[...] = jnp.zeros_like(canvas)
    hpos = lax.broadcasted_iota(jnp.int32, (rows_n, LANES), 0).astype(jnp.float32)
    wpos = lax.broadcasted_iota(jnp.int32, (SPAN, LANES), 0).astype(jnp.float32) - LANES // 2
    spare = jnp.zeros((rows_n, WIN - SPAN), jnp.float32)
    saved = []
    for j, (y, x, c, col, keep) in enumerate(specs):
        rows = profile3(hpos - y)
        if keep is not None:
            rows = tuple(jnp.where(hpos < keep, r, 0.0) for r in rows)
        cols_hi, cols_lo = split_bf16(jnp.concatenate(profile3(wpos - x), axis=1))
        mixed = [
            (c[b] * rows[0] + c[3 + b] * rows[1] + c[6 + b] * rows[2]) * fluxes[j]
            for b in range(3)
        ]
        stamp = presplit_dot(jnp.concatenate(mixed, axis=1), cols_hi, cols_lo, DIMS_NT)
        start = pl.multiple_of(col * LANES, LANES)
        canvas[:, pl.ds(start, WIN)] += pltpu.roll(
            jnp.concatenate([stamp, spare], axis=1), LANES // 2, 1
        )
        saved.append((rows, cols_hi, cols_lo, c, start))
    inner = slice(LANES, LANES + width)
    if final:
        out_ref[...] = img_ref[...] - canvas[:, inner]
        for j in range(own):
            fluxout_ref[j : j + 1, :] = fluxes[j]
        return
    canvas[:, inner] = img_ref[...] - canvas[:, inner]
    canvas[:, 0:LANES] = jnp.zeros((rows_n, LANES), jnp.float32)
    canvas[:, LANES + width :] = jnp.zeros((rows_n, pad_width - LANES - width), jnp.float32)
    fout_ref[...] = jnp.zeros_like(fout_ref)
    lout_ref[...] = jnp.zeros_like(lout_ref)
    partial = []
    for j, (rows, cols_hi, cols_lo, c, start) in enumerate(saved):
        window = pltpu.roll(canvas[:, pl.ds(start, WIN)], WIN - LANES // 2, 1)[:, :SPAN]
        across_all = presplit_dot(window, cols_hi, cols_lo, DIMS_NN)
        grad = None
        for a in range(3):
            for b in range(3):
                paired = jnp.sum(rows[a] * across_all[:, b * LANES : (b + 1) * LANES], axis=0,
                                 keepdims=True)
                term = c[3 * a + b] * paired
                grad = term if grad is None else grad + term
        partial.append(grad)
        fout_ref[j : j + 1, :] = fluxes[j]
        lout_ref[j : j + 1, :] = grad
    top_part = jnp.where(top_first, partial[0], partial[1])
    bot_part = jnp.where(top_first, partial[1], partial[0])
    first_ref, second_ref = up_ref, down_ref
    first_ref[0:1, :] = jnp.where(even, partial[own + 1], partial[own])
    first_ref[1:2, :] = jnp.where(even, bot_part, top_part)
    second_ref[0:1, :] = jnp.where(even, partial[own], partial[own + 1])
    second_ref[1:2, :] = jnp.where(even, top_part, bot_part)


def vmem_operands(*arrays):
    return [pltpu.with_memory_space_constraint(a, pltpu.VMEM) for a in arrays]


def local(image, band_row, col_block, cell_index, offset_y, offset_x, flux_start, psf_coef):
    strip_rows, strip_width = image.shape
    own = band_row.shape[0]
    f32 = jnp.float32
    smem = pl.BlockSpec(memory_space=pltpu.SMEM)
    vmem = pl.BlockSpec(memory_space=pltpu.VMEM)
    packet = jax.ShapeDtypeStruct((SLOTS, LANES), f32)
    send_within, send_across, weight = pl.pallas_call(
        setup_kernel,
        out_shape=(packet, packet, jax.ShapeDtypeStruct((own, LANES), f32)),
        in_specs=[smem] * 4 + [vmem] * 3,
        out_specs=(vmem, vmem, vmem),
    )(band_row, col_block, cell_index, psf_coef, offset_y, offset_x, flux_start)
    got_within, got_across = exchange(send_within, send_across)

    blocks = own + 2
    flops = 2 * 3 * 2 * strip_rows * WIN * 3 * LANES * blocks
    state_shape = jax.ShapeDtypeStruct((SLOTS, LANES), f32)
    part_shape = pltpu.VMEM((2, LANES), f32)
    common = (band_row, col_block, cell_index, psf_coef, got_within, got_across,
              offset_y, offset_x, weight, got_within, got_across, image)

    def phase(final, first, fluxes, partials, swap_within, swap_across):
        kernel = functools.partial(phase_kernel, final, first)
        if final:
            out_shape = (jax.ShapeDtypeStruct((strip_rows, strip_width), f32),
                         jax.ShapeDtypeStruct((own, LANES), f32))
            out_specs = (vmem, vmem)
        else:
            out_shape = (state_shape, state_shape, part_shape, part_shape)
            out_specs = (vmem, vmem, vmem, vmem)
        return pl.pallas_call(
            kernel,
            out_shape=out_shape,
            in_specs=[smem] * 6 + [vmem] * 10,
            out_specs=out_specs,
            scratch_shapes=[pltpu.VMEM((strip_rows, strip_width + 2 * LANES), f32)],
            cost_estimate=pl.CostEstimate(
                flops=flops, transcendentals=blocks * 2 * (strip_rows + WIN) * LANES,
                bytes_accessed=4 * strip_rows * strip_width * 2,
            ),
        )(*common, fluxes, partials, *vmem_operands(swap_within, swap_across))

    state, partials, within, across = phase(False, True, flux_start, flux_start, flux_start, flux_start)
    for iteration in range(1, ITERS):
        swap_within, swap_across = exchange(within, across)
        state, partials, within, across = phase(False, False, state, partials, swap_within, swap_across)
    swap_within, swap_across = exchange(within, across)
    residual, fluxes = phase(True, False, state, partials, swap_within, swap_across)
    return (fluxes, residual)


def solution(mesh):
    return jax.shard_map(
        local,
        mesh=mesh,
        in_specs=(
            P(("groups", "ty"), None),
            P(("groups", "ty")),
            P(("groups", "ty")),
            P(("groups", "ty")),
            P(("groups", "ty"), None),
            P(("groups", "ty"), None),
            P(("groups", "ty"), None),
            P(),
        ),
        out_specs=(P(("groups", "ty"), None), P(("groups", "ty"), None)),
        check_vma=False,
    )
```

```python
import functools

import jax
import jax.numpy as jnp
from jax import lax
from jax.experimental import pallas as pl
from jax.experimental.pallas import tpu as pltpu
from jax.sharding import PartitionSpec as P

REACH = 15
ITERS = 2
LANES = 128
WIN = 384
SPAN = 256
SLOTS = 8

DIMS_NT = (((1,), (1,)), ((), ()))
DIMS_NN = (((1,), (0,)), ((), ()))


def profile3(dist):
    tapered_arg = dist * (1.0 / 15.5)
    tapered = jnp.maximum(0.0, 1.0 - tapered_arg * tapered_arg)
    scaled = dist * (1.0 / 1.7)
    core_part = jnp.exp(-0.5 * scaled * scaled) * tapered
    wing_part = jnp.exp(dist * dist * (-1.0 / 72.0)) * tapered
    return core_part, scaled * core_part, wing_part


def split_dot(lhs, rhs, dims):
    lhs_hi = lhs.astype(jnp.bfloat16)
    lhs_lo = (lhs - lhs_hi.astype(jnp.float32)).astype(jnp.bfloat16)
    rhs_hi = rhs.astype(jnp.bfloat16)
    rhs_lo = (rhs - rhs_hi.astype(jnp.float32)).astype(jnp.bfloat16)

    def one(a, b):
        return lax.dot_general(a, b, dims, preferred_element_type=jnp.float32)

    return one(lhs_hi, rhs_hi) + (one(lhs_hi, rhs_lo) + one(lhs_lo, rhs_hi))


def split_bf16(value):
    hi = value.astype(jnp.bfloat16)
    return hi, (value - hi.astype(jnp.float32)).astype(jnp.bfloat16)


def presplit_dot(lhs, rhs_hi, rhs_lo, dims):
    lhs_hi, lhs_lo = split_bf16(lhs)

    def one(a, b):
        return lax.dot_general(a, b, dims, preferred_element_type=jnp.float32)

    return one(lhs_hi, rhs_hi) + (one(lhs_hi, rhs_lo) + one(lhs_lo, rhs_hi))


def exchange(first, second):
    count = lax.axis_size("ty")
    within = [(i, i ^ 1) for i in range(count) if (i ^ 1) < count]
    across = [(i, i + 1) for i in range(1, count - 1, 2)] + [
        (i + 1, i) for i in range(1, count - 1, 2)
    ]
    return lax.ppermute(first, "ty", within), lax.ppermute(second, "ty", across)


def even_device():
    return lax.axis_index("ty") % 2 == 0


def own_coefs(psf_ref, cell_ref, j):
    cell = cell_ref[j]
    return [psf_ref[k, cell] for k in range(9)]


def weight_kernel(band_ref, cell_ref, psf_ref, oy_ref, ox_ref, w_ref):
    own = oy_ref.shape[0]
    offs = lax.broadcasted_iota(jnp.int32, (32, LANES), 0).astype(jnp.float32) - 15.0
    for j in range(own):
        y = band_ref[j].astype(jnp.float32) + oy_ref[j : j + 1, :]
        x = ox_ref[j : j + 1, :]
        c = own_coefs(psf_ref, cell_ref, j)
        rows = profile3(jnp.floor(y) + offs - y)
        cols = profile3(jnp.floor(x) + offs - x)
        gram_r = [[jnp.sum(rows[a] * rows[b], axis=0, keepdims=True) for b in range(3)] for a in range(3)]
        gram_c = [[jnp.sum(cols[a] * cols[b], axis=0, keepdims=True) for b in range(3)] for a in range(3)]
        weight = None
        for a in range(3):
            for cc in range(3):
                inner = None
                for b in range(3):
                    for d in range(3):
                        term = (c[3 * a + b] * c[3 * cc + d]) * gram_c[b][d]
                        inner = term if inner is None else inner + term
                term = gram_r[a][cc] * inner
                weight = term if weight is None else weight + term
        w_ref[j : j + 1, :] = weight


def setup_kernel(band_ref, col_ref, cell_ref, psf_ref, oy_ref, ox_ref, f_ref, up_ref, down_ref):
    own = oy_ref.shape[0]
    lane = lax.broadcasted_iota(jnp.int32, (1, LANES), 1)
    ys, metas = [], []
    for j in range(own):
        ys.append(band_ref[j].astype(jnp.float32) + oy_ref[j : j + 1, :])
        c = own_coefs(psf_ref, cell_ref, j)
        meta = jnp.zeros((1, LANES), jnp.float32)
        for k in range(9):
            meta = jnp.where(lane == k, c[k], meta)
        metas.append(jnp.where(lane == 9, col_ref[j].astype(jnp.float32), meta))
    top_first = band_ref[0] <= band_ref[1]

    def pick(first, second):
        return jnp.where(top_first, first, second), jnp.where(top_first, second, first)

    tops, bots = zip(*[
        pick(*pair) for pair in (
            (ys[0], ys[1]), (ox_ref[0:1, :], ox_ref[1:2, :]), (f_ref[0:1, :], f_ref[1:2, :]),
            (metas[0], metas[1]),
        )
    ])
    even = even_device()
    first_ref, second_ref = up_ref, down_ref
    first_ref[...] = jnp.zeros_like(first_ref)
    second_ref[...] = jnp.zeros_like(second_ref)
    for r in range(4):
        first_ref[r : r + 1, :] = jnp.where(even, bots[r], tops[r])
        second_ref[r : r + 1, :] = jnp.where(even, tops[r], bots[r])


def phase_kernel(
    final, first,
    band_ref, col_ref, cell_ref, psf_ref, xs1_ref, xs2_ref,
    oy_ref, ox_ref, w_ref, x1_ref, x2_ref, img_ref, f_ref, l_ref, q1_ref, q2_ref,
    *rest,
):
    even = even_device()

    def above(ref1, ref2, row):
        return jnp.where(even, ref2[row : row + 1, :], ref1[row : row + 1, :])

    def below(ref1, ref2, row):
        return jnp.where(even, ref1[row : row + 1, :], ref2[row : row + 1, :])

    if final:
        out_ref, fluxout_ref, canvas = rest
    else:
        fout_ref, lout_ref, up_ref, down_ref, canvas = rest
    rows_n, pad_width = canvas.shape
    strip_rows, width = img_ref.shape
    own = oy_ref.shape[0]
    top_first = band_ref[0] <= band_ref[1]

    if first:
        fluxes = [f_ref[0:1, :], f_ref[1:2, :], above(x1_ref, x2_ref, 2), below(x1_ref, x2_ref, 2)]
    else:
        weights = [w_ref[0:1, :], w_ref[1:2, :], above(q1_ref, q2_ref, 2), below(q1_ref, q2_ref, 2)]
        from_above = above(q1_ref, q2_ref, 0)
        from_below = below(q1_ref, q2_ref, 0)
        extra = [
            jnp.where(top_first, from_above, from_below),
            jnp.where(top_first, from_below, from_above),
            above(q1_ref, q2_ref, 1),
            below(q1_ref, q2_ref, 1),
        ]
        fluxes = []
        for j in range(own + 2):
            grad = l_ref[j : j + 1, :] + extra[j]
            safe = jnp.where(weights[j] == 0.0, 1.0, weights[j])
            fluxes.append(f_ref[j : j + 1, :] + 0.5 * grad / safe)

    specs = []
    for j in range(own):
        y = band_ref[j].astype(jnp.float32) + oy_ref[j : j + 1, :]
        specs.append((y, ox_ref[j : j + 1, :], own_coefs(psf_ref, cell_ref, j), col_ref[j], None))
    specs.append((
        above(x1_ref, x2_ref, 0) - strip_rows, above(x1_ref, x2_ref, 1),
        [jnp.where(even, xs2_ref[3, k], xs1_ref[3, k]) for k in range(9)],
        jnp.where(even, xs2_ref[3, 9], xs1_ref[3, 9]).astype(jnp.int32), REACH,
    ))
    specs.append((
        below(x1_ref, x2_ref, 0) + strip_rows, below(x1_ref, x2_ref, 1),
        [jnp.where(even, xs1_ref[3, k], xs2_ref[3, k]) for k in range(9)],
        jnp.where(even, xs1_ref[3, 9], xs2_ref[3, 9]).astype(jnp.int32), None,
    ))

    canvas[...] = jnp.zeros_like(canvas)
    hpos = lax.broadcasted_iota(jnp.int32, (rows_n, LANES), 0).astype(jnp.float32)
    wpos = lax.broadcasted_iota(jnp.int32, (SPAN, LANES), 0).astype(jnp.float32) - LANES // 2
    spare = jnp.zeros((rows_n, WIN - SPAN), jnp.float32)
    saved = []
    for j, (y, x, c, col, keep) in enumerate(specs):
        rows = profile3(hpos - y)
        if keep is not None:
            rows = tuple(jnp.where(hpos < keep, r, 0.0) for r in rows)
        cols_hi, cols_lo = split_bf16(jnp.concatenate(profile3(wpos - x), axis=1))
        mixed = [
            (c[b] * rows[0] + c[3 + b] * rows[1] + c[6 + b] * rows[2]) * fluxes[j]
            for b in range(3)
        ]
        stamp = presplit_dot(jnp.concatenate(mixed, axis=1), cols_hi, cols_lo, DIMS_NT)
        start = pl.multiple_of(col * LANES, LANES)
        canvas[:, pl.ds(start, WIN)] += pltpu.roll(
            jnp.concatenate([stamp, spare], axis=1), LANES // 2, 1
        )
        saved.append((rows, cols_hi, cols_lo, c, start))
    inner = slice(LANES, LANES + width)
    if final:
        out_ref[...] = img_ref[...] - canvas[:, inner]
        for j in range(own):
            fluxout_ref[j : j + 1, :] = fluxes[j]
        return
    canvas[:, inner] = img_ref[...] - canvas[:, inner]
    canvas[:, 0:LANES] = jnp.zeros((rows_n, LANES), jnp.float32)
    canvas[:, LANES + width :] = jnp.zeros((rows_n, pad_width - LANES - width), jnp.float32)
    fout_ref[...] = jnp.zeros_like(fout_ref)
    lout_ref[...] = jnp.zeros_like(lout_ref)
    partial = []
    for j, (rows, cols_hi, cols_lo, c, start) in enumerate(saved):
        window = pltpu.roll(canvas[:, pl.ds(start, WIN)], WIN - LANES // 2, 1)[:, :SPAN]
        across_all = presplit_dot(window, cols_hi, cols_lo, DIMS_NN)
        grad = None
        for a in range(3):
            for b in range(3):
                paired = jnp.sum(rows[a] * across_all[:, b * LANES : (b + 1) * LANES], axis=0,
                                 keepdims=True)
                term = c[3 * a + b] * paired
                grad = term if grad is None else grad + term
        partial.append(grad)
        fout_ref[j : j + 1, :] = fluxes[j]
        lout_ref[j : j + 1, :] = grad
    top_part = jnp.where(top_first, partial[0], partial[1])
    bot_part = jnp.where(top_first, partial[1], partial[0])
    top_weight = jnp.where(top_first, w_ref[0:1, :], w_ref[1:2, :])
    bot_weight = jnp.where(top_first, w_ref[1:2, :], w_ref[0:1, :])
    first_ref, second_ref = up_ref, down_ref
    first_ref[0:1, :] = jnp.where(even, partial[own + 1], partial[own])
    first_ref[1:2, :] = jnp.where(even, bot_part, top_part)
    first_ref[2:3, :] = jnp.where(even, bot_weight, top_weight)
    second_ref[0:1, :] = jnp.where(even, partial[own], partial[own + 1])
    second_ref[1:2, :] = jnp.where(even, top_part, bot_part)
    second_ref[2:3, :] = jnp.where(even, top_weight, bot_weight)


def vmem_operands(*arrays):
    return [pltpu.with_memory_space_constraint(a, pltpu.VMEM) for a in arrays]


def local(image, band_row, col_block, cell_index, offset_y, offset_x, flux_start, psf_coef):
    strip_rows, strip_width = image.shape
    own = band_row.shape[0]
    f32 = jnp.float32
    smem = pl.BlockSpec(memory_space=pltpu.SMEM)
    vmem = pl.BlockSpec(memory_space=pltpu.VMEM)
    packet = jax.ShapeDtypeStruct((SLOTS, LANES), f32)
    send_within, send_across = pl.pallas_call(
        setup_kernel,
        out_shape=(packet, packet),
        in_specs=[smem] * 4 + [vmem] * 3,
        out_specs=(vmem, vmem),
    )(band_row, col_block, cell_index, psf_coef, offset_y, offset_x, flux_start)
    got_within, got_across = exchange(send_within, send_across)
    weight = pl.pallas_call(
        weight_kernel,
        out_shape=jax.ShapeDtypeStruct((own, LANES), f32),
        in_specs=[smem] * 3 + [vmem] * 2,
        out_specs=vmem,
        cost_estimate=pl.CostEstimate(
            flops=own * 60 * 32 * LANES * 2, transcendentals=own * 4 * 32 * LANES,
            bytes_accessed=4 * 4 * own * LANES,
        ),
    )(band_row, cell_index, psf_coef, offset_y, offset_x)

    blocks = own + 2
    flops = 2 * 3 * 2 * strip_rows * WIN * 3 * LANES * blocks
    state_shape = jax.ShapeDtypeStruct((SLOTS, LANES), f32)
    part_shape = pltpu.VMEM((4, LANES), f32)
    common = (band_row, col_block, cell_index, psf_coef, got_within, got_across,
              offset_y, offset_x, weight, got_within, got_across, image)

    def phase(final, first, fluxes, partials, swap_within, swap_across):
        kernel = functools.partial(phase_kernel, final, first)
        if final:
            out_shape = (jax.ShapeDtypeStruct((strip_rows, strip_width), f32),
                         jax.ShapeDtypeStruct((own, LANES), f32))
            out_specs = (vmem, vmem)
        else:
            out_shape = (state_shape, state_shape, part_shape, part_shape)
            out_specs = (vmem, vmem, vmem, vmem)
        return pl.pallas_call(
            kernel,
            out_shape=out_shape,
            in_specs=[smem] * 6 + [vmem] * 10,
            out_specs=out_specs,
            scratch_shapes=[pltpu.VMEM((strip_rows, strip_width + 2 * LANES), f32)],
            cost_estimate=pl.CostEstimate(
                flops=flops, transcendentals=blocks * 2 * (strip_rows + WIN) * LANES,
                bytes_accessed=4 * strip_rows * strip_width * 2,
            ),
        )(*common, fluxes, partials, *vmem_operands(swap_within, swap_across))

    state, partials, within, across = phase(False, True, flux_start, flux_start, flux_start, flux_start)
    for iteration in range(1, ITERS):
        swap_within, swap_across = exchange(within, across)
        state, partials, within, across = phase(False, False, state, partials, swap_within, swap_across)
    swap_within, swap_across = exchange(within, across)
    residual, fluxes = phase(True, False, state, partials, swap_within, swap_across)
    return (fluxes, residual)


def solution(mesh):
    return jax.shard_map(
        local,
        mesh=mesh,
        in_specs=(
            P(("groups", "ty"), None),
            P(("groups", "ty")),
            P(("groups", "ty")),
            P(("groups", "ty")),
            P(("groups", "ty"), None),
            P(("groups", "ty"), None),
            P(("groups", "ty"), None),
            P(),
        ),
        out_specs=(P(("groups", "ty"), None), P(("groups", "ty"), None)),
        check_vma=False,
    )
```

```python
import functools

import jax
import jax.numpy as jnp
from jax import lax
from jax.experimental import pallas as pl
from jax.experimental.pallas import tpu as pltpu
from jax.sharding import PartitionSpec as P

REACH = 15
ITERS = 2
LANES = 128
WIN = 384
SPAN = 256
SLOTS = 8

DIMS_NT = (((1,), (1,)), ((), ()))
DIMS_NN = (((1,), (0,)), ((), ()))


def profile3(dist):
    tapered_arg = dist * (1.0 / 15.5)
    tapered = jnp.maximum(0.0, 1.0 - tapered_arg * tapered_arg)
    scaled = dist * (1.0 / 1.7)
    core_part = jnp.exp(-0.5 * scaled * scaled) * tapered
    wing_part = jnp.exp(dist * dist * (-1.0 / 72.0)) * tapered
    return core_part, scaled * core_part, wing_part


def split_dot(lhs, rhs, dims):
    lhs_hi = lhs.astype(jnp.bfloat16)
    lhs_lo = (lhs - lhs_hi.astype(jnp.float32)).astype(jnp.bfloat16)
    rhs_hi = rhs.astype(jnp.bfloat16)
    rhs_lo = (rhs - rhs_hi.astype(jnp.float32)).astype(jnp.bfloat16)

    def one(a, b):
        return lax.dot_general(a, b, dims, preferred_element_type=jnp.float32)

    return one(lhs_hi, rhs_hi) + (one(lhs_hi, rhs_lo) + one(lhs_lo, rhs_hi))


def split_bf16(value):
    hi = value.astype(jnp.bfloat16)
    return hi, (value - hi.astype(jnp.float32)).astype(jnp.bfloat16)


def presplit_dot(lhs, rhs_hi, rhs_lo, dims):
    lhs_hi, lhs_lo = split_bf16(lhs)

    def one(a, b):
        return lax.dot_general(a, b, dims, preferred_element_type=jnp.float32)

    return one(lhs_hi, rhs_hi) + (one(lhs_hi, rhs_lo) + one(lhs_lo, rhs_hi))


def exchange(first, second):
    count = lax.axis_size("ty")
    within = [(i, i ^ 1) for i in range(count) if (i ^ 1) < count]
    across = [(i, i + 1) for i in range(1, count - 1, 2)] + [
        (i + 1, i) for i in range(1, count - 1, 2)
    ]
    return lax.ppermute(first, "ty", within), lax.ppermute(second, "ty", across)


def even_device():
    return lax.axis_index("ty") % 2 == 0


def own_coefs(psf_ref, cell_ref, j):
    cell = cell_ref[j]
    return [psf_ref[k, cell] for k in range(9)]


def setup_kernel(band_ref, col_ref, cell_ref, psf_ref, oy_ref, ox_ref, f_ref, up_ref, down_ref, w_ref):
    own = oy_ref.shape[0]
    offs = lax.broadcasted_iota(jnp.int32, (32, LANES), 0).astype(jnp.float32) - 15.0
    lane = lax.broadcasted_iota(jnp.int32, (1, LANES), 1)
    ys, metas, weights = [], [], []
    for j in range(own):
        y = band_ref[j].astype(jnp.float32) + oy_ref[j : j + 1, :]
        x = ox_ref[j : j + 1, :]
        c = own_coefs(psf_ref, cell_ref, j)
        rows = profile3(jnp.floor(y) + offs - y)
        cols = profile3(jnp.floor(x) + offs - x)
        gram_r = [[jnp.sum(rows[a] * rows[b], axis=0, keepdims=True) for b in range(3)] for a in range(3)]
        gram_c = [[jnp.sum(cols[a] * cols[b], axis=0, keepdims=True) for b in range(3)] for a in range(3)]
        weight = None
        for a in range(3):
            for cc in range(3):
                inner = None
                for b in range(3):
                    for d in range(3):
                        term = (c[3 * a + b] * c[3 * cc + d]) * gram_c[b][d]
                        inner = term if inner is None else inner + term
                term = gram_r[a][cc] * inner
                weight = term if weight is None else weight + term
        w_ref[j : j + 1, :] = weight
        meta = jnp.zeros((1, LANES), jnp.float32)
        for k in range(9):
            meta = jnp.where(lane == k, c[k], meta)
        meta = jnp.where(lane == 9, col_ref[j].astype(jnp.float32), meta)
        ys.append(y)
        metas.append(meta)
        weights.append(weight)
    top_first = band_ref[0] <= band_ref[1]

    def pick(first, second):
        return jnp.where(top_first, first, second), jnp.where(top_first, second, first)

    tops, bots = zip(*[
        pick(*pair) for pair in (
            (ys[0], ys[1]), (ox_ref[0:1, :], ox_ref[1:2, :]), (f_ref[0:1, :], f_ref[1:2, :]),
            (weights[0], weights[1]), (metas[0], metas[1]),
        )
    ])
    even = even_device()
    first_ref, second_ref = up_ref, down_ref
    first_ref[...] = jnp.zeros_like(first_ref)
    second_ref[...] = jnp.zeros_like(second_ref)
    for r in range(5):
        first_ref[r : r + 1, :] = jnp.where(even, bots[r], tops[r])
        second_ref[r : r + 1, :] = jnp.where(even, tops[r], bots[r])


def phase_kernel(
    final, first,
    band_ref, col_ref, cell_ref, psf_ref, xs1_ref, xs2_ref,
    oy_ref, ox_ref, w_ref, x1_ref, x2_ref, img_ref, f_ref, l_ref, q1_ref, q2_ref,
    *rest,
):
    even = even_device()

    def above(ref1, ref2, row):
        return jnp.where(even, ref2[row : row + 1, :], ref1[row : row + 1, :])

    def below(ref1, ref2, row):
        return jnp.where(even, ref1[row : row + 1, :], ref2[row : row + 1, :])

    if final:
        out_ref, fluxout_ref, canvas = rest
    else:
        fout_ref, lout_ref, up_ref, down_ref, canvas = rest
    rows_n, pad_width = canvas.shape
    strip_rows, width = img_ref.shape
    own = oy_ref.shape[0]
    top_first = band_ref[0] <= band_ref[1]

    if first:
        fluxes = [f_ref[0:1, :], f_ref[1:2, :], above(x1_ref, x2_ref, 2), below(x1_ref, x2_ref, 2)]
    else:
        weights = [w_ref[0:1, :], w_ref[1:2, :], above(x1_ref, x2_ref, 3), below(x1_ref, x2_ref, 3)]
        from_above = above(q1_ref, q2_ref, 0)
        from_below = below(q1_ref, q2_ref, 0)
        extra = [
            jnp.where(top_first, from_above, from_below),
            jnp.where(top_first, from_below, from_above),
            above(q1_ref, q2_ref, 1),
            below(q1_ref, q2_ref, 1),
        ]
        fluxes = []
        for j in range(own + 2):
            grad = l_ref[j : j + 1, :] + extra[j]
            safe = jnp.where(weights[j] == 0.0, 1.0, weights[j])
            fluxes.append(f_ref[j : j + 1, :] + 0.5 * grad / safe)

    specs = []
    for j in range(own):
        y = band_ref[j].astype(jnp.float32) + oy_ref[j : j + 1, :]
        specs.append((y, ox_ref[j : j + 1, :], own_coefs(psf_ref, cell_ref, j), col_ref[j], None))
    specs.append((
        above(x1_ref, x2_ref, 0) - strip_rows, above(x1_ref, x2_ref, 1),
        [jnp.where(even, xs2_ref[4, k], xs1_ref[4, k]) for k in range(9)],
        jnp.where(even, xs2_ref[4, 9], xs1_ref[4, 9]).astype(jnp.int32), REACH,
    ))
    specs.append((
        below(x1_ref, x2_ref, 0) + strip_rows, below(x1_ref, x2_ref, 1),
        [jnp.where(even, xs1_ref[4, k], xs2_ref[4, k]) for k in range(9)],
        jnp.where(even, xs1_ref[4, 9], xs2_ref[4, 9]).astype(jnp.int32), None,
    ))

    canvas[...] = jnp.zeros_like(canvas)
    hpos = lax.broadcasted_iota(jnp.int32, (rows_n, LANES), 0).astype(jnp.float32)
    wpos = lax.broadcasted_iota(jnp.int32, (SPAN, LANES), 0).astype(jnp.float32) - LANES // 2
    spare = jnp.zeros((rows_n, WIN - SPAN), jnp.float32)
    saved = []
    for j, (y, x, c, col, keep) in enumerate(specs):
        rows = profile3(hpos - y)
        if keep is not None:
            rows = tuple(jnp.where(hpos < keep, r, 0.0) for r in rows)
        cols_hi, cols_lo = split_bf16(jnp.concatenate(profile3(wpos - x), axis=1))
        mixed = [
            (c[b] * rows[0] + c[3 + b] * rows[1] + c[6 + b] * rows[2]) * fluxes[j]
            for b in range(3)
        ]
        stamp = presplit_dot(jnp.concatenate(mixed, axis=1), cols_hi, cols_lo, DIMS_NT)
        start = pl.multiple_of(col * LANES, LANES)
        canvas[:, pl.ds(start, WIN)] += pltpu.roll(
            jnp.concatenate([stamp, spare], axis=1), LANES // 2, 1
        )
        saved.append((rows, cols_hi, cols_lo, c, start))
    inner = slice(LANES, LANES + width)
    if final:
        out_ref[...] = img_ref[...] - canvas[:, inner]
        for j in range(own):
            fluxout_ref[j : j + 1, :] = fluxes[j]
        return
    canvas[:, inner] = img_ref[...] - canvas[:, inner]
    canvas[:, 0:LANES] = jnp.zeros((rows_n, LANES), jnp.float32)
    canvas[:, LANES + width :] = jnp.zeros((rows_n, pad_width - LANES - width), jnp.float32)
    fout_ref[...] = jnp.zeros_like(fout_ref)
    lout_ref[...] = jnp.zeros_like(lout_ref)
    partial = []
    for j, (rows, cols_hi, cols_lo, c, start) in enumerate(saved):
        window = pltpu.roll(canvas[:, pl.ds(start, WIN)], WIN - LANES // 2, 1)[:, :SPAN]
        across_all = presplit_dot(window, cols_hi, cols_lo, DIMS_NN)
        grad = None
        for a in range(3):
            for b in range(3):
                paired = jnp.sum(rows[a] * across_all[:, b * LANES : (b + 1) * LANES], axis=0,
                                 keepdims=True)
                term = c[3 * a + b] * paired
                grad = term if grad is None else grad + term
        partial.append(grad)
        fout_ref[j : j + 1, :] = fluxes[j]
        lout_ref[j : j + 1, :] = grad
    top_part = jnp.where(top_first, partial[0], partial[1])
    bot_part = jnp.where(top_first, partial[1], partial[0])
    first_ref, second_ref = up_ref, down_ref
    first_ref[0:1, :] = jnp.where(even, partial[own + 1], partial[own])
    first_ref[1:2, :] = jnp.where(even, bot_part, top_part)
    second_ref[0:1, :] = jnp.where(even, partial[own], partial[own + 1])
    second_ref[1:2, :] = jnp.where(even, top_part, bot_part)


def vmem_operands(*arrays):
    return [pltpu.with_memory_space_constraint(a, pltpu.VMEM) for a in arrays]


def local(image, band_row, col_block, cell_index, offset_y, offset_x, flux_start, psf_coef):
    strip_rows, strip_width = image.shape
    own = band_row.shape[0]
    f32 = jnp.float32
    smem = pl.BlockSpec(memory_space=pltpu.SMEM)
    vmem = pl.BlockSpec(memory_space=pltpu.VMEM)
    packet = pltpu.VMEM((SLOTS, LANES), f32)
    send_within, send_across, weight = pl.pallas_call(
        setup_kernel,
        out_shape=(packet, packet, pltpu.VMEM((own, LANES), f32)),
        in_specs=[smem] * 4 + [vmem] * 3,
        out_specs=(vmem, vmem, vmem),
    )(band_row, col_block, cell_index, psf_coef, *vmem_operands(offset_y, offset_x, flux_start))
    got_within, got_across = exchange(send_within, send_across)

    blocks = own + 2
    flops = 2 * 3 * 2 * strip_rows * WIN * 3 * LANES * blocks
    state_shape = pltpu.VMEM((SLOTS, LANES), f32)
    part_shape = pltpu.VMEM((2, LANES), f32)
    common = (band_row, col_block, cell_index, psf_coef, got_within, got_across,
              *vmem_operands(offset_y, offset_x, weight, got_within, got_across), image)

    def phase(final, first, fluxes, partials, swap_within, swap_across):
        kernel = functools.partial(phase_kernel, final, first)
        if final:
            out_shape = (jax.ShapeDtypeStruct((strip_rows, strip_width), f32),
                         jax.ShapeDtypeStruct((own, LANES), f32))
            out_specs = (vmem, vmem)
        else:
            out_shape = (state_shape, state_shape, part_shape, part_shape)
            out_specs = (vmem, vmem, vmem, vmem)
        return pl.pallas_call(
            kernel,
            out_shape=out_shape,
            in_specs=[smem] * 6 + [vmem] * 10,
            out_specs=out_specs,
            scratch_shapes=[pltpu.VMEM((strip_rows, strip_width + 2 * LANES), f32)],
            cost_estimate=pl.CostEstimate(
                flops=flops, transcendentals=blocks * 2 * (strip_rows + WIN) * LANES,
                bytes_accessed=4 * strip_rows * strip_width * 2,
            ),
        )(*common, *vmem_operands(fluxes, partials, swap_within, swap_across))

    state, partials, within, across = phase(False, True, flux_start, flux_start, flux_start, flux_start)
    for iteration in range(1, ITERS):
        swap_within, swap_across = exchange(within, across)
        state, partials, within, across = phase(False, False, state, partials, swap_within, swap_across)
    swap_within, swap_across = exchange(within, across)
    residual, fluxes = phase(True, False, state, partials, swap_within, swap_across)
    return (fluxes, residual)


def solution(mesh):
    return jax.shard_map(
        local,
        mesh=mesh,
        in_specs=(
            P(("groups", "ty"), None),
            P(("groups", "ty")),
            P(("groups", "ty")),
            P(("groups", "ty")),
            P(("groups", "ty"), None),
            P(("groups", "ty"), None),
            P(("groups", "ty"), None),
            P(),
        ),
        out_specs=(P(("groups", "ty"), None), P(("groups", "ty"), None)),
        check_vma=False,
    )
```

```python
import functools

import jax
import jax.numpy as jnp
from jax import lax
from jax.experimental import pallas as pl
from jax.experimental.pallas import tpu as pltpu
from jax.sharding import PartitionSpec as P

REACH = 15
ITERS = 2
LANES = 128
WIN = 384
SPAN = 256
SLOTS = 8

DIMS_NT = (((1,), (1,)), ((), ()))
DIMS_NN = (((1,), (0,)), ((), ()))


def profile3(dist):
    tapered_arg = dist * (1.0 / 15.5)
    tapered = jnp.maximum(0.0, 1.0 - tapered_arg * tapered_arg)
    scaled = dist * (1.0 / 1.7)
    core_part = jnp.exp(-0.5 * scaled * scaled) * tapered
    wing_part = jnp.exp(dist * dist * (-1.0 / 72.0)) * tapered
    return core_part, scaled * core_part, wing_part


def split_dot(lhs, rhs, dims):
    lhs_hi = lhs.astype(jnp.bfloat16)
    lhs_lo = (lhs - lhs_hi.astype(jnp.float32)).astype(jnp.bfloat16)
    rhs_hi = rhs.astype(jnp.bfloat16)
    rhs_lo = (rhs - rhs_hi.astype(jnp.float32)).astype(jnp.bfloat16)

    def one(a, b):
        return lax.dot_general(a, b, dims, preferred_element_type=jnp.float32)

    return one(lhs_hi, rhs_hi) + (one(lhs_hi, rhs_lo) + one(lhs_lo, rhs_hi))


def split_bf16(value):
    hi = value.astype(jnp.bfloat16)
    return hi, (value - hi.astype(jnp.float32)).astype(jnp.bfloat16)


def presplit_dot(lhs, rhs_hi, rhs_lo, dims):
    lhs_hi, lhs_lo = split_bf16(lhs)

    def one(a, b):
        return lax.dot_general(a, b, dims, preferred_element_type=jnp.float32)

    return one(lhs_hi, rhs_hi) + (one(lhs_hi, rhs_lo) + one(lhs_lo, rhs_hi))


def exchange(first, second):
    count = lax.axis_size("ty")
    within = [(i, i ^ 1) for i in range(count) if (i ^ 1) < count]
    across = [(i, i + 1) for i in range(1, count - 1, 2)] + [
        (i + 1, i) for i in range(1, count - 1, 2)
    ]
    return lax.ppermute(first, "ty", within), lax.ppermute(second, "ty", across)


def even_device():
    return lax.axis_index("ty") % 2 == 0


def own_coefs(psf_ref, cell_ref, j):
    cell = cell_ref[j]
    return [psf_ref[k, cell] for k in range(9)]


def setup_kernel(band_ref, col_ref, cell_ref, psf_ref, oy_ref, ox_ref, f_ref, up_ref, down_ref, w_ref):
    own = oy_ref.shape[0]
    offs = lax.broadcasted_iota(jnp.int32, (32, LANES), 0).astype(jnp.float32) - 15.0
    lane = lax.broadcasted_iota(jnp.int32, (1, LANES), 1)
    ys, metas, weights = [], [], []
    for j in range(own):
        y = band_ref[j].astype(jnp.float32) + oy_ref[j : j + 1, :]
        x = ox_ref[j : j + 1, :]
        c = own_coefs(psf_ref, cell_ref, j)
        rows = profile3(jnp.floor(y) + offs - y)
        cols = profile3(jnp.floor(x) + offs - x)
        gram_r = [[jnp.sum(rows[a] * rows[b], axis=0, keepdims=True) for b in range(3)] for a in range(3)]
        gram_c = [[jnp.sum(cols[a] * cols[b], axis=0, keepdims=True) for b in range(3)] for a in range(3)]
        weight = None
        for a in range(3):
            for cc in range(3):
                inner = None
                for b in range(3):
                    for d in range(3):
                        term = (c[3 * a + b] * c[3 * cc + d]) * gram_c[b][d]
                        inner = term if inner is None else inner + term
                term = gram_r[a][cc] * inner
                weight = term if weight is None else weight + term
        w_ref[j : j + 1, :] = weight
        meta = jnp.zeros((1, LANES), jnp.float32)
        for k in range(9):
            meta = jnp.where(lane == k, c[k], meta)
        meta = jnp.where(lane == 9, col_ref[j].astype(jnp.float32), meta)
        ys.append(y)
        metas.append(meta)
        weights.append(weight)
    top_first = band_ref[0] <= band_ref[1]

    def pick(first, second):
        return jnp.where(top_first, first, second), jnp.where(top_first, second, first)

    tops, bots = zip(*[
        pick(*pair) for pair in (
            (ys[0], ys[1]), (ox_ref[0:1, :], ox_ref[1:2, :]), (f_ref[0:1, :], f_ref[1:2, :]),
            (weights[0], weights[1]), (metas[0], metas[1]),
        )
    ])
    even = even_device()
    first_ref, second_ref = up_ref, down_ref
    first_ref[...] = jnp.zeros_like(first_ref)
    second_ref[...] = jnp.zeros_like(second_ref)
    for r in range(5):
        first_ref[r : r + 1, :] = jnp.where(even, bots[r], tops[r])
        second_ref[r : r + 1, :] = jnp.where(even, tops[r], bots[r])


def phase_kernel(
    final, first,
    band_ref, col_ref, cell_ref, psf_ref, xs1_ref, xs2_ref,
    oy_ref, ox_ref, w_ref, x1_ref, x2_ref, img_ref, f_ref, l_ref, q1_ref, q2_ref,
    *rest,
):
    even = even_device()

    def above(ref1, ref2, row):
        return jnp.where(even, ref2[row : row + 1, :], ref1[row : row + 1, :])

    def below(ref1, ref2, row):
        return jnp.where(even, ref1[row : row + 1, :], ref2[row : row + 1, :])

    if final:
        out_ref, fluxout_ref, canvas = rest
    else:
        fout_ref, lout_ref, up_ref, down_ref, canvas = rest
    rows_n, pad_width = canvas.shape
    strip_rows, width = img_ref.shape
    own = oy_ref.shape[0]
    top_first = band_ref[0] <= band_ref[1]

    if first:
        fluxes = [f_ref[0:1, :], f_ref[1:2, :], above(x1_ref, x2_ref, 2), below(x1_ref, x2_ref, 2)]
    else:
        weights = [w_ref[0:1, :], w_ref[1:2, :], above(x1_ref, x2_ref, 3), below(x1_ref, x2_ref, 3)]
        from_above = above(q1_ref, q2_ref, 0)
        from_below = below(q1_ref, q2_ref, 0)
        extra = [
            jnp.where(top_first, from_above, from_below),
            jnp.where(top_first, from_below, from_above),
            above(q1_ref, q2_ref, 1),
            below(q1_ref, q2_ref, 1),
        ]
        fluxes = []
        for j in range(own + 2):
            grad = l_ref[j : j + 1, :] + extra[j]
            safe = jnp.where(weights[j] == 0.0, 1.0, weights[j])
            fluxes.append(f_ref[j : j + 1, :] + 0.5 * grad / safe)

    specs = []
    for j in range(own):
        y = band_ref[j].astype(jnp.float32) + oy_ref[j : j + 1, :]
        specs.append((y, ox_ref[j : j + 1, :], own_coefs(psf_ref, cell_ref, j), col_ref[j], None))
    specs.append((
        above(x1_ref, x2_ref, 0) - strip_rows, above(x1_ref, x2_ref, 1),
        [jnp.where(even, xs2_ref[4, k], xs1_ref[4, k]) for k in range(9)],
        jnp.where(even, xs2_ref[4, 9], xs1_ref[4, 9]).astype(jnp.int32), REACH,
    ))
    specs.append((
        below(x1_ref, x2_ref, 0) + strip_rows, below(x1_ref, x2_ref, 1),
        [jnp.where(even, xs1_ref[4, k], xs2_ref[4, k]) for k in range(9)],
        jnp.where(even, xs1_ref[4, 9], xs2_ref[4, 9]).astype(jnp.int32), None,
    ))

    canvas[...] = jnp.zeros_like(canvas)
    hpos = lax.broadcasted_iota(jnp.int32, (rows_n, LANES), 0).astype(jnp.float32)
    wpos = lax.broadcasted_iota(jnp.int32, (SPAN, LANES), 0).astype(jnp.float32) - LANES // 2
    spare = jnp.zeros((rows_n, WIN - SPAN), jnp.float32)
    saved = []
    for j, (y, x, c, col, keep) in enumerate(specs):
        rows = profile3(hpos - y)
        if keep is not None:
            rows = tuple(jnp.where(hpos < keep, r, 0.0) for r in rows)
        cols_hi, cols_lo = split_bf16(jnp.concatenate(profile3(wpos - x), axis=1))
        mixed = [
            (c[b] * rows[0] + c[3 + b] * rows[1] + c[6 + b] * rows[2]) * fluxes[j]
            for b in range(3)
        ]
        stamp = presplit_dot(jnp.concatenate(mixed, axis=1), cols_hi, cols_lo, DIMS_NT)
        start = pl.multiple_of(col * LANES, LANES)
        canvas[:, pl.ds(start, WIN)] += pltpu.roll(
            jnp.concatenate([stamp, spare], axis=1), LANES // 2, 1
        )
        saved.append((rows, cols_hi, cols_lo, c, start))
    inner = slice(LANES, LANES + width)
    if final:
        out_ref[...] = img_ref[...] - canvas[:, inner]
        for j in range(own):
            fluxout_ref[j : j + 1, :] = fluxes[j]
        return
    canvas[:, inner] = img_ref[...] - canvas[:, inner]
    canvas[:, 0:LANES] = jnp.zeros((rows_n, LANES), jnp.float32)
    canvas[:, LANES + width :] = jnp.zeros((rows_n, pad_width - LANES - width), jnp.float32)
    fout_ref[...] = jnp.zeros_like(fout_ref)
    lout_ref[...] = jnp.zeros_like(lout_ref)
    partial = []
    for j, (rows, cols_hi, cols_lo, c, start) in enumerate(saved):
        window = pltpu.roll(canvas[:, pl.ds(start, WIN)], WIN - LANES // 2, 1)[:, :SPAN]
        across_all = presplit_dot(window, cols_hi, cols_lo, DIMS_NN)
        grad = None
        for a in range(3):
            for b in range(3):
                paired = jnp.sum(rows[a] * across_all[:, b * LANES : (b + 1) * LANES], axis=0,
                                 keepdims=True)
                term = c[3 * a + b] * paired
                grad = term if grad is None else grad + term
        partial.append(grad)
        fout_ref[j : j + 1, :] = fluxes[j]
        lout_ref[j : j + 1, :] = grad
    top_part = jnp.where(top_first, partial[0], partial[1])
    bot_part = jnp.where(top_first, partial[1], partial[0])
    first_ref, second_ref = up_ref, down_ref
    first_ref[0:1, :] = jnp.where(even, partial[own + 1], partial[own])
    first_ref[1:2, :] = jnp.where(even, bot_part, top_part)
    second_ref[0:1, :] = jnp.where(even, partial[own], partial[own + 1])
    second_ref[1:2, :] = jnp.where(even, top_part, bot_part)


def vmem_operands(*arrays):
    return [pltpu.with_memory_space_constraint(a, pltpu.VMEM) for a in arrays]


def local(image, band_row, col_block, cell_index, offset_y, offset_x, flux_start, psf_coef):
    strip_rows, strip_width = image.shape
    own = band_row.shape[0]
    f32 = jnp.float32
    smem = pl.BlockSpec(memory_space=pltpu.SMEM)
    vmem = pl.BlockSpec(memory_space=pltpu.VMEM)
    packet = pltpu.VMEM((SLOTS, LANES), f32)
    send_within, send_across, weight = pl.pallas_call(
        setup_kernel,
        out_shape=(packet, packet, pltpu.VMEM((own, LANES), f32)),
        in_specs=[smem] * 4 + [vmem] * 3,
        out_specs=(vmem, vmem, vmem),
    )(band_row, col_block, cell_index, psf_coef, offset_y, offset_x, flux_start)
    got_within, got_across = exchange(send_within, send_across)

    blocks = own + 2
    flops = 2 * 3 * 2 * strip_rows * WIN * 3 * LANES * blocks
    state_shape = pltpu.VMEM((SLOTS, LANES), f32)
    part_shape = pltpu.VMEM((2, LANES), f32)
    common = (band_row, col_block, cell_index, psf_coef, got_within, got_across,
              *vmem_operands(offset_y, offset_x, weight, got_within, got_across), image)

    def phase(final, first, fluxes, partials, swap_within, swap_across):
        kernel = functools.partial(phase_kernel, final, first)
        if final:
            out_shape = (jax.ShapeDtypeStruct((strip_rows, strip_width), f32),
                         jax.ShapeDtypeStruct((own, LANES), f32))
            out_specs = (vmem, vmem)
        else:
            out_shape = (state_shape, state_shape, part_shape, part_shape)
            out_specs = (vmem, vmem, vmem, vmem)
        return pl.pallas_call(
            kernel,
            out_shape=out_shape,
            in_specs=[smem] * 6 + [vmem] * 10,
            out_specs=out_specs,
            scratch_shapes=[pltpu.VMEM((strip_rows, strip_width + 2 * LANES), f32)],
            cost_estimate=pl.CostEstimate(
                flops=flops, transcendentals=blocks * 2 * (strip_rows + WIN) * LANES,
                bytes_accessed=4 * strip_rows * strip_width * 2,
            ),
        )(*common, *vmem_operands(fluxes, partials, swap_within, swap_across))

    state, partials, within, across = phase(False, True, flux_start, flux_start, flux_start, flux_start)
    for iteration in range(1, ITERS):
        swap_within, swap_across = exchange(within, across)
        state, partials, within, across = phase(False, False, state, partials, swap_within, swap_across)
    swap_within, swap_across = exchange(within, across)
    residual, fluxes = phase(True, False, state, partials, swap_within, swap_across)
    return (fluxes, residual)


def solution(mesh):
    return jax.shard_map(
        local,
        mesh=mesh,
        in_specs=(
            P(("groups", "ty"), None),
            P(("groups", "ty")),
            P(("groups", "ty")),
            P(("groups", "ty")),
            P(("groups", "ty"), None),
            P(("groups", "ty"), None),
            P(("groups", "ty"), None),
            P(),
        ),
        out_specs=(P(("groups", "ty"), None), P(("groups", "ty"), None)),
        check_vma=False,
    )
```

```python
import functools

import jax
import jax.numpy as jnp
from jax import lax
from jax.experimental import pallas as pl
from jax.experimental.pallas import tpu as pltpu
from jax.sharding import PartitionSpec as P

REACH = 15
ITERS = 2
LANES = 128
WIN = 384
SPAN = 256
SLOTS = 8

DIMS_NT = (((1,), (1,)), ((), ()))
DIMS_NN = (((1,), (0,)), ((), ()))


def profile3(dist):
    tapered_arg = dist * (1.0 / 15.5)
    tapered = jnp.maximum(0.0, 1.0 - tapered_arg * tapered_arg)
    scaled = dist * (1.0 / 1.7)
    core_part = jnp.exp(-0.5 * scaled * scaled) * tapered
    wing_part = jnp.exp(dist * dist * (-1.0 / 72.0)) * tapered
    return core_part, scaled * core_part, wing_part


def split_dot(lhs, rhs, dims):
    lhs_hi = lhs.astype(jnp.bfloat16)
    lhs_lo = (lhs - lhs_hi.astype(jnp.float32)).astype(jnp.bfloat16)
    rhs_hi = rhs.astype(jnp.bfloat16)
    rhs_lo = (rhs - rhs_hi.astype(jnp.float32)).astype(jnp.bfloat16)

    def one(a, b):
        return lax.dot_general(a, b, dims, preferred_element_type=jnp.float32)

    return one(lhs_hi, rhs_hi) + (one(lhs_hi, rhs_lo) + one(lhs_lo, rhs_hi))


def split_bf16(value):
    hi = value.astype(jnp.bfloat16)
    return hi, (value - hi.astype(jnp.float32)).astype(jnp.bfloat16)


def presplit_dot(lhs, rhs_hi, rhs_lo, dims):
    lhs_hi, lhs_lo = split_bf16(lhs)

    def one(a, b):
        return lax.dot_general(a, b, dims, preferred_element_type=jnp.float32)

    return one(lhs_hi, rhs_hi) + (one(lhs_hi, rhs_lo) + one(lhs_lo, rhs_hi))


def exchange(first, second):
    count = lax.axis_size("ty")
    within = [(i, i ^ 1) for i in range(count) if (i ^ 1) < count]
    across = [(i, i + 1) for i in range(1, count - 1, 2)] + [
        (i + 1, i) for i in range(1, count - 1, 2)
    ]
    return lax.ppermute(first, "ty", within), lax.ppermute(second, "ty", across)


def even_device():
    return lax.axis_index("ty") % 2 == 0


def own_coefs(psf_ref, cell_ref, j):
    cell = cell_ref[j]
    return [psf_ref[k, cell] for k in range(9)]


def setup_kernel(band_ref, col_ref, cell_ref, psf_ref, oy_ref, ox_ref, f_ref, up_ref, down_ref, w_ref):
    own = oy_ref.shape[0]
    offs = lax.broadcasted_iota(jnp.int32, (32, LANES), 0).astype(jnp.float32) - 15.0
    lane = lax.broadcasted_iota(jnp.int32, (1, LANES), 1)
    ys, metas, weights = [], [], []
    for j in range(own):
        y = band_ref[j].astype(jnp.float32) + oy_ref[j : j + 1, :]
        x = ox_ref[j : j + 1, :]
        c = own_coefs(psf_ref, cell_ref, j)
        rows = profile3(jnp.floor(y) + offs - y)
        cols = profile3(jnp.floor(x) + offs - x)
        gram_r = [[jnp.sum(rows[a] * rows[b], axis=0, keepdims=True) for b in range(3)] for a in range(3)]
        gram_c = [[jnp.sum(cols[a] * cols[b], axis=0, keepdims=True) for b in range(3)] for a in range(3)]
        weight = None
        for a in range(3):
            for cc in range(3):
                inner = None
                for b in range(3):
                    for d in range(3):
                        term = (c[3 * a + b] * c[3 * cc + d]) * gram_c[b][d]
                        inner = term if inner is None else inner + term
                term = gram_r[a][cc] * inner
                weight = term if weight is None else weight + term
        w_ref[j : j + 1, :] = weight
        meta = jnp.zeros((1, LANES), jnp.float32)
        for k in range(9):
            meta = jnp.where(lane == k, c[k], meta)
        meta = jnp.where(lane == 9, col_ref[j].astype(jnp.float32), meta)
        ys.append(y)
        metas.append(meta)
        weights.append(weight)
    top_first = band_ref[0] <= band_ref[1]

    def pick(first, second):
        return jnp.where(top_first, first, second), jnp.where(top_first, second, first)

    tops, bots = zip(*[
        pick(*pair) for pair in (
            (ys[0], ys[1]), (ox_ref[0:1, :], ox_ref[1:2, :]), (f_ref[0:1, :], f_ref[1:2, :]),
            (weights[0], weights[1]), (metas[0], metas[1]),
        )
    ])
    even = even_device()
    first_ref, second_ref = up_ref, down_ref
    first_ref[...] = jnp.zeros_like(first_ref)
    second_ref[...] = jnp.zeros_like(second_ref)
    for r in range(5):
        first_ref[r : r + 1, :] = jnp.where(even, bots[r], tops[r])
        second_ref[r : r + 1, :] = jnp.where(even, tops[r], bots[r])


def phase_kernel(
    final, first,
    band_ref, col_ref, cell_ref, psf_ref, xs1_ref, xs2_ref,
    oy_ref, ox_ref, w_ref, x1_ref, x2_ref, img_ref, f_ref, l_ref, q1_ref, q2_ref,
    *rest,
):
    even = even_device()

    def above(ref1, ref2, row):
        return jnp.where(even, ref2[row : row + 1, :], ref1[row : row + 1, :])

    def below(ref1, ref2, row):
        return jnp.where(even, ref1[row : row + 1, :], ref2[row : row + 1, :])

    if final:
        out_ref, fluxout_ref, canvas = rest
    else:
        fout_ref, lout_ref, up_ref, down_ref, canvas = rest
    rows_n, pad_width = canvas.shape
    strip_rows, width = img_ref.shape
    own = oy_ref.shape[0]
    top_first = band_ref[0] <= band_ref[1]

    if first:
        fluxes = [f_ref[0:1, :], f_ref[1:2, :], above(x1_ref, x2_ref, 2), below(x1_ref, x2_ref, 2)]
    else:
        weights = [w_ref[0:1, :], w_ref[1:2, :], above(x1_ref, x2_ref, 3), below(x1_ref, x2_ref, 3)]
        from_above = above(q1_ref, q2_ref, 0)
        from_below = below(q1_ref, q2_ref, 0)
        extra = [
            jnp.where(top_first, from_above, from_below),
            jnp.where(top_first, from_below, from_above),
            above(q1_ref, q2_ref, 1),
            below(q1_ref, q2_ref, 1),
        ]
        fluxes = []
        for j in range(own + 2):
            grad = l_ref[j : j + 1, :] + extra[j]
            safe = jnp.where(weights[j] == 0.0, 1.0, weights[j])
            fluxes.append(f_ref[j : j + 1, :] + 0.5 * grad / safe)

    specs = []
    for j in range(own):
        y = band_ref[j].astype(jnp.float32) + oy_ref[j : j + 1, :]
        specs.append((y, ox_ref[j : j + 1, :], own_coefs(psf_ref, cell_ref, j), col_ref[j], None))
    specs.append((
        above(x1_ref, x2_ref, 0) - strip_rows, above(x1_ref, x2_ref, 1),
        [jnp.where(even, xs2_ref[4, k], xs1_ref[4, k]) for k in range(9)],
        jnp.where(even, xs2_ref[4, 9], xs1_ref[4, 9]).astype(jnp.int32), REACH,
    ))
    specs.append((
        below(x1_ref, x2_ref, 0) + strip_rows, below(x1_ref, x2_ref, 1),
        [jnp.where(even, xs1_ref[4, k], xs2_ref[4, k]) for k in range(9)],
        jnp.where(even, xs1_ref[4, 9], xs2_ref[4, 9]).astype(jnp.int32), None,
    ))

    canvas[...] = jnp.zeros_like(canvas)
    hpos = lax.broadcasted_iota(jnp.int32, (rows_n, LANES), 0).astype(jnp.float32)
    wpos = lax.broadcasted_iota(jnp.int32, (SPAN, LANES), 0).astype(jnp.float32) - LANES // 2
    spare = jnp.zeros((rows_n, WIN - SPAN), jnp.float32)
    saved = []
    for j, (y, x, c, col, keep) in enumerate(specs):
        rows = profile3(hpos - y)
        if keep is not None:
            rows = tuple(jnp.where(hpos < keep, r, 0.0) for r in rows)
        cols_hi, cols_lo = split_bf16(jnp.concatenate(profile3(wpos - x), axis=1))
        mixed = [
            (c[b] * rows[0] + c[3 + b] * rows[1] + c[6 + b] * rows[2]) * fluxes[j]
            for b in range(3)
        ]
        stamp = presplit_dot(jnp.concatenate(mixed, axis=1), cols_hi, cols_lo, DIMS_NT)
        start = pl.multiple_of(col * LANES, LANES)
        canvas[:, pl.ds(start, WIN)] += pltpu.roll(
            jnp.concatenate([stamp, spare], axis=1), LANES // 2, 1
        )
        saved.append((rows, cols_hi, cols_lo, c, start))
    inner = slice(LANES, LANES + width)
    if final:
        out_ref[...] = img_ref[...] - canvas[:, inner]
        for j in range(own):
            fluxout_ref[j : j + 1, :] = fluxes[j]
        return
    canvas[:, inner] = img_ref[...] - canvas[:, inner]
    canvas[:, 0:LANES] = jnp.zeros((rows_n, LANES), jnp.float32)
    canvas[:, LANES + width :] = jnp.zeros((rows_n, pad_width - LANES - width), jnp.float32)
    fout_ref[...] = jnp.zeros_like(fout_ref)
    lout_ref[...] = jnp.zeros_like(lout_ref)
    partial = []
    for j, (rows, cols_hi, cols_lo, c, start) in enumerate(saved):
        window = pltpu.roll(canvas[:, pl.ds(start, WIN)], WIN - LANES // 2, 1)[:, :SPAN]
        across_all = presplit_dot(window, cols_hi, cols_lo, DIMS_NN)
        grad = None
        for a in range(3):
            for b in range(3):
                paired = jnp.sum(rows[a] * across_all[:, b * LANES : (b + 1) * LANES], axis=0,
                                 keepdims=True)
                term = c[3 * a + b] * paired
                grad = term if grad is None else grad + term
        partial.append(grad)
        fout_ref[j : j + 1, :] = fluxes[j]
        lout_ref[j : j + 1, :] = grad
    top_part = jnp.where(top_first, partial[0], partial[1])
    bot_part = jnp.where(top_first, partial[1], partial[0])
    first_ref, second_ref = up_ref, down_ref
    first_ref[0:1, :] = jnp.where(even, partial[own + 1], partial[own])
    first_ref[1:2, :] = jnp.where(even, bot_part, top_part)
    second_ref[0:1, :] = jnp.where(even, partial[own], partial[own + 1])
    second_ref[1:2, :] = jnp.where(even, top_part, bot_part)


def vmem_operands(*arrays):
    return [pltpu.with_memory_space_constraint(a, pltpu.VMEM) for a in arrays]


def local(image, band_row, col_block, cell_index, offset_y, offset_x, flux_start, psf_coef):
    strip_rows, strip_width = image.shape
    own = band_row.shape[0]
    f32 = jnp.float32
    smem = pl.BlockSpec(memory_space=pltpu.SMEM)
    vmem = pl.BlockSpec(memory_space=pltpu.VMEM)
    packet = pltpu.VMEM((SLOTS, LANES), f32)
    send_within, send_across, weight = pl.pallas_call(
        setup_kernel,
        out_shape=(packet, packet, pltpu.VMEM((own, LANES), f32)),
        in_specs=[smem] * 4 + [vmem] * 3,
        out_specs=(vmem, vmem, vmem),
    )(band_row, col_block, cell_index, psf_coef, offset_y, offset_x, flux_start)
    got_within, got_across = exchange(send_within, send_across)

    blocks = own + 2
    flops = 2 * 3 * 2 * strip_rows * WIN * 3 * LANES * blocks
    state_shape = pltpu.VMEM((SLOTS, LANES), f32)
    part_shape = pltpu.VMEM((2, LANES), f32)
    common = (band_row, col_block, cell_index, psf_coef, got_within, got_across,
              *vmem_operands(offset_y, offset_x, weight, got_within, got_across, image))

    def phase(final, first, fluxes, partials, swap_within, swap_across):
        kernel = functools.partial(phase_kernel, final, first)
        if final:
            out_shape = (jax.ShapeDtypeStruct((strip_rows, strip_width), f32),
                         jax.ShapeDtypeStruct((own, LANES), f32))
            out_specs = (vmem, vmem)
        else:
            out_shape = (state_shape, state_shape, part_shape, part_shape)
            out_specs = (vmem, vmem, vmem, vmem)
        return pl.pallas_call(
            kernel,
            out_shape=out_shape,
            in_specs=[smem] * 6 + [vmem] * 10,
            out_specs=out_specs,
            scratch_shapes=[pltpu.VMEM((strip_rows, strip_width + 2 * LANES), f32)],
            cost_estimate=pl.CostEstimate(
                flops=flops, transcendentals=blocks * 2 * (strip_rows + WIN) * LANES,
                bytes_accessed=4 * strip_rows * strip_width * 2,
            ),
        )(*common, *vmem_operands(fluxes, partials, swap_within, swap_across))

    state, partials, within, across = phase(False, True, flux_start, flux_start, flux_start, flux_start)
    for iteration in range(1, ITERS):
        swap_within, swap_across = exchange(within, across)
        state, partials, within, across = phase(False, False, state, partials, swap_within, swap_across)
    swap_within, swap_across = exchange(within, across)
    residual, fluxes = phase(True, False, state, partials, swap_within, swap_across)
    return (fluxes, residual)


def solution(mesh):
    return jax.shard_map(
        local,
        mesh=mesh,
        in_specs=(
            P(("groups", "ty"), None),
            P(("groups", "ty")),
            P(("groups", "ty")),
            P(("groups", "ty")),
            P(("groups", "ty"), None),
            P(("groups", "ty"), None),
            P(("groups", "ty"), None),
            P(),
        ),
        out_specs=(P(("groups", "ty"), None), P(("groups", "ty"), None)),
        check_vma=False,
    )
```

```python
import functools

import jax
import jax.numpy as jnp
from jax import lax
from jax.experimental import pallas as pl
from jax.experimental.pallas import tpu as pltpu
from jax.sharding import PartitionSpec as P

REACH = 15
ITERS = 2
LANES = 128
WIN = 384
SPAN = 256
SLOTS = 8

DIMS_NT = (((1,), (1,)), ((), ()))
DIMS_NN = (((1,), (0,)), ((), ()))


def profile3(dist):
    tapered_arg = dist * (1.0 / 15.5)
    tapered = jnp.maximum(0.0, 1.0 - tapered_arg * tapered_arg)
    scaled = dist * (1.0 / 1.7)
    core_part = jnp.exp(-0.5 * scaled * scaled) * tapered
    wing_part = jnp.exp(dist * dist * (-1.0 / 72.0)) * tapered
    return core_part, scaled * core_part, wing_part


def split_dot(lhs, rhs, dims):
    lhs_hi = lhs.astype(jnp.bfloat16)
    lhs_lo = (lhs - lhs_hi.astype(jnp.float32)).astype(jnp.bfloat16)
    rhs_hi = rhs.astype(jnp.bfloat16)
    rhs_lo = (rhs - rhs_hi.astype(jnp.float32)).astype(jnp.bfloat16)

    def one(a, b):
        return lax.dot_general(a, b, dims, preferred_element_type=jnp.float32)

    return one(lhs_hi, rhs_hi) + (one(lhs_hi, rhs_lo) + one(lhs_lo, rhs_hi))


def split_bf16(value):
    hi = value.astype(jnp.bfloat16)
    return hi, (value - hi.astype(jnp.float32)).astype(jnp.bfloat16)


def presplit_dot(lhs, rhs_hi, rhs_lo, dims):
    lhs_hi, lhs_lo = split_bf16(lhs)

    def one(a, b):
        return lax.dot_general(a, b, dims, preferred_element_type=jnp.float32)

    return one(lhs_hi, rhs_hi) + (one(lhs_hi, rhs_lo) + one(lhs_lo, rhs_hi))


def exchange(first, second):
    count = lax.axis_size("ty")
    within = [(i, i ^ 1) for i in range(count) if (i ^ 1) < count]
    across = [(i, i + 1) for i in range(1, count - 1, 2)] + [
        (i + 1, i) for i in range(1, count - 1, 2)
    ]
    return lax.ppermute(first, "ty", within), lax.ppermute(second, "ty", across)


def even_device():
    return lax.axis_index("ty") % 2 == 0


def own_coefs(psf_ref, cell_ref, j):
    cell = cell_ref[j]
    return [psf_ref[k, cell] for k in range(9)]


def setup_kernel(band_ref, col_ref, cell_ref, psf_ref, oy_ref, ox_ref, f_ref, up_ref, down_ref, w_ref):
    own = oy_ref.shape[0]
    offs = lax.broadcasted_iota(jnp.int32, (32, LANES), 0).astype(jnp.float32) - 15.0
    lane = lax.broadcasted_iota(jnp.int32, (1, LANES), 1)
    ys, metas, weights = [], [], []
    for j in range(own):
        y = band_ref[j].astype(jnp.float32) + oy_ref[j : j + 1, :]
        x = ox_ref[j : j + 1, :]
        c = own_coefs(psf_ref, cell_ref, j)
        rows = profile3(jnp.floor(y) + offs - y)
        cols = profile3(jnp.floor(x) + offs - x)
        gram_r = [[jnp.sum(rows[a] * rows[b], axis=0, keepdims=True) for b in range(3)] for a in range(3)]
        gram_c = [[jnp.sum(cols[a] * cols[b], axis=0, keepdims=True) for b in range(3)] for a in range(3)]
        weight = None
        for a in range(3):
            for cc in range(3):
                inner = None
                for b in range(3):
                    for d in range(3):
                        term = (c[3 * a + b] * c[3 * cc + d]) * gram_c[b][d]
                        inner = term if inner is None else inner + term
                term = gram_r[a][cc] * inner
                weight = term if weight is None else weight + term
        w_ref[j : j + 1, :] = weight
        meta = jnp.zeros((1, LANES), jnp.float32)
        for k in range(9):
            meta = jnp.where(lane == k, c[k], meta)
        meta = jnp.where(lane == 9, col_ref[j].astype(jnp.float32), meta)
        ys.append(y)
        metas.append(meta)
        weights.append(weight)
    top_first = band_ref[0] <= band_ref[1]

    def pick(first, second):
        return jnp.where(top_first, first, second), jnp.where(top_first, second, first)

    tops, bots = zip(*[
        pick(*pair) for pair in (
            (ys[0], ys[1]), (ox_ref[0:1, :], ox_ref[1:2, :]), (f_ref[0:1, :], f_ref[1:2, :]),
            (weights[0], weights[1]), (metas[0], metas[1]),
        )
    ])
    even = even_device()
    first_ref, second_ref = up_ref, down_ref
    first_ref[...] = jnp.zeros_like(first_ref)
    second_ref[...] = jnp.zeros_like(second_ref)
    for r in range(5):
        first_ref[r : r + 1, :] = jnp.where(even, bots[r], tops[r])
        second_ref[r : r + 1, :] = jnp.where(even, tops[r], bots[r])


def phase_kernel(
    final, first,
    band_ref, col_ref, cell_ref, psf_ref, xs1_ref, xs2_ref,
    oy_ref, ox_ref, w_ref, x1_ref, x2_ref, img_ref, f_ref, l_ref, q1_ref, q2_ref,
    *rest,
):
    even = even_device()

    def above(ref1, ref2, row):
        return jnp.where(even, ref2[row : row + 1, :], ref1[row : row + 1, :])

    def below(ref1, ref2, row):
        return jnp.where(even, ref1[row : row + 1, :], ref2[row : row + 1, :])

    if final:
        out_ref, fluxout_ref, canvas = rest
    else:
        fout_ref, lout_ref, up_ref, down_ref, canvas = rest
    rows_n, pad_width = canvas.shape
    strip_rows, width = img_ref.shape
    own = oy_ref.shape[0]
    top_first = band_ref[0] <= band_ref[1]

    if first:
        fluxes = [f_ref[0:1, :], f_ref[1:2, :], above(x1_ref, x2_ref, 2), below(x1_ref, x2_ref, 2)]
    else:
        weights = [w_ref[0:1, :], w_ref[1:2, :], above(x1_ref, x2_ref, 3), below(x1_ref, x2_ref, 3)]
        from_above = above(q1_ref, q2_ref, 0)
        from_below = below(q1_ref, q2_ref, 0)
        extra = [
            jnp.where(top_first, from_above, from_below),
            jnp.where(top_first, from_below, from_above),
            above(q1_ref, q2_ref, 1),
            below(q1_ref, q2_ref, 1),
        ]
        fluxes = []
        for j in range(own + 2):
            grad = l_ref[j : j + 1, :] + extra[j]
            safe = jnp.where(weights[j] == 0.0, 1.0, weights[j])
            fluxes.append(f_ref[j : j + 1, :] + 0.5 * grad / safe)

    specs = []
    for j in range(own):
        y = band_ref[j].astype(jnp.float32) + oy_ref[j : j + 1, :]
        specs.append((y, ox_ref[j : j + 1, :], own_coefs(psf_ref, cell_ref, j), col_ref[j], None))
    specs.append((
        above(x1_ref, x2_ref, 0) - strip_rows, above(x1_ref, x2_ref, 1),
        [jnp.where(even, xs2_ref[4, k], xs1_ref[4, k]) for k in range(9)],
        jnp.where(even, xs2_ref[4, 9], xs1_ref[4, 9]).astype(jnp.int32), REACH,
    ))
    specs.append((
        below(x1_ref, x2_ref, 0) + strip_rows, below(x1_ref, x2_ref, 1),
        [jnp.where(even, xs1_ref[4, k], xs2_ref[4, k]) for k in range(9)],
        jnp.where(even, xs1_ref[4, 9], xs2_ref[4, 9]).astype(jnp.int32), None,
    ))

    canvas[...] = jnp.zeros_like(canvas)
    hpos = lax.broadcasted_iota(jnp.int32, (rows_n, LANES), 0).astype(jnp.float32)
    wpos = lax.broadcasted_iota(jnp.int32, (SPAN, LANES), 0).astype(jnp.float32) - LANES // 2
    spare = jnp.zeros((rows_n, WIN - SPAN), jnp.float32)
    saved = []
    bands = [(0, rows_n)] * own + [(0, 16), (rows_n - 16, 16)]
    for j, (y, x, c, col, keep) in enumerate(specs):
        row0, count = bands[j]
        rpos = hpos[row0 : row0 + count]
        rows = profile3(rpos - y)
        if keep is not None:
            rows = tuple(jnp.where(rpos < keep, r, 0.0) for r in rows)
        cols_hi, cols_lo = split_bf16(jnp.concatenate(profile3(wpos - x), axis=1))
        mixed = [
            (c[b] * rows[0] + c[3 + b] * rows[1] + c[6 + b] * rows[2]) * fluxes[j]
            for b in range(3)
        ]
        stamp = presplit_dot(jnp.concatenate(mixed, axis=1), cols_hi, cols_lo, DIMS_NT)
        start = pl.multiple_of(col * LANES, LANES)
        canvas[row0 : row0 + count, pl.ds(start, WIN)] += pltpu.roll(
            jnp.concatenate([stamp, spare[:count]], axis=1), LANES // 2, 1
        )
        saved.append((rows, cols_hi, cols_lo, c, start, row0, count))
    inner = slice(LANES, LANES + width)
    if final:
        out_ref[...] = img_ref[...] - canvas[:, inner]
        for j in range(own):
            fluxout_ref[j : j + 1, :] = fluxes[j]
        return
    canvas[:, inner] = img_ref[...] - canvas[:, inner]
    canvas[:, 0:LANES] = jnp.zeros((rows_n, LANES), jnp.float32)
    canvas[:, LANES + width :] = jnp.zeros((rows_n, pad_width - LANES - width), jnp.float32)
    fout_ref[...] = jnp.zeros_like(fout_ref)
    lout_ref[...] = jnp.zeros_like(lout_ref)
    partial = []
    for j, (rows, cols_hi, cols_lo, c, start, row0, count) in enumerate(saved):
        window = pltpu.roll(
            canvas[row0 : row0 + count, pl.ds(start, WIN)], WIN - LANES // 2, 1
        )[:, :SPAN]
        across_all = presplit_dot(window, cols_hi, cols_lo, DIMS_NN)
        grad = None
        for a in range(3):
            for b in range(3):
                paired = jnp.sum(rows[a] * across_all[:, b * LANES : (b + 1) * LANES], axis=0,
                                 keepdims=True)
                term = c[3 * a + b] * paired
                grad = term if grad is None else grad + term
        partial.append(grad)
        fout_ref[j : j + 1, :] = fluxes[j]
        lout_ref[j : j + 1, :] = grad
    top_part = jnp.where(top_first, partial[0], partial[1])
    bot_part = jnp.where(top_first, partial[1], partial[0])
    first_ref, second_ref = up_ref, down_ref
    first_ref[0:1, :] = jnp.where(even, partial[own + 1], partial[own])
    first_ref[1:2, :] = jnp.where(even, bot_part, top_part)
    second_ref[0:1, :] = jnp.where(even, partial[own], partial[own + 1])
    second_ref[1:2, :] = jnp.where(even, top_part, bot_part)


def vmem_operands(*arrays):
    return [pltpu.with_memory_space_constraint(a, pltpu.VMEM) for a in arrays]


def local(image, band_row, col_block, cell_index, offset_y, offset_x, flux_start, psf_coef):
    strip_rows, strip_width = image.shape
    own = band_row.shape[0]
    f32 = jnp.float32
    smem = pl.BlockSpec(memory_space=pltpu.SMEM)
    vmem = pl.BlockSpec(memory_space=pltpu.VMEM)
    packet = pltpu.VMEM((SLOTS, LANES), f32)
    send_within, send_across, weight = pl.pallas_call(
        setup_kernel,
        out_shape=(packet, packet, pltpu.VMEM((own, LANES), f32)),
        in_specs=[smem] * 4 + [vmem] * 3,
        out_specs=(vmem, vmem, vmem),
    )(band_row, col_block, cell_index, psf_coef, offset_y, offset_x, flux_start)
    got_within, got_across = exchange(send_within, send_across)

    blocks = own + 2
    flops = 2 * 3 * 2 * strip_rows * WIN * 3 * LANES * blocks
    state_shape = pltpu.VMEM((SLOTS, LANES), f32)
    part_shape = pltpu.VMEM((2, LANES), f32)
    common = (band_row, col_block, cell_index, psf_coef, got_within, got_across,
              *vmem_operands(offset_y, offset_x, weight, got_within, got_across), image)

    def phase(final, first, fluxes, partials, swap_within, swap_across):
        kernel = functools.partial(phase_kernel, final, first)
        if final:
            out_shape = (jax.ShapeDtypeStruct((strip_rows, strip_width), f32),
                         jax.ShapeDtypeStruct((own, LANES), f32))
            out_specs = (vmem, vmem)
        else:
            out_shape = (state_shape, state_shape, part_shape, part_shape)
            out_specs = (vmem, vmem, vmem, vmem)
        return pl.pallas_call(
            kernel,
            out_shape=out_shape,
            in_specs=[smem] * 6 + [vmem] * 10,
            out_specs=out_specs,
            scratch_shapes=[pltpu.VMEM((strip_rows, strip_width + 2 * LANES), f32)],
            cost_estimate=pl.CostEstimate(
                flops=flops, transcendentals=blocks * 2 * (strip_rows + WIN) * LANES,
                bytes_accessed=4 * strip_rows * strip_width * 2,
            ),
        )(*common, *vmem_operands(fluxes, partials, swap_within, swap_across))

    state, partials, within, across = phase(False, True, flux_start, flux_start, flux_start, flux_start)
    for iteration in range(1, ITERS):
        swap_within, swap_across = exchange(within, across)
        state, partials, within, across = phase(False, False, state, partials, swap_within, swap_across)
    swap_within, swap_across = exchange(within, across)
    residual, fluxes = phase(True, False, state, partials, swap_within, swap_across)
    return (fluxes, residual)


def solution(mesh):
    return jax.shard_map(
        local,
        mesh=mesh,
        in_specs=(
            P(("groups", "ty"), None),
            P(("groups", "ty")),
            P(("groups", "ty")),
            P(("groups", "ty")),
            P(("groups", "ty"), None),
            P(("groups", "ty"), None),
            P(("groups", "ty"), None),
            P(),
        ),
        out_specs=(P(("groups", "ty"), None), P(("groups", "ty"), None)),
        check_vma=False,
    )
```

```python
import functools

import jax
import jax.numpy as jnp
from jax import lax
from jax.experimental import pallas as pl
from jax.experimental.pallas import tpu as pltpu
from jax.sharding import PartitionSpec as P

REACH = 15
ITERS = 2
LANES = 128
WIN = 384
SPAN = 256
SLOTS = 8

DIMS_NT = (((1,), (1,)), ((), ()))
DIMS_NN = (((1,), (0,)), ((), ()))


def profile3(dist):
    tapered_arg = dist * (1.0 / 15.5)
    tapered = jnp.maximum(0.0, 1.0 - tapered_arg * tapered_arg)
    scaled = dist * (1.0 / 1.7)
    core_part = jnp.exp(-0.5 * scaled * scaled) * tapered
    wing_part = jnp.exp(dist * dist * (-1.0 / 72.0)) * tapered
    return core_part, scaled * core_part, wing_part


def split_dot(lhs, rhs, dims):
    lhs_hi = lhs.astype(jnp.bfloat16)
    lhs_lo = (lhs - lhs_hi.astype(jnp.float32)).astype(jnp.bfloat16)
    rhs_hi = rhs.astype(jnp.bfloat16)
    rhs_lo = (rhs - rhs_hi.astype(jnp.float32)).astype(jnp.bfloat16)

    def one(a, b):
        return lax.dot_general(a, b, dims, preferred_element_type=jnp.float32)

    return one(lhs_hi, rhs_hi) + (one(lhs_hi, rhs_lo) + one(lhs_lo, rhs_hi))


def split_bf16(value):
    hi = value.astype(jnp.bfloat16)
    return hi, (value - hi.astype(jnp.float32)).astype(jnp.bfloat16)


def presplit_dot(lhs, rhs_hi, rhs_lo, dims):
    lhs_hi, lhs_lo = split_bf16(lhs)

    def one(a, b):
        return lax.dot_general(a, b, dims, preferred_element_type=jnp.float32)

    return one(lhs_hi, rhs_hi) + (one(lhs_hi, rhs_lo) + one(lhs_lo, rhs_hi))


def exchange(first, second):
    count = lax.axis_size("ty")
    within = [(i, i ^ 1) for i in range(count) if (i ^ 1) < count]
    across = [(i, i + 1) for i in range(1, count - 1, 2)] + [
        (i + 1, i) for i in range(1, count - 1, 2)
    ]
    return lax.ppermute(first, "ty", within), lax.ppermute(second, "ty", across)


def even_device():
    return lax.axis_index("ty") % 2 == 0


def own_coefs(psf_ref, cell_ref, j):
    cell = cell_ref[j]
    return [psf_ref[k, cell] for k in range(9)]


def setup_kernel(band_ref, col_ref, cell_ref, psf_ref, oy_ref, ox_ref, f_ref, up_ref, down_ref, w_ref):
    own = oy_ref.shape[0]
    offs = lax.broadcasted_iota(jnp.int32, (32, LANES), 0).astype(jnp.float32) - 15.0
    lane = lax.broadcasted_iota(jnp.int32, (1, LANES), 1)
    ys, metas, weights = [], [], []
    for j in range(own):
        y = band_ref[j].astype(jnp.float32) + oy_ref[j : j + 1, :]
        x = ox_ref[j : j + 1, :]
        c = own_coefs(psf_ref, cell_ref, j)
        rows = profile3(jnp.floor(y) + offs - y)
        cols = profile3(jnp.floor(x) + offs - x)
        gram_r = [[jnp.sum(rows[a] * rows[b], axis=0, keepdims=True) for b in range(3)] for a in range(3)]
        gram_c = [[jnp.sum(cols[a] * cols[b], axis=0, keepdims=True) for b in range(3)] for a in range(3)]
        weight = None
        for a in range(3):
            for cc in range(3):
                inner = None
                for b in range(3):
                    for d in range(3):
                        term = (c[3 * a + b] * c[3 * cc + d]) * gram_c[b][d]
                        inner = term if inner is None else inner + term
                term = gram_r[a][cc] * inner
                weight = term if weight is None else weight + term
        w_ref[j : j + 1, :] = weight
        meta = jnp.zeros((1, LANES), jnp.float32)
        for k in range(9):
            meta = jnp.where(lane == k, c[k], meta)
        meta = jnp.where(lane == 9, col_ref[j].astype(jnp.float32), meta)
        ys.append(y)
        metas.append(meta)
        weights.append(weight)
    top_first = band_ref[0] <= band_ref[1]

    def pick(first, second):
        return jnp.where(top_first, first, second), jnp.where(top_first, second, first)

    tops, bots = zip(*[
        pick(*pair) for pair in (
            (ys[0], ys[1]), (ox_ref[0:1, :], ox_ref[1:2, :]), (f_ref[0:1, :], f_ref[1:2, :]),
            (weights[0], weights[1]), (metas[0], metas[1]),
        )
    ])
    even = even_device()
    first_ref, second_ref = up_ref, down_ref
    first_ref[...] = jnp.zeros_like(first_ref)
    second_ref[...] = jnp.zeros_like(second_ref)
    for r in range(5):
        first_ref[r : r + 1, :] = jnp.where(even, bots[r], tops[r])
        second_ref[r : r + 1, :] = jnp.where(even, tops[r], bots[r])


def phase_kernel(
    final, first,
    band_ref, col_ref, cell_ref, psf_ref, xs1_ref, xs2_ref,
    oy_ref, ox_ref, w_ref, x1_ref, x2_ref, img_ref, f_ref, l_ref, q1_ref, q2_ref,
    *rest,
):
    even = even_device()

    def above(ref1, ref2, row):
        return jnp.where(even, ref2[row : row + 1, :], ref1[row : row + 1, :])

    def below(ref1, ref2, row):
        return jnp.where(even, ref1[row : row + 1, :], ref2[row : row + 1, :])

    if final:
        out_ref, fluxout_ref, canvas = rest
    else:
        fout_ref, lout_ref, up_ref, down_ref, canvas = rest
    rows_n, pad_width = canvas.shape
    strip_rows, width = img_ref.shape
    own = oy_ref.shape[0]
    top_first = band_ref[0] <= band_ref[1]

    if first:
        fluxes = [f_ref[0:1, :], f_ref[1:2, :], above(x1_ref, x2_ref, 2), below(x1_ref, x2_ref, 2)]
    else:
        weights = [w_ref[0:1, :], w_ref[1:2, :], above(x1_ref, x2_ref, 3), below(x1_ref, x2_ref, 3)]
        from_above = above(q1_ref, q2_ref, 0)
        from_below = below(q1_ref, q2_ref, 0)
        extra = [
            jnp.where(top_first, from_above, from_below),
            jnp.where(top_first, from_below, from_above),
            above(q1_ref, q2_ref, 1),
            below(q1_ref, q2_ref, 1),
        ]
        fluxes = []
        for j in range(own + 2):
            grad = l_ref[j : j + 1, :] + extra[j]
            safe = jnp.where(weights[j] == 0.0, 1.0, weights[j])
            fluxes.append(f_ref[j : j + 1, :] + 0.5 * grad / safe)

    specs = []
    for j in range(own):
        y = band_ref[j].astype(jnp.float32) + oy_ref[j : j + 1, :]
        specs.append((y, ox_ref[j : j + 1, :], own_coefs(psf_ref, cell_ref, j), col_ref[j], None))
    specs.append((
        above(x1_ref, x2_ref, 0) - strip_rows, above(x1_ref, x2_ref, 1),
        [jnp.where(even, xs2_ref[4, k], xs1_ref[4, k]) for k in range(9)],
        jnp.where(even, xs2_ref[4, 9], xs1_ref[4, 9]).astype(jnp.int32), REACH,
    ))
    specs.append((
        below(x1_ref, x2_ref, 0) + strip_rows, below(x1_ref, x2_ref, 1),
        [jnp.where(even, xs1_ref[4, k], xs2_ref[4, k]) for k in range(9)],
        jnp.where(even, xs1_ref[4, 9], xs2_ref[4, 9]).astype(jnp.int32), None,
    ))

    canvas[...] = jnp.zeros_like(canvas)
    hpos = lax.broadcasted_iota(jnp.int32, (rows_n, LANES), 0).astype(jnp.float32)
    wpos = lax.broadcasted_iota(jnp.int32, (SPAN, LANES), 0).astype(jnp.float32) - LANES // 2
    spare = jnp.zeros((rows_n, WIN - SPAN), jnp.float32)
    saved = []
    reach_rows = rows_n - 16
    bands = [(pl.multiple_of(band_ref[j] // 2, 8), reach_rows) for j in range(own)]
    bands += [(0, 16), (rows_n - 16, 16)]
    for j, (y, x, c, col, keep) in enumerate(specs):
        row0, count = bands[j]
        rpos = hpos[:count] + (row0 if j >= own else row0.astype(jnp.float32))
        rows = profile3(rpos - y)
        if keep is not None:
            rows = tuple(jnp.where(rpos < keep, r, 0.0) for r in rows)
        cols_hi, cols_lo = split_bf16(jnp.concatenate(profile3(wpos - x), axis=1))
        mixed = [
            (c[b] * rows[0] + c[3 + b] * rows[1] + c[6 + b] * rows[2]) * fluxes[j]
            for b in range(3)
        ]
        stamp = presplit_dot(jnp.concatenate(mixed, axis=1), cols_hi, cols_lo, DIMS_NT)
        start = pl.multiple_of(col * LANES, LANES)
        canvas[pl.ds(row0, count), pl.ds(start, WIN)] += pltpu.roll(
            jnp.concatenate([stamp, spare[:count]], axis=1), LANES // 2, 1
        )
        saved.append((rows, cols_hi, cols_lo, c, start, row0, count))
    inner = slice(LANES, LANES + width)
    if final:
        out_ref[...] = img_ref[...] - canvas[:, inner]
        for j in range(own):
            fluxout_ref[j : j + 1, :] = fluxes[j]
        return
    canvas[:, inner] = img_ref[...] - canvas[:, inner]
    canvas[:, 0:LANES] = jnp.zeros((rows_n, LANES), jnp.float32)
    canvas[:, LANES + width :] = jnp.zeros((rows_n, pad_width - LANES - width), jnp.float32)
    fout_ref[...] = jnp.zeros_like(fout_ref)
    lout_ref[...] = jnp.zeros_like(lout_ref)
    partial = []
    for j, (rows, cols_hi, cols_lo, c, start, row0, count) in enumerate(saved):
        window = pltpu.roll(
            canvas[pl.ds(row0, count), pl.ds(start, WIN)], WIN - LANES // 2, 1
        )[:, :SPAN]
        across_all = presplit_dot(window, cols_hi, cols_lo, DIMS_NN)
        grad = None
        for a in range(3):
            for b in range(3):
                paired = jnp.sum(rows[a] * across_all[:, b * LANES : (b + 1) * LANES], axis=0,
                                 keepdims=True)
                term = c[3 * a + b] * paired
                grad = term if grad is None else grad + term
        partial.append(grad)
        fout_ref[j : j + 1, :] = fluxes[j]
        lout_ref[j : j + 1, :] = grad
    top_part = jnp.where(top_first, partial[0], partial[1])
    bot_part = jnp.where(top_first, partial[1], partial[0])
    first_ref, second_ref = up_ref, down_ref
    first_ref[0:1, :] = jnp.where(even, partial[own + 1], partial[own])
    first_ref[1:2, :] = jnp.where(even, bot_part, top_part)
    second_ref[0:1, :] = jnp.where(even, partial[own], partial[own + 1])
    second_ref[1:2, :] = jnp.where(even, top_part, bot_part)


def vmem_operands(*arrays):
    return [pltpu.with_memory_space_constraint(a, pltpu.VMEM) for a in arrays]


def local(image, band_row, col_block, cell_index, offset_y, offset_x, flux_start, psf_coef):
    strip_rows, strip_width = image.shape
    own = band_row.shape[0]
    f32 = jnp.float32
    smem = pl.BlockSpec(memory_space=pltpu.SMEM)
    vmem = pl.BlockSpec(memory_space=pltpu.VMEM)
    packet = pltpu.VMEM((SLOTS, LANES), f32)
    send_within, send_across, weight = pl.pallas_call(
        setup_kernel,
        out_shape=(packet, packet, pltpu.VMEM((own, LANES), f32)),
        in_specs=[smem] * 4 + [vmem] * 3,
        out_specs=(vmem, vmem, vmem),
    )(band_row, col_block, cell_index, psf_coef, offset_y, offset_x, flux_start)
    got_within, got_across = exchange(send_within, send_across)

    blocks = own + 2
    flops = 2 * 3 * 2 * strip_rows * WIN * 3 * LANES * blocks
    state_shape = pltpu.VMEM((SLOTS, LANES), f32)
    part_shape = pltpu.VMEM((2, LANES), f32)
    common = (band_row, col_block, cell_index, psf_coef, got_within, got_across,
              *vmem_operands(offset_y, offset_x, weight, got_within, got_across), image)

    def phase(final, first, fluxes, partials, swap_within, swap_across):
        kernel = functools.partial(phase_kernel, final, first)
        if final:
            out_shape = (jax.ShapeDtypeStruct((strip_rows, strip_width), f32),
                         jax.ShapeDtypeStruct((own, LANES), f32))
            out_specs = (vmem, vmem)
        else:
            out_shape = (state_shape, state_shape, part_shape, part_shape)
            out_specs = (vmem, vmem, vmem, vmem)
        return pl.pallas_call(
            kernel,
            out_shape=out_shape,
            in_specs=[smem] * 6 + [vmem] * 10,
            out_specs=out_specs,
            scratch_shapes=[pltpu.VMEM((strip_rows, strip_width + 2 * LANES), f32)],
            cost_estimate=pl.CostEstimate(
                flops=flops, transcendentals=blocks * 2 * (strip_rows + WIN) * LANES,
                bytes_accessed=4 * strip_rows * strip_width * 2,
            ),
        )(*common, *vmem_operands(fluxes, partials, swap_within, swap_across))

    state, partials, within, across = phase(False, True, flux_start, flux_start, flux_start, flux_start)
    for iteration in range(1, ITERS):
        swap_within, swap_across = exchange(within, across)
        state, partials, within, across = phase(False, False, state, partials, swap_within, swap_across)
    swap_within, swap_across = exchange(within, across)
    residual, fluxes = phase(True, False, state, partials, swap_within, swap_across)
    return (fluxes, residual)


def solution(mesh):
    return jax.shard_map(
        local,
        mesh=mesh,
        in_specs=(
            P(("groups", "ty"), None),
            P(("groups", "ty")),
            P(("groups", "ty")),
            P(("groups", "ty")),
            P(("groups", "ty"), None),
            P(("groups", "ty"), None),
            P(("groups", "ty"), None),
            P(),
        ),
        out_specs=(P(("groups", "ty"), None), P(("groups", "ty"), None)),
        check_vma=False,
    )
```
